32 devices in a mesh: group: 8 (over y, x, core), tensor: 4 (over z).
Axes of the slice: x: 2, y: 2, z: 4, core: 2. Of those that a mesh axis runs over, the one named last changes fastest.
Arguments:
- hidden: bfloat16 [768, 4096], P('group'), may hold values from -6 to 6
- query_weight: bfloat16 [4096, 4096], P(None, 'tensor'), may hold values from -0.09375 to 0.09375
- out_weight: bfloat16 [4096, 4096], P('tensor'), may hold values from -0.75 to 0.75
- prefix_keys: bfloat16 [9216, 16, 1024], P('group', None, 'tensor')
- prefix_values: bfloat16 [9216, 16, 1024], P('group', None, 'tensor'), may hold values from -6 to 6
- block_table: int32 [144, 64], P('group'), may hold values from 0 to 1151, as said below
- prompt_len: int32 [144], replicated, may hold values from 1 to 1024
- prompt_group: int32 [768], P('group'), may hold values from 0 to 143, as said below
- suffix_keys: bfloat16 [768, 128, 1024], P('group', None, 'tensor')
- suffix_values: bfloat16 [768, 128, 1024], P('group', None, 'tensor'), may hold values from -6 to 6
- suffix_len: int32 [768], P('group'), may hold values from 1 to 128
Outputs:
- attn_out: bfloat16 [768, 4096], P('group', 'tensor')
The draws below stay inside these ranges and needn't reach their ends.
Inputs may be any that keep to these rules, and one draw needn't show every extreme that they name: `prompt_group`: each of the 144 prompt groups holds 4 to 8 requests, both sizes occurring; no two requests among one index of group's 96 requests share a prompt group. `block_table`: the 18 consecutive rows of one index of group list each of that index's 18 * 64 pool blocks exactly once.
All inputs are finite; a program needn't handle non-finite values.
Results may differ from the reference program's by a relative error of at most 0.0045.
The reference program's roundings to bfloat16 on the way (of `rotated`, `far_rounded` and `attn`) count: a program that leaves them out, or rounds other values in their place, can miss the bound.
Values may be sent and summed in bfloat16 or wider, within the bound.
No kernel may reach another device: no remote copies, remote signals or barrier semaphores. Data moves between devices by JAX's collectives and lax.ppermute only.
A program may use at most 192 MiB of HBM per device.

```python
import math
import jax
import jax.numpy as jnp
from jax import lax

D = 4096
NH = 32
KVH = 8
HD = 128
REQ_DEV = 96
BLOCK = 16
PMAX = 1024
SMAX = 128
GMAX = 8
GMIN = 4
PG_DEV = 18
NPG = 144
REQS = 768
PBLK = 64


def draw_prefix_keys(key, part):
    base = jax.random.normal(jax.random.fold_in(key, 1), (NPG * PBLK, BLOCK, KVH * HD), jnp.float32)
    return base.astype(jnp.bfloat16)


def draw_suffix_keys(key, part):
    base = jax.random.normal(jax.random.fold_in(key, 3), (REQS, SMAX, KVH * HD), jnp.float32)
    return base.astype(jnp.bfloat16)


def draw_block_table(key, part):
    holders = NPG // PG_DEV
    splits = jax.random.split(jax.random.fold_in(key, 7), holders)
    perms = jax.vmap(lambda single: jax.random.permutation(single, PG_DEV * PBLK))(splits)
    return perms.reshape(NPG, PBLK).astype(jnp.int32)


def draw_prompt_len(key, part):
    lengths = jax.random.randint(jax.random.fold_in(key, 8), (NPG,), 1, PMAX + 1, jnp.int32)
    where_full = jax.random.randint(jax.random.fold_in(key, 9), (), 0, NPG, jnp.int32)
    return lengths.at[where_full].set(PMAX)


def draw_suffix_len(key, part):
    lengths = jax.random.randint(jax.random.fold_in(key, 10), (REQS,), 1, SMAX + 1, jnp.int32)
    where_full = jax.random.randint(jax.random.fold_in(key, 12), (), 0, REQS, jnp.int32)
    return lengths.at[where_full].set(SMAX)


def draw_prompt_group(key, part):
    span_width = GMAX - GMIN
    first_key = jax.random.fold_in(key, 31)
    second_key = jax.random.fold_in(key, 32)
    third_key = jax.random.fold_in(key, 33)
    fourth_key = jax.random.fold_in(key, 34)
    order = jax.random.permutation(first_key, NPG)
    remaining = REQS - NPG * GMIN - span_width
    ranks = jax.random.permutation(second_key, (NPG - 2) * span_width)
    chosen = jnp.sum((ranks < remaining).astype(jnp.int32).reshape(NPG - 2, span_width), axis=1)
    extra = jnp.concatenate([jnp.array([span_width], jnp.int32), jnp.array([0], jnp.int32), chosen.astype(jnp.int32)])
    sizes = jnp.zeros((NPG,), jnp.int32).at[order].set(GMIN + extra)
    deal = jax.random.permutation(third_key, NPG).astype(jnp.int32)
    sequence = jnp.repeat(deal, sizes[deal], total_repeat_length=REQS)
    holders = NPG // PG_DEV
    places = jnp.arange(REQS, dtype=jnp.int32)
    device_index = places % holders
    local_index = places // holders
    splits = jax.random.split(fourth_key, holders)
    slot_perms = jax.vmap(lambda single: jax.random.permutation(single, REQ_DEV))(splits).astype(jnp.int32)
    target = device_index * REQ_DEV + slot_perms[device_index, local_index]
    return jnp.zeros((REQS,), jnp.int32).at[target].set(sequence)


def shard_levels(own_key, shape, pieces, smallest, largest):
    loudness, own = 1.0, jax.random.fold_in(own_key, 6)
    for dim, shards_of in pieces:
        draws = jnp.exp(jax.random.uniform(jax.random.fold_in(own, dim), (shards_of,), jnp.float32, smallest / len(pieces), largest / len(pieces)))
        loudness = loudness * jnp.repeat(draws, shape[dim] // shards_of).reshape([-1 if axis == dim else 1 for axis in range(len(shape))])
    return loudness


def gaussian(rng, dims, spread, bound, cuts=(), kind=jnp.bfloat16):
    gain = shard_levels(rng, dims, cuts, -0.22, 0.18) if cuts else 1.0
    values = jax.random.normal(rng, dims, jnp.float32) * spread * gain
    return jnp.minimum(jnp.maximum(values, -bound), bound).astype(kind)


def setup_inputs(seed: int = 0) -> dict:
    seeds = jax.random.split(jax.random.key(seed), 12)
    hidden = gaussian(seeds[0], (REQS, D), 1.0, 6.0, ((0, 8),))
    query_weight = gaussian(seeds[1], (D, NH * HD), D ** -0.5, 0.09375, ((1, 4),))
    out_weight = gaussian(seeds[2], (NH * HD, D), (max(NH * HD // 64, 1)) ** -0.5, 0.75, ((0, 4),))
    prefix_keys = draw_prefix_keys(jax.random.fold_in(seeds[11], 71), 0)
    prefix_values = gaussian(seeds[4], (NPG * PBLK, BLOCK, KVH * HD), 1.0, 6.0, ((0, 8), (2, 4)))
    block_table = draw_block_table(jax.random.fold_in(seeds[11], 71), 0)
    prompt_len = draw_prompt_len(jax.random.fold_in(seeds[11], 71), 0)
    prompt_group = draw_prompt_group(jax.random.fold_in(seeds[11], 71), 0)
    suffix_keys = draw_suffix_keys(jax.random.fold_in(seeds[11], 71), 0)
    suffix_values = gaussian(seeds[9], (REQS, SMAX, KVH * HD), 1.0, 6.0, ((0, 8), (2, 4)))
    suffix_len = draw_suffix_len(jax.random.fold_in(seeds[11], 71), 0)
    return dict(hidden=hidden, query_weight=query_weight, out_weight=out_weight, prefix_keys=prefix_keys, prefix_values=prefix_values, block_table=block_table, prompt_len=prompt_len, prompt_group=prompt_group, suffix_keys=suffix_keys, suffix_values=suffix_values, suffix_len=suffix_len)


rope_base = 10000.0
masked_score = -1e+30

def rotate(projected, position):
    half = projected.shape[-1] // 2
    freqs = rope_base ** (-(2.0 * jnp.arange(half, dtype=jnp.float32)) / projected.shape[-1])
    angles = position.astype(jnp.float32)[:, None, None] * freqs
    cosine = jnp.cos(angles)
    sine = jnp.sin(angles)
    former = projected[..., :half]
    latter = projected[..., half:]
    return jnp.concatenate([former * cosine - latter * sine, latter * cosine + former * sine], axis=-1)

def softmax_parts(scores, valid_mask):
    masked = jnp.where(valid_mask, scores, masked_score)
    maximum = lax.optimization_barrier(jnp.max(masked, axis=-1))
    weights = jnp.where(valid_mask, jnp.exp(masked - maximum[..., None]), 0.0)
    return (maximum, lax.optimization_barrier(jnp.sum(weights, axis=-1)), weights.astype(jnp.bfloat16))

def combine(far_peak, far_total, far_acc, near_peak, near_total, near_acc):
    highest = jnp.maximum(far_peak, near_peak)
    far_factor = jnp.exp(far_peak - highest)
    near_factor = jnp.exp(near_peak - highest)
    numer = far_acc * far_factor[..., None] + near_acc * near_factor[..., None]
    denom = far_total * far_factor + near_total * near_factor
    return numer / denom[..., None]

def reference(hidden, query_weight, out_weight, prefix_keys, prefix_values, block_table, prompt_len, prompt_group, suffix_keys, suffix_values, suffix_len):
    requests = hidden.shape[0]
    score_scale = 1.0 / math.sqrt(HD)
    projected = jnp.dot(hidden, query_weight, preferred_element_type=jnp.float32).reshape(requests, NH, HD)
    position = prompt_len[prompt_group] + suffix_len - 1
    rotated = lax.optimization_barrier(rotate(projected, position).astype(jnp.bfloat16))

    def one_request(items):
        query, group_id, near_len, near_keys, near_values = items
        heads = query.reshape(KVH, NH // KVH, HD).astype(jnp.float32)
        holder = group_id // PG_DEV
        blocks = holder * (PG_DEV * PBLK) + block_table[group_id]
        far_keys = prefix_keys[blocks].reshape(PMAX, KVH, HD).astype(jnp.float32)
        far_values = prefix_values[blocks].reshape(PMAX, KVH, HD).astype(jnp.float32)
        far_scores = jnp.einsum('kgd,tkd->kgt', heads, far_keys) * score_scale
        far_valid = jnp.arange(PMAX, dtype=jnp.int32) < prompt_len[group_id]
        far_peak, far_total, far_rounded = softmax_parts(far_scores, far_valid)
        far_rounded = lax.optimization_barrier(far_rounded)
        far_acc = jnp.einsum('kgt,tkd->kgd', far_rounded.astype(jnp.float32), far_values)
        own_keys = near_keys.reshape(SMAX, KVH, HD).astype(jnp.float32)
        own_values = near_values.reshape(SMAX, KVH, HD).astype(jnp.float32)
        near_scores = jnp.einsum('kgd,tkd->kgt', heads, own_keys) * score_scale
        near_valid = jnp.arange(SMAX, dtype=jnp.int32) < near_len
        near_peak, near_total, near_rounded = softmax_parts(near_scores, near_valid)
        near_rounded = lax.optimization_barrier(near_rounded)
        near_acc = jnp.einsum('kgt,tkd->kgd', near_rounded.astype(jnp.float32), own_values)
        merged = combine(far_peak, far_total, far_acc, near_peak, near_total, near_acc)
        return merged.reshape(NH * HD).astype(jnp.bfloat16)
    attn = lax.map(one_request, (rotated, prompt_group, suffix_len, suffix_keys, suffix_values))
    return jnp.dot(attn, out_weight, preferred_element_type=jnp.float32).astype(jnp.bfloat16)
```

```python
import math

import jax
import jax.numpy as jnp
from jax import lax
from jax.sharding import PartitionSpec as P

HD = 128


rope_base = 10000.0
masked_score = -1e30


def rotate(projected, position):
    half = projected.shape[-1] // 2
    freqs = rope_base ** (-(2.0 * jnp.arange(half, dtype=jnp.float32)) / projected.shape[-1])
    angles = position.astype(jnp.float32)[:, None, None] * freqs
    cosine = jnp.cos(angles)
    sine = jnp.sin(angles)
    former = projected[..., :half]
    latter = projected[..., half:]
    return jnp.concatenate(
        [former * cosine - latter * sine, latter * cosine + former * sine], axis=-1
    )


def softmax_parts(scores, valid_mask):
    masked = jnp.where(valid_mask, scores, masked_score)
    maximum = jnp.max(masked, axis=-1)
    weights = jnp.where(valid_mask, jnp.exp(masked - maximum[..., None]), 0.0)
    return (maximum, jnp.sum(weights, axis=-1), weights.astype(jnp.bfloat16))


def combine(far_peak, far_total, far_acc, near_peak, near_total, near_acc):
    highest = jnp.maximum(far_peak, near_peak)
    far_factor = jnp.exp(far_peak - highest)
    near_factor = jnp.exp(near_peak - highest)
    numer = far_acc * far_factor[..., None] + near_acc * near_factor[..., None]
    denom = far_total * far_factor + near_total * near_factor
    return numer / denom[..., None]


def spread_lanes(queries, kv_heads):
    lead = queries.shape[:-3]
    share = queries.shape[-2]
    eye = (jnp.arange(kv_heads)[:, None] == jnp.arange(kv_heads)[None, :]).astype(queries.dtype)
    eye = eye.reshape((1,) * len(lead) + (kv_heads, 1, kv_heads, 1))
    wide = queries[..., None, :] * eye
    return wide.reshape(lead + (kv_heads * share, kv_heads * HD))


def pick_lanes(wide, kv_heads):
    lead = wide.shape[:-2]
    share = wide.shape[-2] // kv_heads
    w = wide.reshape(lead + (kv_heads, share, kv_heads, HD))
    return jnp.stack([w[..., k, :, k, :] for k in range(kv_heads)], axis=-3)


def body(
    hidden,
    query_weight,
    out_weight,
    prefix_keys,
    prefix_values,
    block_table,
    prompt_len,
    prompt_group,
    suffix_keys,
    suffix_values,
    suffix_len,
):
    groups = lax.axis_size("group")
    local_groups = block_table.shape[0]
    first_group = lax.axis_index("group") * local_groups
    requests = hidden.shape[0]
    width = prefix_keys.shape[2]
    kv_heads = width // HD
    q_heads = query_weight.shape[1] // HD
    share = q_heads // kv_heads
    score_scale = 1.0 / math.sqrt(HD)

    projected = jnp.dot(hidden, query_weight, preferred_element_type=jnp.float32).reshape(
        requests, q_heads, HD
    )
    position = prompt_len[prompt_group] + suffix_len - 1
    rotated = rotate(projected, position).astype(jnp.bfloat16)

    slots = jnp.arange(groups * local_groups, dtype=jnp.int32)
    picks = (slots[:, None] == prompt_group[None, :]).astype(jnp.bfloat16)
    outgoing = jnp.dot(
        picks, rotated.reshape(requests, q_heads * HD), preferred_element_type=jnp.float32
    ).astype(jnp.bfloat16)
    arrived = lax.all_to_all(
        outgoing.reshape(groups, local_groups, q_heads * HD),
        "group",
        split_axis=0,
        concat_axis=0,
        tiled=True,
    )
    far_queries = jnp.transpose(
        arrived.reshape(groups, local_groups, kv_heads, share, HD), (1, 0, 2, 3, 4)
    )
    far_queries = spread_lanes(far_queries, kv_heads).reshape(
        local_groups, groups * q_heads, width
    )
    far_keys = prefix_keys[block_table].reshape(local_groups, -1, width)
    far_values = prefix_values[block_table].reshape(local_groups, -1, width)
    key_count = far_keys.shape[1]
    my_lengths = lax.dynamic_slice_in_dim(prompt_len, first_group, local_groups)
    far_valid = jnp.arange(key_count, dtype=jnp.int32)[None, None, :] < my_lengths[:, None, None]
    far_scores = (
        jnp.einsum("jqc,jtc->jqt", far_queries, far_keys, preferred_element_type=jnp.float32)
        * score_scale
    )
    held_peak, held_total, held_weights = softmax_parts(far_scores, far_valid)
    held_wide = jnp.einsum(
        "jqt,jtc->jqc", held_weights, far_values, preferred_element_type=jnp.float32
    )
    held_acc = pick_lanes(held_wide.reshape(local_groups, groups, q_heads, width), kv_heads)
    held_acc = jnp.transpose(
        held_acc.reshape(local_groups, groups, q_heads, HD), (1, 0, 2, 3)
    )
    stats = jnp.concatenate(
        [
            held_peak.reshape(local_groups, groups, q_heads),
            held_total.reshape(local_groups, groups, q_heads),
            jnp.zeros((local_groups, groups, HD - 2 * q_heads), jnp.float32),
        ],
        axis=-1,
    )
    stats = jnp.transpose(stats, (1, 0, 2))[:, :, None, :]
    packed = jnp.concatenate([held_acc, stats], axis=2)
    back = lax.all_to_all(packed, "group", split_axis=0, concat_axis=0, tiled=True)
    holder = prompt_group // local_groups
    slot_index = prompt_group % local_groups
    mine = back[holder, slot_index]
    far_acc = mine[:, :q_heads, :]
    far_peak = mine[:, q_heads, :q_heads]
    far_total = mine[:, q_heads, q_heads : 2 * q_heads]

    near_queries = spread_lanes(rotated.reshape(requests, kv_heads, share, HD), kv_heads)
    own_count = suffix_keys.shape[1]
    near_valid = jnp.arange(own_count, dtype=jnp.int32)[None, None, :] < suffix_len[:, None, None]
    near_scores = (
        jnp.einsum("rqc,rtc->rqt", near_queries, suffix_keys, preferred_element_type=jnp.float32)
        * score_scale
    )
    near_peak, near_total, near_weights = softmax_parts(near_scores, near_valid)
    near_wide = jnp.einsum(
        "rqt,rtc->rqc", near_weights, suffix_values, preferred_element_type=jnp.float32
    )
    near_acc = pick_lanes(near_wide, kv_heads).reshape(requests, q_heads, HD)
    attn = combine(far_peak, far_total, far_acc, near_peak, near_total, near_acc)
    attn = attn.reshape(requests, q_heads * HD).astype(jnp.bfloat16)
    partial_out = jnp.dot(attn, out_weight, preferred_element_type=jnp.float32)
    return lax.psum_scatter(partial_out, "tensor", scatter_dimension=1, tiled=True).astype(
        jnp.bfloat16
    )


def solution(mesh):
    in_specs = (
        P("group", None),
        P(None, "tensor"),
        P("tensor", None),
        P("group", None, "tensor"),
        P("group", None, "tensor"),
        P("group", None),
        P(),
        P("group"),
        P("group", None, "tensor"),
        P("group", None, "tensor"),
        P("group"),
    )
    out_specs = P("group", "tensor")
    return jax.shard_map(body, mesh=mesh, in_specs=in_specs, out_specs=out_specs, check_vma=False)
```

```python
import math

import jax
import jax.numpy as jnp
from jax import lax
from jax.sharding import PartitionSpec as P

HD = 128


rope_base = 10000.0
masked_score = -1e30


def rotate(projected, position):
    half = projected.shape[-1] // 2
    freqs = rope_base ** (-(2.0 * jnp.arange(half, dtype=jnp.float32)) / projected.shape[-1])
    angles = position.astype(jnp.float32)[:, None, None] * freqs
    cosine = jnp.cos(angles)
    sine = jnp.sin(angles)
    former = projected[..., :half]
    latter = projected[..., half:]
    return jnp.concatenate(
        [former * cosine - latter * sine, latter * cosine + former * sine], axis=-1
    )


def softmax_parts(scores, valid_mask):
    masked = jnp.where(valid_mask, scores, masked_score)
    maximum = jnp.max(masked, axis=-1)
    weights = jnp.where(valid_mask, jnp.exp(masked - maximum[..., None]), 0.0)
    return (maximum, jnp.sum(weights, axis=-1), weights.astype(jnp.bfloat16))


def combine(far_peak, far_total, far_acc, near_peak, near_total, near_acc):
    highest = jnp.maximum(far_peak, near_peak)
    far_factor = jnp.exp(far_peak - highest)
    near_factor = jnp.exp(near_peak - highest)
    numer = far_acc * far_factor[..., None] + near_acc * near_factor[..., None]
    denom = far_total * far_factor + near_total * near_factor
    return numer / denom[..., None]


def spread_lanes(queries, kv_heads):
    lead = queries.shape[:-3]
    share = queries.shape[-2]
    eye = (jnp.arange(kv_heads)[:, None] == jnp.arange(kv_heads)[None, :]).astype(queries.dtype)
    eye = eye.reshape((1,) * len(lead) + (kv_heads, 1, kv_heads, 1))
    wide = queries[..., None, :] * eye
    return wide.reshape(lead + (kv_heads * share, kv_heads * HD))


def pick_lanes(wide, kv_heads):
    lead = wide.shape[:-2]
    share = wide.shape[-2] // kv_heads
    w = wide.reshape(lead + (kv_heads, share, kv_heads, HD))
    return jnp.stack([w[..., k, :, k, :] for k in range(kv_heads)], axis=-3)


def body(
    hidden,
    query_weight,
    out_weight,
    prefix_keys,
    prefix_values,
    block_table,
    prompt_len,
    prompt_group,
    suffix_keys,
    suffix_values,
    suffix_len,
):
    groups = lax.axis_size("group")
    local_groups = block_table.shape[0]
    first_group = lax.axis_index("group") * local_groups
    requests = hidden.shape[0]
    width = prefix_keys.shape[2]
    kv_heads = width // HD
    q_heads = query_weight.shape[1] // HD
    share = q_heads // kv_heads
    score_scale = 1.0 / math.sqrt(HD)

    projected = jnp.dot(hidden, query_weight, preferred_element_type=jnp.float32).reshape(
        requests, q_heads, HD
    )
    position = prompt_len[prompt_group] + suffix_len - 1
    rotated = rotate(projected, position).astype(jnp.bfloat16)

    slots = jnp.arange(groups * local_groups, dtype=jnp.int32)
    picks = (slots[:, None] == prompt_group[None, :]).astype(jnp.bfloat16)
    outgoing = jnp.dot(
        picks, rotated.reshape(requests, q_heads * HD), preferred_element_type=jnp.float32
    ).astype(jnp.bfloat16)
    arrived = lax.all_to_all(
        outgoing.reshape(groups, local_groups, q_heads * HD),
        "group",
        split_axis=0,
        concat_axis=0,
        tiled=True,
    )
    far_queries = jnp.transpose(
        arrived.reshape(groups, local_groups, kv_heads, share, HD), (1, 0, 2, 3, 4)
    )
    far_queries = spread_lanes(far_queries, kv_heads).reshape(
        local_groups, groups * q_heads, width
    )
    far_keys = prefix_keys[block_table].reshape(local_groups, -1, width)
    far_values = prefix_values[block_table].reshape(local_groups, -1, width)
    key_count = far_keys.shape[1]
    my_lengths = lax.dynamic_slice_in_dim(prompt_len, first_group, local_groups)
    far_valid = jnp.arange(key_count, dtype=jnp.int32)[None, None, :] < my_lengths[:, None, None]
    far_scores = (
        jnp.einsum("jqc,jtc->jqt", far_queries, far_keys, preferred_element_type=jnp.float32)
        * score_scale
    )
    held_peak, held_total, held_weights = softmax_parts(far_scores, far_valid)
    held_wide = jnp.einsum(
        "jqt,jtc->jqc", held_weights, far_values, preferred_element_type=jnp.float32
    )
    held_acc = pick_lanes(held_wide.reshape(local_groups, groups, q_heads, width), kv_heads)
    held_acc = jnp.transpose(
        held_acc.reshape(local_groups, groups, q_heads, HD), (1, 0, 2, 3)
    )
    stats = jnp.concatenate(
        [
            held_peak.reshape(local_groups, groups, q_heads),
            held_total.reshape(local_groups, groups, q_heads),
            jnp.zeros((local_groups, groups, HD - 2 * q_heads), jnp.float32),
        ],
        axis=-1,
    )
    stats = jnp.transpose(stats, (1, 0, 2))[:, :, None, :]
    packed = jnp.concatenate([held_acc, stats], axis=2)
    back = lax.all_to_all(packed, "group", split_axis=0, concat_axis=0, tiled=True)
    holder = prompt_group // local_groups
    slot_index = prompt_group % local_groups
    mine = back[holder, slot_index]
    far_acc = mine[:, :q_heads, :]
    far_peak = mine[:, q_heads, :q_heads]
    far_total = mine[:, q_heads, q_heads : 2 * q_heads]

    near_queries = spread_lanes(rotated.reshape(requests, kv_heads, share, HD), kv_heads)
    own_count = suffix_keys.shape[1]
    near_valid = jnp.arange(own_count, dtype=jnp.int32)[None, None, :] < suffix_len[:, None, None]
    near_scores = (
        jnp.einsum("rqc,rtc->rqt", near_queries, suffix_keys, preferred_element_type=jnp.float32)
        * score_scale
    )
    near_peak, near_total, near_weights = softmax_parts(near_scores, near_valid)
    near_wide = jnp.einsum(
        "rqt,rtc->rqc", near_weights, suffix_values, preferred_element_type=jnp.float32
    )
    near_acc = pick_lanes(near_wide, kv_heads).reshape(requests, q_heads, HD)
    attn = combine(far_peak, far_total, far_acc, near_peak, near_total, near_acc)
    attn = attn.reshape(requests, q_heads * HD).astype(jnp.bfloat16)
    partial_out = jnp.dot(attn, out_weight, preferred_element_type=jnp.float32)
    parts = lax.axis_size("tensor")
    pieces = lax.all_to_all(
        partial_out.reshape(requests, parts, -1), "tensor", split_axis=1, concat_axis=1, tiled=True
    )
    return jnp.sum(pieces, axis=1).astype(jnp.bfloat16)


def solution(mesh):
    in_specs = (
        P("group", None),
        P(None, "tensor"),
        P("tensor", None),
        P("group", None, "tensor"),
        P("group", None, "tensor"),
        P("group", None),
        P(),
        P("group"),
        P("group", None, "tensor"),
        P("group", None, "tensor"),
        P("group"),
    )
    out_specs = P("group", "tensor")
    return jax.shard_map(body, mesh=mesh, in_specs=in_specs, out_specs=out_specs, check_vma=False)
```

```python
import math

import jax
import jax.numpy as jnp
from jax import lax
from jax.experimental import pallas as pl
from jax.experimental.pallas import tpu as pltpu
from jax.sharding import PartitionSpec as P

HD = 128


rope_base = 10000.0
masked_score = -1e30


def rotate(projected, position):
    half = projected.shape[-1] // 2
    freqs = rope_base ** (-(2.0 * jnp.arange(half, dtype=jnp.float32)) / projected.shape[-1])
    angles = position.astype(jnp.float32)[:, None, None] * freqs
    cosine = jnp.cos(angles)
    sine = jnp.sin(angles)
    former = projected[..., :half]
    latter = projected[..., half:]
    return jnp.concatenate(
        [former * cosine - latter * sine, latter * cosine + former * sine], axis=-1
    )


def softmax_parts(scores, valid_mask):
    masked = jnp.where(valid_mask, scores, masked_score)
    maximum = jnp.max(masked, axis=-1)
    weights = jnp.where(valid_mask, jnp.exp(masked - maximum[..., None]), 0.0)
    return (maximum, jnp.sum(weights, axis=-1), weights.astype(jnp.bfloat16))


def combine(far_peak, far_total, far_acc, near_peak, near_total, near_acc):
    highest = jnp.maximum(far_peak, near_peak)
    far_factor = jnp.exp(far_peak - highest)
    near_factor = jnp.exp(near_peak - highest)
    numer = far_acc * far_factor[..., None] + near_acc * near_factor[..., None]
    denom = far_total * far_factor + near_total * near_factor
    return numer / denom[..., None]


def spread_lanes(queries, kv_heads):
    lead = queries.shape[:-3]
    share = queries.shape[-2]
    eye = (jnp.arange(kv_heads)[:, None] == jnp.arange(kv_heads)[None, :]).astype(queries.dtype)
    eye = eye.reshape((1,) * len(lead) + (kv_heads, 1, kv_heads, 1))
    wide = queries[..., None, :] * eye
    return wide.reshape(lead + (kv_heads * share, kv_heads * HD))


def pick_lanes(wide, kv_heads):
    lead = wide.shape[:-2]
    share = wide.shape[-2] // kv_heads
    w = wide.reshape(lead + (kv_heads, share, kv_heads, HD))
    return jnp.stack([w[..., k, :, k, :] for k in range(kv_heads)], axis=-3)


def far_kernel(
    table_ref, len_ref, q_ref, k_hbm, v_hbm, acc_ref, stat_ref, kbuf, vbuf, sems, *, share, scale
):
    j = pl.program_id(0)
    steps = pl.num_programs(0)
    pblk = kbuf.shape[1]
    width = kbuf.shape[3]
    kv_heads = width // HD

    def fetch(group, slot):
        def one(b, carry):
            idx = table_ref[group * pblk + b]
            pltpu.make_async_copy(k_hbm.at[idx], kbuf.at[slot, b], sems.at[0, slot]).start()
            pltpu.make_async_copy(v_hbm.at[idx], vbuf.at[slot, b], sems.at[1, slot]).start()
            return carry

        lax.fori_loop(0, pblk, one, 0, unroll=8)

    @pl.when(j == 0)
    def _():
        fetch(0, 0)

    slot = j % 2

    @pl.when(j + 1 < steps)
    def _():
        fetch(j + 1, 1 - slot)

    pltpu.make_async_copy(k_hbm.at[pl.ds(0, pblk)], kbuf.at[slot], sems.at[0, slot]).wait()
    pltpu.make_async_copy(v_hbm.at[pl.ds(0, pblk)], vbuf.at[slot], sems.at[1, slot]).wait()
    keys = kbuf[slot].reshape(-1, width)
    values = vbuf[slot].reshape(-1, width)
    queries = q_ref[0]
    scores = (
        lax.dot_general(
            queries, keys, (((1,), (1,)), ((), ())), preferred_element_type=jnp.float32
        )
        * scale
    )
    valid = lax.broadcasted_iota(jnp.int32, scores.shape, 1) < len_ref[j]
    masked = jnp.where(valid, scores, masked_score)
    peak = jnp.max(masked, axis=1, keepdims=True)
    weights = jnp.where(valid, jnp.exp(masked - peak), 0.0)
    total = jnp.sum(weights, axis=1, keepdims=True)
    wide = jnp.dot(weights.astype(jnp.bfloat16), values, preferred_element_type=jnp.float32)
    rows = wide.shape[0]
    row_head = (lax.broadcasted_iota(jnp.int32, (rows, HD), 0) // share) % kv_heads
    acc = jnp.zeros((rows, HD), jnp.float32)
    for k in range(kv_heads):
        acc = jnp.where(row_head == k, wide[:, k * HD : (k + 1) * HD], acc)
    acc_ref[0] = acc
    lane = lax.broadcasted_iota(jnp.int32, (rows, HD), 1)
    stat_ref[0] = jnp.where(lane < HD // 2, peak, total)


def far_attention(table, lengths, queries, prefix_keys, prefix_values, share, scale):
    local_groups, pblk = table.shape
    _, rows, width = queries.shape
    block = prefix_keys.shape[1]
    tokens = pblk * block
    kernel = lambda *refs: far_kernel(*refs, share=share, scale=scale)
    grid_spec = pltpu.PrefetchScalarGridSpec(
        num_scalar_prefetch=2,
        grid=(local_groups,),
        in_specs=[
            pl.BlockSpec((1, rows, width), lambda j, *_: (j, 0, 0)),
            pl.BlockSpec(memory_space=pl.ANY),
            pl.BlockSpec(memory_space=pl.ANY),
        ],
        out_specs=[
            pl.BlockSpec((1, rows, HD), lambda j, *_: (j, 0, 0)),
            pl.BlockSpec((1, rows, HD), lambda j, *_: (j, 0, 0)),
        ],
        scratch_shapes=[
            pltpu.VMEM((2, pblk, block, width), prefix_keys.dtype),
            pltpu.VMEM((2, pblk, block, width), prefix_values.dtype),
            pltpu.SemaphoreType.DMA((2, 2)),
        ],
    )
    cost = pl.CostEstimate(
        flops=4 * local_groups * rows * tokens * width,
        transcendentals=local_groups * rows * tokens,
        bytes_accessed=2 * local_groups * tokens * width * 2 + 3 * local_groups * rows * width * 2,
    )
    return pl.pallas_call(
        kernel,
        grid_spec=grid_spec,
        out_shape=[
            jax.ShapeDtypeStruct((local_groups, rows, HD), jnp.float32),
            jax.ShapeDtypeStruct((local_groups, rows, HD), jnp.float32),
        ],
        compiler_params=pltpu.CompilerParams(dimension_semantics=("arbitrary",)),
        cost_estimate=cost,
    )(table.reshape(-1), lengths, queries, prefix_keys, prefix_values)


def body(
    hidden,
    query_weight,
    out_weight,
    prefix_keys,
    prefix_values,
    block_table,
    prompt_len,
    prompt_group,
    suffix_keys,
    suffix_values,
    suffix_len,
):
    groups = lax.axis_size("group")
    local_groups = block_table.shape[0]
    first_group = lax.axis_index("group") * local_groups
    requests = hidden.shape[0]
    width = prefix_keys.shape[2]
    kv_heads = width // HD
    q_heads = query_weight.shape[1] // HD
    share = q_heads // kv_heads
    score_scale = 1.0 / math.sqrt(HD)

    projected = jnp.dot(hidden, query_weight, preferred_element_type=jnp.float32).reshape(
        requests, q_heads, HD
    )
    position = prompt_len[prompt_group] + suffix_len - 1
    rotated = rotate(projected, position).astype(jnp.bfloat16)

    slots = jnp.arange(groups * local_groups, dtype=jnp.int32)
    picks = (slots[:, None] == prompt_group[None, :]).astype(jnp.bfloat16)
    outgoing = jnp.dot(
        picks, rotated.reshape(requests, q_heads * HD), preferred_element_type=jnp.float32
    ).astype(jnp.bfloat16)
    arrived = lax.all_to_all(
        outgoing.reshape(groups, local_groups, q_heads * HD),
        "group",
        split_axis=0,
        concat_axis=0,
        tiled=True,
    )
    far_queries = jnp.transpose(
        arrived.reshape(groups, local_groups, kv_heads, share, HD), (1, 0, 2, 3, 4)
    )
    far_queries = spread_lanes(far_queries, kv_heads).reshape(
        local_groups, groups * q_heads, width
    )
    my_lengths = lax.dynamic_slice_in_dim(prompt_len, first_group, local_groups)
    held_acc, held_stat = far_attention(
        block_table, my_lengths, far_queries, prefix_keys, prefix_values, share, score_scale
    )
    held_acc = jnp.transpose(held_acc.reshape(local_groups, groups, q_heads, HD), (1, 0, 2, 3))
    held_peak = held_stat[:, :, 0]
    held_total = held_stat[:, :, HD // 2]
    stats = jnp.concatenate(
        [
            held_peak.reshape(local_groups, groups, q_heads),
            held_total.reshape(local_groups, groups, q_heads),
            jnp.zeros((local_groups, groups, HD - 2 * q_heads), jnp.float32),
        ],
        axis=-1,
    )
    stats = jnp.transpose(stats, (1, 0, 2))[:, :, None, :]
    packed = jnp.concatenate([held_acc, stats], axis=2)
    back = lax.all_to_all(packed, "group", split_axis=0, concat_axis=0, tiled=True)
    holder = prompt_group // local_groups
    slot_index = prompt_group % local_groups
    mine = back[holder, slot_index]
    far_acc = mine[:, :q_heads, :]
    far_peak = mine[:, q_heads, :q_heads]
    far_total = mine[:, q_heads, q_heads : 2 * q_heads]

    near_queries = spread_lanes(rotated.reshape(requests, kv_heads, share, HD), kv_heads)
    own_count = suffix_keys.shape[1]
    near_valid = jnp.arange(own_count, dtype=jnp.int32)[None, None, :] < suffix_len[:, None, None]
    near_scores = (
        jnp.einsum("rqc,rtc->rqt", near_queries, suffix_keys, preferred_element_type=jnp.float32)
        * score_scale
    )
    near_peak, near_total, near_weights = softmax_parts(near_scores, near_valid)
    near_wide = jnp.einsum(
        "rqt,rtc->rqc", near_weights, suffix_values, preferred_element_type=jnp.float32
    )
    near_acc = pick_lanes(near_wide, kv_heads).reshape(requests, q_heads, HD)
    attn = combine(far_peak, far_total, far_acc, near_peak, near_total, near_acc)
    attn = attn.reshape(requests, q_heads * HD).astype(jnp.bfloat16)
    partial_out = jnp.dot(attn, out_weight, preferred_element_type=jnp.float32)
    parts = lax.axis_size("tensor")
    pieces = lax.all_to_all(
        partial_out.reshape(requests, parts, -1), "tensor", split_axis=1, concat_axis=1, tiled=True
    )
    return jnp.sum(pieces, axis=1).astype(jnp.bfloat16)


def solution(mesh):
    in_specs = (
        P("group", None),
        P(None, "tensor"),
        P("tensor", None),
        P("group", None, "tensor"),
        P("group", None, "tensor"),
        P("group", None),
        P(),
        P("group"),
        P("group", None, "tensor"),
        P("group", None, "tensor"),
        P("group"),
    )
    out_specs = P("group", "tensor")
    return jax.shard_map(body, mesh=mesh, in_specs=in_specs, out_specs=out_specs, check_vma=False)
```

```python
import math

import jax
import jax.numpy as jnp
from jax import lax
from jax.experimental import pallas as pl
from jax.experimental.pallas import tpu as pltpu
from jax.sharding import PartitionSpec as P

HD = 128


rope_base = 10000.0
masked_score = -1e30


def rotate(projected, position):
    half = projected.shape[-1] // 2
    freqs = rope_base ** (-(2.0 * jnp.arange(half, dtype=jnp.float32)) / projected.shape[-1])
    angles = position.astype(jnp.float32)[:, None, None] * freqs
    cosine = jnp.cos(angles)
    sine = jnp.sin(angles)
    former = projected[..., :half]
    latter = projected[..., half:]
    return jnp.concatenate(
        [former * cosine - latter * sine, latter * cosine + former * sine], axis=-1
    )


def softmax_parts(scores, valid_mask):
    masked = jnp.where(valid_mask, scores, masked_score)
    maximum = jnp.max(masked, axis=-1)
    weights = jnp.where(valid_mask, jnp.exp(masked - maximum[..., None]), 0.0)
    return (maximum, jnp.sum(weights, axis=-1), weights.astype(jnp.bfloat16))


def combine(far_peak, far_total, far_acc, near_peak, near_total, near_acc):
    highest = jnp.maximum(far_peak, near_peak)
    far_factor = jnp.exp(far_peak - highest)
    near_factor = jnp.exp(near_peak - highest)
    numer = far_acc * far_factor[..., None] + near_acc * near_factor[..., None]
    denom = far_total * far_factor + near_total * near_factor
    return numer / denom[..., None]


def spread_lanes(queries, kv_heads):
    lead = queries.shape[:-3]
    share = queries.shape[-2]
    eye = (jnp.arange(kv_heads)[:, None] == jnp.arange(kv_heads)[None, :]).astype(queries.dtype)
    eye = eye.reshape((1,) * len(lead) + (kv_heads, 1, kv_heads, 1))
    wide = queries[..., None, :] * eye
    return wide.reshape(lead + (kv_heads * share, kv_heads * HD))


def pick_lanes(wide, kv_heads):
    lead = wide.shape[:-2]
    share = wide.shape[-2] // kv_heads
    w = wide.reshape(lead + (kv_heads, share, kv_heads, HD))
    return jnp.stack([w[..., k, :, k, :] for k in range(kv_heads)], axis=-3)


def far_kernel(
    table_ref, len_ref, q_ref, k_hbm, v_hbm, acc_ref, stat_ref, kbuf, vbuf, sems, *, share, scale
):
    j = pl.program_id(0)
    steps = pl.num_programs(0)
    pblk = kbuf.shape[1]
    width = kbuf.shape[3]
    kv_heads = width // HD

    block = kbuf.shape[2]

    @pl.when(j == 0)
    def _():
        vbuf[...] = jnp.zeros_like(vbuf)

    def used_blocks(group):
        return (len_ref[group] + block - 1) // block

    def fetch(group, slot):
        def one(b, carry):
            idx = table_ref[group * pblk + b]
            pltpu.make_async_copy(k_hbm.at[idx], kbuf.at[slot, b], sems.at[0, slot, b]).start()
            pltpu.make_async_copy(v_hbm.at[idx], vbuf.at[slot, b], sems.at[1, slot, b]).start()
            return carry

        lax.fori_loop(0, used_blocks(group), one, 0)

    @pl.when(j == 0)
    def _():
        fetch(0, 0)

    slot = j % 2

    @pl.when(j + 1 < steps)
    def _():
        fetch(j + 1, 1 - slot)

    def settle(b, carry):
        pltpu.make_async_copy(k_hbm.at[0], kbuf.at[slot, b], sems.at[0, slot, b]).wait()
        pltpu.make_async_copy(v_hbm.at[0], vbuf.at[slot, b], sems.at[1, slot, b]).wait()
        return carry

    lax.fori_loop(0, used_blocks(j), settle, 0)
    keys = kbuf[slot].reshape(-1, width)
    values = vbuf[slot].reshape(-1, width)
    queries = q_ref[0]
    scores = (
        lax.dot_general(
            queries, keys, (((1,), (1,)), ((), ())), preferred_element_type=jnp.float32
        )
        * scale
    )
    valid = lax.broadcasted_iota(jnp.int32, scores.shape, 1) < len_ref[j]
    masked = jnp.where(valid, scores, masked_score)
    peak = jnp.max(masked, axis=1, keepdims=True)
    weights = jnp.where(valid, jnp.exp(masked - peak), 0.0)
    total = jnp.sum(weights, axis=1, keepdims=True)
    wide = jnp.dot(weights.astype(jnp.bfloat16), values, preferred_element_type=jnp.float32)
    rows = wide.shape[0]
    row_head = (lax.broadcasted_iota(jnp.int32, (rows, HD), 0) // share) % kv_heads
    acc = jnp.zeros((rows, HD), jnp.float32)
    for k in range(kv_heads):
        acc = jnp.where(row_head == k, wide[:, k * HD : (k + 1) * HD], acc)
    acc_ref[0] = acc
    lane = lax.broadcasted_iota(jnp.int32, (rows, HD), 1)
    stat_ref[0] = jnp.where(lane < HD // 2, peak, total)


def far_attention(table, lengths, queries, prefix_keys, prefix_values, share, scale):
    local_groups, pblk = table.shape
    _, rows, width = queries.shape
    block = prefix_keys.shape[1]
    tokens = pblk * block
    kernel = lambda *refs: far_kernel(*refs, share=share, scale=scale)
    grid_spec = pltpu.PrefetchScalarGridSpec(
        num_scalar_prefetch=2,
        grid=(local_groups,),
        in_specs=[
            pl.BlockSpec((1, rows, width), lambda j, *_: (j, 0, 0)),
            pl.BlockSpec(memory_space=pl.ANY),
            pl.BlockSpec(memory_space=pl.ANY),
        ],
        out_specs=[
            pl.BlockSpec((1, rows, HD), lambda j, *_: (j, 0, 0)),
            pl.BlockSpec((1, rows, HD), lambda j, *_: (j, 0, 0)),
        ],
        scratch_shapes=[
            pltpu.VMEM((2, pblk, block, width), prefix_keys.dtype),
            pltpu.VMEM((2, pblk, block, width), prefix_values.dtype),
            pltpu.SemaphoreType.DMA((2, 2, pblk)),
        ],
    )
    cost = pl.CostEstimate(
        flops=4 * local_groups * rows * tokens * width,
        transcendentals=local_groups * rows * tokens,
        bytes_accessed=2 * local_groups * tokens * width * 2 + 3 * local_groups * rows * width * 2,
    )
    return pl.pallas_call(
        kernel,
        grid_spec=grid_spec,
        out_shape=[
            jax.ShapeDtypeStruct((local_groups, rows, HD), jnp.float32),
            jax.ShapeDtypeStruct((local_groups, rows, HD), jnp.float32),
        ],
        compiler_params=pltpu.CompilerParams(dimension_semantics=("arbitrary",)),
        cost_estimate=cost,
    )(table.reshape(-1), lengths, queries, prefix_keys, prefix_values)


def body(
    hidden,
    query_weight,
    out_weight,
    prefix_keys,
    prefix_values,
    block_table,
    prompt_len,
    prompt_group,
    suffix_keys,
    suffix_values,
    suffix_len,
):
    groups = lax.axis_size("group")
    local_groups = block_table.shape[0]
    first_group = lax.axis_index("group") * local_groups
    requests = hidden.shape[0]
    width = prefix_keys.shape[2]
    kv_heads = width // HD
    q_heads = query_weight.shape[1] // HD
    share = q_heads // kv_heads
    score_scale = 1.0 / math.sqrt(HD)

    projected = jnp.dot(hidden, query_weight, preferred_element_type=jnp.float32).reshape(
        requests, q_heads, HD
    )
    position = prompt_len[prompt_group] + suffix_len - 1
    rotated = rotate(projected, position).astype(jnp.bfloat16)

    slots = jnp.arange(groups * local_groups, dtype=jnp.int32)
    picks = (slots[:, None] == prompt_group[None, :]).astype(jnp.bfloat16)
    outgoing = jnp.dot(
        picks, rotated.reshape(requests, q_heads * HD), preferred_element_type=jnp.float32
    ).astype(jnp.bfloat16)
    arrived = lax.all_to_all(
        outgoing.reshape(groups, local_groups, q_heads * HD),
        "group",
        split_axis=0,
        concat_axis=0,
        tiled=True,
    )
    far_queries = jnp.transpose(
        arrived.reshape(groups, local_groups, kv_heads, share, HD), (1, 0, 2, 3, 4)
    )
    far_queries = spread_lanes(far_queries, kv_heads).reshape(
        local_groups, groups * q_heads, width
    )
    my_lengths = lax.dynamic_slice_in_dim(prompt_len, first_group, local_groups)
    held_acc, held_stat = far_attention(
        block_table, my_lengths, far_queries, prefix_keys, prefix_values, share, score_scale
    )
    held_acc = jnp.transpose(held_acc.reshape(local_groups, groups, q_heads, HD), (1, 0, 2, 3))
    held_peak = held_stat[:, :, 0]
    held_total = held_stat[:, :, HD // 2]
    stats = jnp.concatenate(
        [
            held_peak.reshape(local_groups, groups, q_heads),
            held_total.reshape(local_groups, groups, q_heads),
            jnp.zeros((local_groups, groups, HD - 2 * q_heads), jnp.float32),
        ],
        axis=-1,
    )
    stats = jnp.transpose(stats, (1, 0, 2))[:, :, None, :]
    packed = jnp.concatenate([held_acc, stats], axis=2)
    back = lax.all_to_all(packed, "group", split_axis=0, concat_axis=0, tiled=True)
    holder = prompt_group // local_groups
    slot_index = prompt_group % local_groups
    mine = back[holder, slot_index]
    far_acc = mine[:, :q_heads, :]
    far_peak = mine[:, q_heads, :q_heads]
    far_total = mine[:, q_heads, q_heads : 2 * q_heads]

    near_queries = spread_lanes(rotated.reshape(requests, kv_heads, share, HD), kv_heads)
    own_count = suffix_keys.shape[1]
    near_valid = jnp.arange(own_count, dtype=jnp.int32)[None, None, :] < suffix_len[:, None, None]
    near_scores = (
        jnp.einsum("rqc,rtc->rqt", near_queries, suffix_keys, preferred_element_type=jnp.float32)
        * score_scale
    )
    near_peak, near_total, near_weights = softmax_parts(near_scores, near_valid)
    near_wide = jnp.einsum(
        "rqt,rtc->rqc", near_weights, suffix_values, preferred_element_type=jnp.float32
    )
    near_acc = pick_lanes(near_wide, kv_heads).reshape(requests, q_heads, HD)
    attn = combine(far_peak, far_total, far_acc, near_peak, near_total, near_acc)
    attn = attn.reshape(requests, q_heads * HD).astype(jnp.bfloat16)
    partial_out = jnp.dot(attn, out_weight, preferred_element_type=jnp.float32)
    return lax.psum_scatter(partial_out, "tensor", scatter_dimension=1, tiled=True).astype(
        jnp.bfloat16
    )


def solution(mesh):
    in_specs = (
        P("group", None),
        P(None, "tensor"),
        P("tensor", None),
        P("group", None, "tensor"),
        P("group", None, "tensor"),
        P("group", None),
        P(),
        P("group"),
        P("group", None, "tensor"),
        P("group", None, "tensor"),
        P("group"),
    )
    out_specs = P("group", "tensor")
    return jax.shard_map(body, mesh=mesh, in_specs=in_specs, out_specs=out_specs, check_vma=False)
```

```python
import math

import jax
import jax.numpy as jnp
from jax import lax
from jax.experimental import pallas as pl
from jax.experimental.pallas import tpu as pltpu
from jax.sharding import PartitionSpec as P

HD = 128


rope_base = 10000.0
masked_score = -1e30


def rotate(projected, position):
    half = projected.shape[-1] // 2
    freqs = rope_base ** (-(2.0 * jnp.arange(half, dtype=jnp.float32)) / projected.shape[-1])
    angles = position.astype(jnp.float32)[:, None, None] * freqs
    cosine = jnp.cos(angles)
    sine = jnp.sin(angles)
    former = projected[..., :half]
    latter = projected[..., half:]
    return jnp.concatenate(
        [former * cosine - latter * sine, latter * cosine + former * sine], axis=-1
    )


def softmax_parts(scores, valid_mask):
    masked = jnp.where(valid_mask, scores, masked_score)
    maximum = jnp.max(masked, axis=-1)
    weights = jnp.where(valid_mask, jnp.exp(masked - maximum[..., None]), 0.0)
    return (maximum, jnp.sum(weights, axis=-1), weights.astype(jnp.bfloat16))


def combine(far_peak, far_total, far_acc, near_peak, near_total, near_acc):
    highest = jnp.maximum(far_peak, near_peak)
    far_factor = jnp.exp(far_peak - highest)
    near_factor = jnp.exp(near_peak - highest)
    numer = far_acc * far_factor[..., None] + near_acc * near_factor[..., None]
    denom = far_total * far_factor + near_total * near_factor
    return numer / denom[..., None]


def spread_lanes(queries, kv_heads):
    lead = queries.shape[:-3]
    share = queries.shape[-2]
    eye = (jnp.arange(kv_heads)[:, None] == jnp.arange(kv_heads)[None, :]).astype(queries.dtype)
    eye = eye.reshape((1,) * len(lead) + (kv_heads, 1, kv_heads, 1))
    wide = queries[..., None, :] * eye
    return wide.reshape(lead + (kv_heads * share, kv_heads * HD))


def pick_lanes(wide, kv_heads):
    lead = wide.shape[:-2]
    share = wide.shape[-2] // kv_heads
    w = wide.reshape(lead + (kv_heads, share, kv_heads, HD))
    return jnp.stack([w[..., k, :, k, :] for k in range(kv_heads)], axis=-3)


def far_kernel(
    table_ref, len_ref, q_ref, k_hbm, v_hbm, acc_ref, stat_ref, kbuf, vbuf, sems, *, share, scale
):
    j = pl.program_id(0)
    steps = pl.num_programs(0)
    pblk = kbuf.shape[1]
    width = kbuf.shape[3]
    kv_heads = width // HD

    block = kbuf.shape[2]

    @pl.when(j == 0)
    def _():
        vbuf[...] = jnp.zeros_like(vbuf)

    chunk = 8

    def used_chunks(group):
        return (len_ref[group] + block * chunk - 1) // (block * chunk)

    def fetch(group, slot):
        def one(c, carry):
            for i in range(chunk):
                b = c * chunk + i
                idx = table_ref[group * pblk + b]
                pltpu.make_async_copy(k_hbm.at[idx], kbuf.at[slot, b], sems.at[0, slot, c]).start()
                pltpu.make_async_copy(v_hbm.at[idx], vbuf.at[slot, b], sems.at[1, slot, c]).start()
            return carry

        lax.fori_loop(0, used_chunks(group), one, 0)

    @pl.when(j == 0)
    def _():
        fetch(0, 0)

    slot = j % 2

    @pl.when(j + 1 < steps)
    def _():
        fetch(j + 1, 1 - slot)

    def settle(c, carry):
        part = pl.ds(pl.multiple_of(c * chunk, chunk), chunk)
        pltpu.make_async_copy(
            k_hbm.at[pl.ds(0, chunk)], kbuf.at[slot, part], sems.at[0, slot, c]
        ).wait()
        pltpu.make_async_copy(
            v_hbm.at[pl.ds(0, chunk)], vbuf.at[slot, part], sems.at[1, slot, c]
        ).wait()
        return carry

    lax.fori_loop(0, used_chunks(j), settle, 0)
    keys = kbuf[slot].reshape(-1, width)
    values = vbuf[slot].reshape(-1, width)
    queries = q_ref[0]
    scores = (
        lax.dot_general(
            queries, keys, (((1,), (1,)), ((), ())), preferred_element_type=jnp.float32
        )
        * scale
    )
    valid = lax.broadcasted_iota(jnp.int32, scores.shape, 1) < len_ref[j]
    masked = jnp.where(valid, scores, masked_score)
    peak = jnp.max(masked, axis=1, keepdims=True)
    weights = jnp.where(valid, jnp.exp(masked - peak), 0.0)
    total = jnp.sum(weights, axis=1, keepdims=True)
    wide = jnp.dot(weights.astype(jnp.bfloat16), values, preferred_element_type=jnp.float32)
    rows = wide.shape[0]
    row_head = (lax.broadcasted_iota(jnp.int32, (rows, HD), 0) // share) % kv_heads
    acc = jnp.zeros((rows, HD), jnp.float32)
    for k in range(kv_heads):
        acc = jnp.where(row_head == k, wide[:, k * HD : (k + 1) * HD], acc)
    acc_ref[0] = acc
    lane = lax.broadcasted_iota(jnp.int32, (rows, HD), 1)
    stat_ref[0] = jnp.where(lane < HD // 2, peak, total)


def far_attention(table, lengths, queries, prefix_keys, prefix_values, share, scale):
    local_groups, pblk = table.shape
    assert pblk % 8 == 0
    _, rows, width = queries.shape
    block = prefix_keys.shape[1]
    tokens = pblk * block
    kernel = lambda *refs: far_kernel(*refs, share=share, scale=scale)
    grid_spec = pltpu.PrefetchScalarGridSpec(
        num_scalar_prefetch=2,
        grid=(local_groups,),
        in_specs=[
            pl.BlockSpec((1, rows, width), lambda j, *_: (j, 0, 0)),
            pl.BlockSpec(memory_space=pl.ANY),
            pl.BlockSpec(memory_space=pl.ANY),
        ],
        out_specs=[
            pl.BlockSpec((1, rows, HD), lambda j, *_: (j, 0, 0)),
            pl.BlockSpec((1, rows, HD), lambda j, *_: (j, 0, 0)),
        ],
        scratch_shapes=[
            pltpu.VMEM((2, pblk, block, width), prefix_keys.dtype),
            pltpu.VMEM((2, pblk, block, width), prefix_values.dtype),
            pltpu.SemaphoreType.DMA((2, 2, pblk // 8)),
        ],
    )
    cost = pl.CostEstimate(
        flops=4 * local_groups * rows * tokens * width,
        transcendentals=local_groups * rows * tokens,
        bytes_accessed=2 * local_groups * tokens * width * 2 + 3 * local_groups * rows * width * 2,
    )
    return pl.pallas_call(
        kernel,
        grid_spec=grid_spec,
        out_shape=[
            jax.ShapeDtypeStruct((local_groups, rows, HD), jnp.float32),
            jax.ShapeDtypeStruct((local_groups, rows, HD), jnp.float32),
        ],
        compiler_params=pltpu.CompilerParams(dimension_semantics=("arbitrary",)),
        cost_estimate=cost,
    )(table.reshape(-1), lengths, queries, prefix_keys, prefix_values)


def body(
    hidden,
    query_weight,
    out_weight,
    prefix_keys,
    prefix_values,
    block_table,
    prompt_len,
    prompt_group,
    suffix_keys,
    suffix_values,
    suffix_len,
):
    groups = lax.axis_size("group")
    local_groups = block_table.shape[0]
    first_group = lax.axis_index("group") * local_groups
    requests = hidden.shape[0]
    width = prefix_keys.shape[2]
    kv_heads = width // HD
    q_heads = query_weight.shape[1] // HD
    share = q_heads // kv_heads
    score_scale = 1.0 / math.sqrt(HD)

    projected = jnp.dot(hidden, query_weight, preferred_element_type=jnp.float32).reshape(
        requests, q_heads, HD
    )
    position = prompt_len[prompt_group] + suffix_len - 1
    rotated = rotate(projected, position).astype(jnp.bfloat16)

    slots = jnp.arange(groups * local_groups, dtype=jnp.int32)
    picks = (slots[:, None] == prompt_group[None, :]).astype(jnp.bfloat16)
    outgoing = jnp.dot(
        picks, rotated.reshape(requests, q_heads * HD), preferred_element_type=jnp.float32
    ).astype(jnp.bfloat16)
    arrived = lax.all_to_all(
        outgoing.reshape(groups, local_groups, q_heads * HD),
        "group",
        split_axis=0,
        concat_axis=0,
        tiled=True,
    )
    far_queries = jnp.transpose(
        arrived.reshape(groups, local_groups, kv_heads, share, HD), (1, 0, 2, 3, 4)
    )
    far_queries = spread_lanes(far_queries, kv_heads).reshape(
        local_groups, groups * q_heads, width
    )
    my_lengths = lax.dynamic_slice_in_dim(prompt_len, first_group, local_groups)
    held_acc, held_stat = far_attention(
        block_table, my_lengths, far_queries, prefix_keys, prefix_values, share, score_scale
    )
    held_acc = jnp.transpose(held_acc.reshape(local_groups, groups, q_heads, HD), (1, 0, 2, 3))
    held_peak = held_stat[:, :, 0]
    held_total = held_stat[:, :, HD // 2]
    stats = jnp.concatenate(
        [
            held_peak.reshape(local_groups, groups, q_heads),
            held_total.reshape(local_groups, groups, q_heads),
            jnp.zeros((local_groups, groups, HD - 2 * q_heads), jnp.float32),
        ],
        axis=-1,
    )
    stats = jnp.transpose(stats, (1, 0, 2))[:, :, None, :]
    packed = jnp.concatenate([held_acc, stats], axis=2)
    back = lax.all_to_all(packed, "group", split_axis=0, concat_axis=0, tiled=True)
    holder = prompt_group // local_groups
    slot_index = prompt_group % local_groups
    mine = back[holder, slot_index]
    far_acc = mine[:, :q_heads, :]
    far_peak = mine[:, q_heads, :q_heads]
    far_total = mine[:, q_heads, q_heads : 2 * q_heads]

    near_queries = spread_lanes(rotated.reshape(requests, kv_heads, share, HD), kv_heads)
    own_count = suffix_keys.shape[1]
    near_valid = jnp.arange(own_count, dtype=jnp.int32)[None, None, :] < suffix_len[:, None, None]
    near_scores = (
        jnp.einsum("rqc,rtc->rqt", near_queries, suffix_keys, preferred_element_type=jnp.float32)
        * score_scale
    )
    near_peak, near_total, near_weights = softmax_parts(near_scores, near_valid)
    near_wide = jnp.einsum(
        "rqt,rtc->rqc", near_weights, suffix_values, preferred_element_type=jnp.float32
    )
    near_acc = pick_lanes(near_wide, kv_heads).reshape(requests, q_heads, HD)
    attn = combine(far_peak, far_total, far_acc, near_peak, near_total, near_acc)
    attn = attn.reshape(requests, q_heads * HD).astype(jnp.bfloat16)
    partial_out = jnp.dot(attn, out_weight, preferred_element_type=jnp.float32)
    return lax.psum_scatter(partial_out, "tensor", scatter_dimension=1, tiled=True).astype(
        jnp.bfloat16
    )


def solution(mesh):
    in_specs = (
        P("group", None),
        P(None, "tensor"),
        P("tensor", None),
        P("group", None, "tensor"),
        P("group", None, "tensor"),
        P("group", None),
        P(),
        P("group"),
        P("group", None, "tensor"),
        P("group", None, "tensor"),
        P("group"),
    )
    out_specs = P("group", "tensor")
    return jax.shard_map(body, mesh=mesh, in_specs=in_specs, out_specs=out_specs, check_vma=False)
```

```python
import math

import jax
import jax.numpy as jnp
from jax import lax
from jax.experimental import pallas as pl
from jax.experimental.pallas import tpu as pltpu
from jax.sharding import PartitionSpec as P

HD = 128


rope_base = 10000.0
masked_score = -1e30


def rotate(projected, position):
    half = projected.shape[-1] // 2
    freqs = rope_base ** (-(2.0 * jnp.arange(half, dtype=jnp.float32)) / projected.shape[-1])
    angles = position.astype(jnp.float32)[:, None, None] * freqs
    cosine = jnp.cos(angles)
    sine = jnp.sin(angles)
    former = projected[..., :half]
    latter = projected[..., half:]
    return jnp.concatenate(
        [former * cosine - latter * sine, latter * cosine + former * sine], axis=-1
    )


def softmax_parts(scores, valid_mask):
    masked = jnp.where(valid_mask, scores, masked_score)
    maximum = jnp.max(masked, axis=-1)
    weights = jnp.where(valid_mask, jnp.exp(masked - maximum[..., None]), 0.0)
    return (maximum, jnp.sum(weights, axis=-1), weights.astype(jnp.bfloat16))


def combine(far_peak, far_total, far_acc, near_peak, near_total, near_acc):
    highest = jnp.maximum(far_peak, near_peak)
    far_factor = jnp.exp(far_peak - highest)
    near_factor = jnp.exp(near_peak - highest)
    numer = far_acc * far_factor[..., None] + near_acc * near_factor[..., None]
    denom = far_total * far_factor + near_total * near_factor
    return numer / denom[..., None]


def spread_lanes(queries, kv_heads):
    lead = queries.shape[:-3]
    share = queries.shape[-2]
    eye = (jnp.arange(kv_heads)[:, None] == jnp.arange(kv_heads)[None, :]).astype(queries.dtype)
    eye = eye.reshape((1,) * len(lead) + (kv_heads, 1, kv_heads, 1))
    wide = queries[..., None, :] * eye
    return wide.reshape(lead + (kv_heads * share, kv_heads * HD))


def pick_lanes(wide, kv_heads):
    lead = wide.shape[:-2]
    share = wide.shape[-2] // kv_heads
    w = wide.reshape(lead + (kv_heads, share, kv_heads, HD))
    return jnp.stack([w[..., k, :, k, :] for k in range(kv_heads)], axis=-3)


def far_kernel(
    table_ref, len_ref, q_ref, k_hbm, v_hbm, out_ref, kbuf, vbuf, sbuf, wbuf, sems, *, share, scale
):
    j = pl.program_id(0)
    steps = pl.num_programs(0)
    pblk = kbuf.shape[1]
    block = kbuf.shape[2]
    width = kbuf.shape[3]
    kv_heads = width // HD
    sources = out_ref.shape[0]
    q_heads = out_ref.shape[2] - 1
    chunk = 8
    tile_blocks = 16
    tile = tile_blocks * block

    @pl.when(j == 0)
    def _():
        vbuf[...] = jnp.zeros_like(vbuf)

    def used_chunks(group):
        return (len_ref[group] + block * chunk - 1) // (block * chunk)

    def fetch(group, slot):
        def one(c, carry):
            for i in range(chunk):
                b = c * chunk + i
                idx = table_ref[group * pblk + b]
                pltpu.make_async_copy(k_hbm.at[idx], kbuf.at[slot, b], sems.at[0, slot, c]).start()
                pltpu.make_async_copy(v_hbm.at[idx], vbuf.at[slot, b], sems.at[1, slot, c]).start()
            return carry

        lax.fori_loop(0, used_chunks(group), one, 0)

    @pl.when(j == 0)
    def _():
        fetch(0, 0)

    slot = j % 2

    @pl.when(j + 1 < steps)
    def _():
        fetch(j + 1, 1 - slot)

    def settle(c, carry):
        part = pl.ds(pl.multiple_of(c * chunk, chunk), chunk)
        pltpu.make_async_copy(
            k_hbm.at[pl.ds(0, chunk)], kbuf.at[slot, part], sems.at[0, slot, c]
        ).wait()
        pltpu.make_async_copy(
            v_hbm.at[pl.ds(0, chunk)], vbuf.at[slot, part], sems.at[1, slot, c]
        ).wait()
        return carry

    lax.fori_loop(0, used_chunks(j), settle, 0)

    length = len_ref[j]
    used_tiles = (length + tile - 1) // tile
    queries = q_ref[0]

    def score_tile(c, carry):
        keys = kbuf[slot, pl.ds(pl.multiple_of(c * tile_blocks, tile_blocks), tile_blocks)]
        part = lax.dot_general(
            queries, keys.reshape(tile, width), (((1,), (1,)), ((), ())),
            preferred_element_type=jnp.float32,
        )
        sbuf[:, pl.ds(pl.multiple_of(c * tile, tile), tile)] = part * scale
        return carry

    lax.fori_loop(0, used_tiles, score_tile, 0)
    scores = sbuf[...]
    valid = lax.broadcasted_iota(jnp.int32, scores.shape, 1) < length
    masked = jnp.where(valid, scores, masked_score)
    peak = jnp.max(masked, axis=1, keepdims=True)
    weights = jnp.where(valid, jnp.exp(masked - peak), 0.0)
    total = jnp.sum(weights, axis=1, keepdims=True)
    wbuf[...] = weights.astype(jnp.bfloat16)
    rows = scores.shape[0]

    def value_tile(c, acc):
        values = vbuf[slot, pl.ds(pl.multiple_of(c * tile_blocks, tile_blocks), tile_blocks)]
        w = wbuf[:, pl.ds(pl.multiple_of(c * tile, tile), tile)]
        return acc + jnp.dot(
            w, values.reshape(tile, width), preferred_element_type=jnp.float32
        )

    wide = lax.fori_loop(0, used_tiles, value_tile, jnp.zeros((rows, width), jnp.float32))
    row_head = (lax.broadcasted_iota(jnp.int32, (rows, HD), 0) // share) % kv_heads
    acc = jnp.zeros((rows, HD), jnp.float32)
    for k in range(kv_heads):
        acc = jnp.where(row_head == k, wide[:, k * HD : (k + 1) * HD], acc)
    out_ref[:, 0, :q_heads, :] = acc.reshape(sources, q_heads, HD)
    lane = lax.broadcasted_iota(jnp.int32, (sources, q_heads, HD), 2)
    head = lax.broadcasted_iota(jnp.int32, (sources, q_heads, HD), 1)
    peak3 = jnp.broadcast_to(peak, (rows, HD)).reshape(sources, q_heads, HD)
    total3 = jnp.broadcast_to(total, (rows, HD)).reshape(sources, q_heads, HD)
    stat = jnp.where(lane == head, peak3, 0.0) + jnp.where(lane == head + q_heads, total3, 0.0)
    out_ref[:, 0, q_heads, :] = jnp.sum(stat, axis=1)


def far_attention(table, lengths, queries, prefix_keys, prefix_values, share, scale, sources):
    local_groups, pblk = table.shape
    assert pblk % 16 == 0
    _, rows, width = queries.shape
    q_heads = rows // sources
    assert 2 * q_heads <= HD
    block = prefix_keys.shape[1]
    tokens = pblk * block
    kernel = lambda *refs: far_kernel(*refs, share=share, scale=scale)
    grid_spec = pltpu.PrefetchScalarGridSpec(
        num_scalar_prefetch=2,
        grid=(local_groups,),
        in_specs=[
            pl.BlockSpec((1, rows, width), lambda j, *_: (j, 0, 0)),
            pl.BlockSpec(memory_space=pl.ANY),
            pl.BlockSpec(memory_space=pl.ANY),
        ],
        out_specs=pl.BlockSpec((sources, 1, q_heads + 1, HD), lambda j, *_: (0, j, 0, 0)),
        scratch_shapes=[
            pltpu.VMEM((2, pblk, block, width), prefix_keys.dtype),
            pltpu.VMEM((2, pblk, block, width), prefix_values.dtype),
            pltpu.VMEM((rows, tokens), jnp.float32),
            pltpu.VMEM((rows, tokens), jnp.bfloat16),
            pltpu.SemaphoreType.DMA((2, 2, pblk // 8)),
        ],
    )
    cost = pl.CostEstimate(
        flops=4 * local_groups * rows * tokens * width,
        transcendentals=local_groups * rows * tokens,
        bytes_accessed=2 * local_groups * tokens * width * 2 + 3 * local_groups * rows * width * 2,
    )
    return pl.pallas_call(
        kernel,
        grid_spec=grid_spec,
        out_shape=jax.ShapeDtypeStruct((sources, local_groups, q_heads + 1, HD), jnp.float32),
        compiler_params=pltpu.CompilerParams(dimension_semantics=("arbitrary",)),
        cost_estimate=cost,
    )(table.reshape(-1), lengths, queries, prefix_keys, prefix_values)


def body(
    hidden,
    query_weight,
    out_weight,
    prefix_keys,
    prefix_values,
    block_table,
    prompt_len,
    prompt_group,
    suffix_keys,
    suffix_values,
    suffix_len,
):
    groups = lax.axis_size("group")
    local_groups = block_table.shape[0]
    first_group = lax.axis_index("group") * local_groups
    requests = hidden.shape[0]
    width = prefix_keys.shape[2]
    kv_heads = width // HD
    q_heads = query_weight.shape[1] // HD
    share = q_heads // kv_heads
    score_scale = 1.0 / math.sqrt(HD)

    projected = jnp.dot(hidden, query_weight, preferred_element_type=jnp.float32).reshape(
        requests, q_heads, HD
    )
    position = prompt_len[prompt_group] + suffix_len - 1
    rotated = rotate(projected, position).astype(jnp.bfloat16)

    slots = jnp.arange(groups * local_groups, dtype=jnp.int32)
    picks = (slots[:, None] == prompt_group[None, :]).astype(jnp.bfloat16)
    outgoing = jnp.dot(
        picks, rotated.reshape(requests, q_heads * HD), preferred_element_type=jnp.float32
    ).astype(jnp.bfloat16)
    arrived = lax.all_to_all(
        outgoing.reshape(groups, local_groups, q_heads * HD),
        "group",
        split_axis=0,
        concat_axis=0,
        tiled=True,
    )
    far_queries = jnp.transpose(
        arrived.reshape(groups, local_groups, kv_heads, share, HD), (1, 0, 2, 3, 4)
    )
    far_queries = spread_lanes(far_queries, kv_heads).reshape(
        local_groups, groups * q_heads, width
    )
    my_lengths = lax.dynamic_slice_in_dim(prompt_len, first_group, local_groups)
    packed = far_attention(
        block_table, my_lengths, far_queries, prefix_keys, prefix_values, share, score_scale,
        groups,
    )
    back = lax.all_to_all(packed, "group", split_axis=0, concat_axis=0, tiled=True)
    holder = prompt_group // local_groups
    slot_index = prompt_group % local_groups
    mine = back[holder, slot_index]
    far_acc = mine[:, :q_heads, :]
    far_peak = mine[:, q_heads, :q_heads]
    far_total = mine[:, q_heads, q_heads : 2 * q_heads]

    near_queries = spread_lanes(rotated.reshape(requests, kv_heads, share, HD), kv_heads)
    own_count = suffix_keys.shape[1]
    near_valid = jnp.arange(own_count, dtype=jnp.int32)[None, None, :] < suffix_len[:, None, None]
    near_scores = (
        jnp.einsum("rqc,rtc->rqt", near_queries, suffix_keys, preferred_element_type=jnp.float32)
        * score_scale
    )
    near_peak, near_total, near_weights = softmax_parts(near_scores, near_valid)
    near_wide = jnp.einsum(
        "rqt,rtc->rqc", near_weights, suffix_values, preferred_element_type=jnp.float32
    )
    near_acc = pick_lanes(near_wide, kv_heads).reshape(requests, q_heads, HD)
    attn = combine(far_peak, far_total, far_acc, near_peak, near_total, near_acc)
    attn = attn.reshape(requests, q_heads * HD).astype(jnp.bfloat16)
    partial_out = jnp.dot(attn, out_weight, preferred_element_type=jnp.float32)
    return lax.psum_scatter(partial_out, "tensor", scatter_dimension=1, tiled=True).astype(
        jnp.bfloat16
    )


def solution(mesh):
    in_specs = (
        P("group", None),
        P(None, "tensor"),
        P("tensor", None),
        P("group", None, "tensor"),
        P("group", None, "tensor"),
        P("group", None),
        P(),
        P("group"),
        P("group", None, "tensor"),
        P("group", None, "tensor"),
        P("group"),
    )
    out_specs = P("group", "tensor")
    return jax.shard_map(body, mesh=mesh, in_specs=in_specs, out_specs=out_specs, check_vma=False)
```

```python
import math

import jax
import jax.numpy as jnp
from jax import lax
from jax.experimental import pallas as pl
from jax.experimental.pallas import tpu as pltpu
from jax.sharding import PartitionSpec as P

HD = 128


rope_base = 10000.0
masked_score = -1e30


def rotate(projected, position):
    half = projected.shape[-1] // 2
    freqs = rope_base ** (-(2.0 * jnp.arange(half, dtype=jnp.float32)) / projected.shape[-1])
    angles = position.astype(jnp.float32)[:, None, None] * freqs
    cosine = jnp.cos(angles)
    sine = jnp.sin(angles)
    former = projected[..., :half]
    latter = projected[..., half:]
    return jnp.concatenate(
        [former * cosine - latter * sine, latter * cosine + former * sine], axis=-1
    )


def softmax_parts(scores, valid_mask):
    masked = jnp.where(valid_mask, scores, masked_score)
    maximum = jnp.max(masked, axis=-1)
    weights = jnp.where(valid_mask, jnp.exp(masked - maximum[..., None]), 0.0)
    return (maximum, jnp.sum(weights, axis=-1), weights.astype(jnp.bfloat16))


def combine(far_peak, far_total, far_acc, near_peak, near_total, near_acc):
    highest = jnp.maximum(far_peak, near_peak)
    far_factor = jnp.exp(far_peak - highest)
    near_factor = jnp.exp(near_peak - highest)
    numer = far_acc * far_factor[..., None] + near_acc * near_factor[..., None]
    denom = far_total * far_factor + near_total * near_factor
    return numer / denom[..., None]


def spread_lanes(queries, kv_heads):
    lead = queries.shape[:-3]
    share = queries.shape[-2]
    eye = (jnp.arange(kv_heads)[:, None] == jnp.arange(kv_heads)[None, :]).astype(queries.dtype)
    eye = eye.reshape((1,) * len(lead) + (kv_heads, 1, kv_heads, 1))
    wide = queries[..., None, :] * eye
    return wide.reshape(lead + (kv_heads * share, kv_heads * HD))


def pick_lanes(wide, kv_heads):
    lead = wide.shape[:-2]
    share = wide.shape[-2] // kv_heads
    w = wide.reshape(lead + (kv_heads, share, kv_heads, HD))
    return jnp.stack([w[..., k, :, k, :] for k in range(kv_heads)], axis=-3)


def far_kernel(
    table_ref, len_ref, q_ref, k_hbm, v_hbm, out_ref, kbuf, vbuf, sbuf, wbuf, abuf, sems, *,
    share, scale,
):
    j = pl.program_id(0)
    steps = pl.num_programs(0)
    pblk = kbuf.shape[1]
    block = kbuf.shape[2]
    width = kbuf.shape[3]
    kv_heads = width // HD
    sources = out_ref.shape[0]
    q_heads = out_ref.shape[2] - 1
    chunk = 8
    tile_blocks = 16
    tile = tile_blocks * block

    @pl.when(j == 0)
    def _():
        vbuf[...] = jnp.zeros_like(vbuf)

    def used_chunks(group):
        return (len_ref[group] + block * chunk - 1) // (block * chunk)

    def fetch(group, slot):
        def one(c, carry):
            for i in range(chunk):
                b = c * chunk + i
                idx = table_ref[group * pblk + b]
                pltpu.make_async_copy(k_hbm.at[idx], kbuf.at[slot, b], sems.at[0, slot, c]).start()
                pltpu.make_async_copy(v_hbm.at[idx], vbuf.at[slot, b], sems.at[1, slot, c]).start()
            return carry

        lax.fori_loop(0, used_chunks(group), one, 0)

    @pl.when(j == 0)
    def _():
        fetch(0, 0)

    slot = j % 2

    @pl.when(j + 1 < steps)
    def _():
        fetch(j + 1, 1 - slot)

    def settle(c, carry):
        part = pl.ds(pl.multiple_of(c * chunk, chunk), chunk)
        pltpu.make_async_copy(
            k_hbm.at[pl.ds(0, chunk)], kbuf.at[slot, part], sems.at[0, slot, c]
        ).wait()
        pltpu.make_async_copy(
            v_hbm.at[pl.ds(0, chunk)], vbuf.at[slot, part], sems.at[1, slot, c]
        ).wait()
        return carry

    lax.fori_loop(0, used_chunks(j), settle, 0)

    length = len_ref[j]
    used_tiles = (length + tile - 1) // tile
    queries = q_ref[0]

    n_tiles = pblk // tile_blocks
    for c in range(n_tiles):

        @pl.when(c < used_tiles)
        def _():
            keys = kbuf[slot, c * tile_blocks : (c + 1) * tile_blocks].reshape(tile, width)
            part = lax.dot_general(
                queries, keys, (((1,), (1,)), ((), ())), preferred_element_type=jnp.float32
            )
            sbuf[:, c * tile : (c + 1) * tile] = part * scale

    scores = sbuf[...]
    valid = lax.broadcasted_iota(jnp.int32, scores.shape, 1) < length
    masked = jnp.where(valid, scores, masked_score)
    peak = jnp.max(masked, axis=1, keepdims=True)
    weights = jnp.where(valid, jnp.exp(masked - peak), 0.0)
    total = jnp.sum(weights, axis=1, keepdims=True)
    wbuf[...] = weights.astype(jnp.bfloat16)
    rows = scores.shape[0]
    abuf[...] = jnp.zeros_like(abuf)
    for c in range(n_tiles):

        @pl.when(c < used_tiles)
        def _():
            values = vbuf[slot, c * tile_blocks : (c + 1) * tile_blocks].reshape(tile, width)
            abuf[...] += jnp.dot(
                wbuf[:, c * tile : (c + 1) * tile], values, preferred_element_type=jnp.float32
            )

    wide = abuf[...]
    row_head = (lax.broadcasted_iota(jnp.int32, (rows, HD), 0) // share) % kv_heads
    acc = jnp.zeros((rows, HD), jnp.float32)
    for k in range(kv_heads):
        acc = jnp.where(row_head == k, wide[:, k * HD : (k + 1) * HD], acc)
    out_ref[:, 0, :q_heads, :] = acc.reshape(sources, q_heads, HD)
    lane = lax.broadcasted_iota(jnp.int32, (sources, q_heads, HD), 2)
    head = lax.broadcasted_iota(jnp.int32, (sources, q_heads, HD), 1)
    peak3 = jnp.broadcast_to(peak, (rows, HD)).reshape(sources, q_heads, HD)
    total3 = jnp.broadcast_to(total, (rows, HD)).reshape(sources, q_heads, HD)
    stat = jnp.where(lane == head, peak3, 0.0) + jnp.where(lane == head + q_heads, total3, 0.0)
    out_ref[:, 0, q_heads, :] = jnp.sum(stat, axis=1)


def far_attention(table, lengths, queries, prefix_keys, prefix_values, share, scale, sources):
    local_groups, pblk = table.shape
    assert pblk % 16 == 0
    _, rows, width = queries.shape
    q_heads = rows // sources
    assert 2 * q_heads <= HD
    block = prefix_keys.shape[1]
    tokens = pblk * block
    kernel = lambda *refs: far_kernel(*refs, share=share, scale=scale)
    grid_spec = pltpu.PrefetchScalarGridSpec(
        num_scalar_prefetch=2,
        grid=(local_groups,),
        in_specs=[
            pl.BlockSpec((1, rows, width), lambda j, *_: (j, 0, 0)),
            pl.BlockSpec(memory_space=pl.ANY),
            pl.BlockSpec(memory_space=pl.ANY),
        ],
        out_specs=pl.BlockSpec((sources, 1, q_heads + 1, HD), lambda j, *_: (0, j, 0, 0)),
        scratch_shapes=[
            pltpu.VMEM((2, pblk, block, width), prefix_keys.dtype),
            pltpu.VMEM((2, pblk, block, width), prefix_values.dtype),
            pltpu.VMEM((rows, tokens), jnp.float32),
            pltpu.VMEM((rows, tokens), jnp.bfloat16),
            pltpu.VMEM((rows, width), jnp.float32),
            pltpu.SemaphoreType.DMA((2, 2, pblk // 8)),
        ],
    )
    cost = pl.CostEstimate(
        flops=4 * local_groups * rows * tokens * width,
        transcendentals=local_groups * rows * tokens,
        bytes_accessed=2 * local_groups * tokens * width * 2 + 3 * local_groups * rows * width * 2,
    )
    return pl.pallas_call(
        kernel,
        grid_spec=grid_spec,
        out_shape=jax.ShapeDtypeStruct((sources, local_groups, q_heads + 1, HD), jnp.float32),
        compiler_params=pltpu.CompilerParams(dimension_semantics=("arbitrary",)),
        cost_estimate=cost,
    )(table.reshape(-1), lengths, queries, prefix_keys, prefix_values)


def body(
    hidden,
    query_weight,
    out_weight,
    prefix_keys,
    prefix_values,
    block_table,
    prompt_len,
    prompt_group,
    suffix_keys,
    suffix_values,
    suffix_len,
):
    groups = lax.axis_size("group")
    local_groups = block_table.shape[0]
    first_group = lax.axis_index("group") * local_groups
    requests = hidden.shape[0]
    width = prefix_keys.shape[2]
    kv_heads = width // HD
    q_heads = query_weight.shape[1] // HD
    share = q_heads // kv_heads
    score_scale = 1.0 / math.sqrt(HD)

    projected = jnp.dot(hidden, query_weight, preferred_element_type=jnp.float32).reshape(
        requests, q_heads, HD
    )
    position = prompt_len[prompt_group] + suffix_len - 1
    rotated = rotate(projected, position).astype(jnp.bfloat16)

    slots = jnp.arange(groups * local_groups, dtype=jnp.int32)
    picks = (slots[:, None] == prompt_group[None, :]).astype(jnp.bfloat16)
    outgoing = jnp.dot(
        picks, rotated.reshape(requests, q_heads * HD), preferred_element_type=jnp.float32
    ).astype(jnp.bfloat16)
    arrived = lax.all_to_all(
        outgoing.reshape(groups, local_groups, q_heads * HD),
        "group",
        split_axis=0,
        concat_axis=0,
        tiled=True,
    )
    far_queries = jnp.transpose(
        arrived.reshape(groups, local_groups, kv_heads, share, HD), (1, 0, 2, 3, 4)
    )
    far_queries = spread_lanes(far_queries, kv_heads).reshape(
        local_groups, groups * q_heads, width
    )
    my_lengths = lax.dynamic_slice_in_dim(prompt_len, first_group, local_groups)
    packed = far_attention(
        block_table, my_lengths, far_queries, prefix_keys, prefix_values, share, score_scale,
        groups,
    )
    back = lax.all_to_all(packed, "group", split_axis=0, concat_axis=0, tiled=True)
    holder = prompt_group // local_groups
    slot_index = prompt_group % local_groups
    mine = back[holder, slot_index]
    far_acc = mine[:, :q_heads, :]
    far_peak = mine[:, q_heads, :q_heads]
    far_total = mine[:, q_heads, q_heads : 2 * q_heads]

    near_queries = spread_lanes(rotated.reshape(requests, kv_heads, share, HD), kv_heads)
    own_count = suffix_keys.shape[1]
    near_valid = jnp.arange(own_count, dtype=jnp.int32)[None, None, :] < suffix_len[:, None, None]
    near_scores = (
        jnp.einsum("rqc,rtc->rqt", near_queries, suffix_keys, preferred_element_type=jnp.float32)
        * score_scale
    )
    near_peak, near_total, near_weights = softmax_parts(near_scores, near_valid)
    near_wide = jnp.einsum(
        "rqt,rtc->rqc", near_weights, suffix_values, preferred_element_type=jnp.float32
    )
    near_acc = pick_lanes(near_wide, kv_heads).reshape(requests, q_heads, HD)
    attn = combine(far_peak, far_total, far_acc, near_peak, near_total, near_acc)
    attn = attn.reshape(requests, q_heads * HD).astype(jnp.bfloat16)
    partial_out = jnp.dot(attn, out_weight, preferred_element_type=jnp.float32)
    return lax.psum_scatter(partial_out, "tensor", scatter_dimension=1, tiled=True).astype(
        jnp.bfloat16
    )


def solution(mesh):
    in_specs = (
        P("group", None),
        P(None, "tensor"),
        P("tensor", None),
        P("group", None, "tensor"),
        P("group", None, "tensor"),
        P("group", None),
        P(),
        P("group"),
        P("group", None, "tensor"),
        P("group", None, "tensor"),
        P("group"),
    )
    out_specs = P("group", "tensor")
    return jax.shard_map(body, mesh=mesh, in_specs=in_specs, out_specs=out_specs, check_vma=False)
```

```python
import math

import jax
import jax.numpy as jnp
from jax import lax
from jax.experimental import pallas as pl
from jax.experimental.pallas import tpu as pltpu
from jax.sharding import PartitionSpec as P

HD = 128


rope_base = 10000.0
masked_score = -1e30


def rotate(projected, position):
    half = projected.shape[-1] // 2
    freqs = rope_base ** (-(2.0 * jnp.arange(half, dtype=jnp.float32)) / projected.shape[-1])
    angles = position.astype(jnp.float32)[:, None, None] * freqs
    cosine = jnp.cos(angles)
    sine = jnp.sin(angles)
    former = projected[..., :half]
    latter = projected[..., half:]
    return jnp.concatenate(
        [former * cosine - latter * sine, latter * cosine + former * sine], axis=-1
    )


def softmax_parts(scores, valid_mask):
    masked = jnp.where(valid_mask, scores, masked_score)
    maximum = jnp.max(masked, axis=-1)
    weights = jnp.where(valid_mask, jnp.exp(masked - maximum[..., None]), 0.0)
    return (maximum, jnp.sum(weights, axis=-1), weights.astype(jnp.bfloat16))


def combine(far_peak, far_total, far_acc, near_peak, near_total, near_acc):
    highest = jnp.maximum(far_peak, near_peak)
    far_factor = jnp.exp(far_peak - highest)
    near_factor = jnp.exp(near_peak - highest)
    numer = far_acc * far_factor[..., None] + near_acc * near_factor[..., None]
    denom = far_total * far_factor + near_total * near_factor
    return numer / denom[..., None]


def spread_lanes(queries, kv_heads):
    lead = queries.shape[:-3]
    share = queries.shape[-2]
    eye = (jnp.arange(kv_heads)[:, None] == jnp.arange(kv_heads)[None, :]).astype(queries.dtype)
    eye = eye.reshape((1,) * len(lead) + (kv_heads, 1, kv_heads, 1))
    wide = queries[..., None, :] * eye
    return wide.reshape(lead + (kv_heads * share, kv_heads * HD))


def pick_lanes(wide, kv_heads):
    lead = wide.shape[:-2]
    share = wide.shape[-2] // kv_heads
    w = wide.reshape(lead + (kv_heads, share, kv_heads, HD))
    return jnp.stack([w[..., k, :, k, :] for k in range(kv_heads)], axis=-3)


def far_kernel(
    table_ref, len_ref, q_ref, k_hbm, v_hbm, acc_ref, stat_ref, kbuf, vbuf, sems, *, share, scale
):
    j = pl.program_id(0)
    steps = pl.num_programs(0)
    pblk = kbuf.shape[1]
    width = kbuf.shape[3]
    kv_heads = width // HD

    block = kbuf.shape[2]

    @pl.when(j == 0)
    def _():
        vbuf[...] = jnp.zeros_like(vbuf)

    chunk = 8

    def used_chunks(group):
        return (len_ref[group] + block * chunk - 1) // (block * chunk)

    def fetch(group, slot):
        def one(c, carry):
            for i in range(chunk):
                b = c * chunk + i
                idx = table_ref[group * pblk + b]
                pltpu.make_async_copy(k_hbm.at[idx], kbuf.at[slot, b], sems.at[0, slot, c]).start()
                pltpu.make_async_copy(v_hbm.at[idx], vbuf.at[slot, b], sems.at[1, slot, c]).start()
            return carry

        lax.fori_loop(0, used_chunks(group), one, 0)

    @pl.when(j == 0)
    def _():
        fetch(0, 0)

    slot = j % 2

    @pl.when(j + 1 < steps)
    def _():
        fetch(j + 1, 1 - slot)

    def settle(c, carry):
        part = pl.ds(pl.multiple_of(c * chunk, chunk), chunk)
        pltpu.make_async_copy(
            k_hbm.at[pl.ds(0, chunk)], kbuf.at[slot, part], sems.at[0, slot, c]
        ).wait()
        pltpu.make_async_copy(
            v_hbm.at[pl.ds(0, chunk)], vbuf.at[slot, part], sems.at[1, slot, c]
        ).wait()
        return carry

    lax.fori_loop(0, used_chunks(j), settle, 0)
    keys = kbuf[slot].reshape(-1, width)
    values = vbuf[slot].reshape(-1, width)
    queries = q_ref[0]
    scores = (
        lax.dot_general(
            queries, keys, (((1,), (1,)), ((), ())), preferred_element_type=jnp.float32
        )
        * scale
    )
    valid = lax.broadcasted_iota(jnp.int32, scores.shape, 1) < len_ref[j]
    masked = jnp.where(valid, scores, masked_score)
    peak = jnp.max(masked, axis=1, keepdims=True)
    weights = jnp.where(valid, jnp.exp(masked - peak), 0.0)
    total = jnp.sum(weights, axis=1, keepdims=True)
    wide = jnp.dot(weights.astype(jnp.bfloat16), values, preferred_element_type=jnp.float32)
    rows = wide.shape[0]
    row_head = (lax.broadcasted_iota(jnp.int32, (rows, HD), 0) // share) % kv_heads
    acc = jnp.zeros((rows, HD), jnp.float32)
    for k in range(kv_heads):
        acc = jnp.where(row_head == k, wide[:, k * HD : (k + 1) * HD], acc)
    acc_ref[0] = acc
    lane = lax.broadcasted_iota(jnp.int32, (rows, HD), 1)
    stat_ref[0] = jnp.where(lane < HD // 2, peak, total)


def far_attention(table, lengths, queries, prefix_keys, prefix_values, share, scale):
    local_groups, pblk = table.shape
    assert pblk % 8 == 0
    _, rows, width = queries.shape
    block = prefix_keys.shape[1]
    tokens = pblk * block
    kernel = lambda *refs: far_kernel(*refs, share=share, scale=scale)
    grid_spec = pltpu.PrefetchScalarGridSpec(
        num_scalar_prefetch=2,
        grid=(local_groups,),
        in_specs=[
            pl.BlockSpec((1, rows, width), lambda j, *_: (j, 0, 0)),
            pl.BlockSpec(memory_space=pl.ANY),
            pl.BlockSpec(memory_space=pl.ANY),
        ],
        out_specs=[
            pl.BlockSpec((1, rows, HD), lambda j, *_: (j, 0, 0)),
            pl.BlockSpec((1, rows, HD), lambda j, *_: (j, 0, 0)),
        ],
        scratch_shapes=[
            pltpu.VMEM((2, pblk, block, width), prefix_keys.dtype),
            pltpu.VMEM((2, pblk, block, width), prefix_values.dtype),
            pltpu.SemaphoreType.DMA((2, 2, pblk // 8)),
        ],
    )
    cost = pl.CostEstimate(
        flops=4 * local_groups * rows * tokens * width,
        transcendentals=local_groups * rows * tokens,
        bytes_accessed=2 * local_groups * tokens * width * 2 + 3 * local_groups * rows * width * 2,
    )
    return pl.pallas_call(
        kernel,
        grid_spec=grid_spec,
        out_shape=[
            jax.ShapeDtypeStruct((local_groups, rows, HD), jnp.float32),
            jax.ShapeDtypeStruct((local_groups, rows, HD), jnp.float32),
        ],
        compiler_params=pltpu.CompilerParams(dimension_semantics=("arbitrary",)),
        cost_estimate=cost,
    )(table.reshape(-1), lengths, queries, prefix_keys, prefix_values)


def body(
    hidden,
    query_weight,
    out_weight,
    prefix_keys,
    prefix_values,
    block_table,
    prompt_len,
    prompt_group,
    suffix_keys,
    suffix_values,
    suffix_len,
):
    groups = lax.axis_size("group")
    local_groups = block_table.shape[0]
    first_group = lax.axis_index("group") * local_groups
    requests = hidden.shape[0]
    width = prefix_keys.shape[2]
    kv_heads = width // HD
    q_heads = query_weight.shape[1] // HD
    share = q_heads // kv_heads
    score_scale = 1.0 / math.sqrt(HD)

    projected = jnp.dot(hidden, query_weight, preferred_element_type=jnp.float32).reshape(
        requests, q_heads, HD
    )
    position = prompt_len[prompt_group] + suffix_len - 1
    rotated = rotate(projected, position).astype(jnp.bfloat16)

    slots = jnp.arange(groups * local_groups, dtype=jnp.int32)
    picks = (slots[:, None] == prompt_group[None, :]).astype(jnp.bfloat16)
    outgoing = jnp.dot(
        picks, rotated.reshape(requests, q_heads * HD), preferred_element_type=jnp.float32
    ).astype(jnp.bfloat16)
    arrived = lax.all_to_all(
        outgoing.reshape(groups, local_groups, q_heads * HD),
        "group",
        split_axis=0,
        concat_axis=0,
        tiled=True,
    )
    far_queries = jnp.transpose(
        arrived.reshape(groups, local_groups, kv_heads, share, HD), (1, 0, 2, 3, 4)
    )
    far_queries = spread_lanes(far_queries, kv_heads).reshape(
        local_groups, groups * q_heads, width
    )
    my_lengths = lax.dynamic_slice_in_dim(prompt_len, first_group, local_groups)
    held_acc, held_stat = far_attention(
        block_table, my_lengths, far_queries, prefix_keys, prefix_values, share, score_scale
    )
    held_acc = jnp.transpose(held_acc.reshape(local_groups, groups, q_heads, HD), (1, 0, 2, 3))
    held_peak = held_stat[:, :, 0]
    held_total = held_stat[:, :, HD // 2]
    stats = jnp.concatenate(
        [
            held_peak.reshape(local_groups, groups, q_heads),
            held_total.reshape(local_groups, groups, q_heads),
            jnp.zeros((local_groups, groups, HD - 2 * q_heads), jnp.float32),
        ],
        axis=-1,
    )
    stats = jnp.transpose(stats, (1, 0, 2))[:, :, None, :]
    packed = jnp.concatenate([held_acc, stats], axis=2)
    back = lax.all_to_all(packed, "group", split_axis=0, concat_axis=0, tiled=True)
    holder = prompt_group // local_groups
    slot_index = prompt_group % local_groups
    mine = back[holder, slot_index]
    far_acc = mine[:, :q_heads, :]
    far_peak = mine[:, q_heads, :q_heads]
    far_total = mine[:, q_heads, q_heads : 2 * q_heads]

    near_queries = spread_lanes(rotated.reshape(requests, kv_heads, share, HD), kv_heads)
    own_count = suffix_keys.shape[1]
    near_valid = jnp.arange(own_count, dtype=jnp.int32)[None, None, :] < suffix_len[:, None, None]
    near_scores = (
        jnp.einsum("rqc,rtc->rqt", near_queries, suffix_keys, preferred_element_type=jnp.float32)
        * score_scale
    )
    near_peak, near_total, near_weights = softmax_parts(near_scores, near_valid)
    near_wide = jnp.einsum(
        "rqt,rtc->rqc", near_weights, suffix_values, preferred_element_type=jnp.float32
    )
    near_acc = pick_lanes(near_wide, kv_heads).reshape(requests, q_heads, HD)
    attn = combine(far_peak, far_total, far_acc, near_peak, near_total, near_acc)
    attn = attn.reshape(requests, q_heads * HD).astype(jnp.bfloat16)
    half = requests // 2
    outs = []
    for rows in (slice(0, half), slice(half, requests)):
        partial_out = jnp.dot(attn[rows], out_weight, preferred_element_type=jnp.float32)
        outs.append(
            lax.psum_scatter(partial_out, "tensor", scatter_dimension=1, tiled=True).astype(
                jnp.bfloat16
            )
        )
    return jnp.concatenate(outs, axis=0)


def solution(mesh):
    in_specs = (
        P("group", None),
        P(None, "tensor"),
        P("tensor", None),
        P("group", None, "tensor"),
        P("group", None, "tensor"),
        P("group", None),
        P(),
        P("group"),
        P("group", None, "tensor"),
        P("group", None, "tensor"),
        P("group"),
    )
    out_specs = P("group", "tensor")
    return jax.shard_map(body, mesh=mesh, in_specs=in_specs, out_specs=out_specs, check_vma=False)
```

```python
import math

import jax
import jax.numpy as jnp
from jax import lax
from jax.experimental import pallas as pl
from jax.experimental.pallas import tpu as pltpu
from jax.sharding import PartitionSpec as P

HD = 128


rope_base = 10000.0
masked_score = -1e30


def rotate(projected, position):
    half = projected.shape[-1] // 2
    freqs = rope_base ** (-(2.0 * jnp.arange(half, dtype=jnp.float32)) / projected.shape[-1])
    angles = position.astype(jnp.float32)[:, None, None] * freqs
    cosine = jnp.cos(angles)
    sine = jnp.sin(angles)
    former = projected[..., :half]
    latter = projected[..., half:]
    return jnp.concatenate(
        [former * cosine - latter * sine, latter * cosine + former * sine], axis=-1
    )


def softmax_parts(scores, valid_mask):
    masked = jnp.where(valid_mask, scores, masked_score)
    maximum = jnp.max(masked, axis=-1)
    weights = jnp.where(valid_mask, jnp.exp(masked - maximum[..., None]), 0.0)
    return (maximum, jnp.sum(weights, axis=-1), weights.astype(jnp.bfloat16))


def combine(far_peak, far_total, far_acc, near_peak, near_total, near_acc):
    highest = jnp.maximum(far_peak, near_peak)
    far_factor = jnp.exp(far_peak - highest)
    near_factor = jnp.exp(near_peak - highest)
    numer = far_acc * far_factor[..., None] + near_acc * near_factor[..., None]
    denom = far_total * far_factor + near_total * near_factor
    return numer / denom[..., None]


def spread_lanes(queries, kv_heads):
    lead = queries.shape[:-3]
    share = queries.shape[-2]
    eye = (jnp.arange(kv_heads)[:, None] == jnp.arange(kv_heads)[None, :]).astype(queries.dtype)
    eye = eye.reshape((1,) * len(lead) + (kv_heads, 1, kv_heads, 1))
    wide = queries[..., None, :] * eye
    return wide.reshape(lead + (kv_heads * share, kv_heads * HD))


def pick_lanes(wide, kv_heads):
    lead = wide.shape[:-2]
    share = wide.shape[-2] // kv_heads
    w = wide.reshape(lead + (kv_heads, share, kv_heads, HD))
    return jnp.stack([w[..., k, :, k, :] for k in range(kv_heads)], axis=-3)


def far_kernel(
    table_ref, len_ref, q_ref, k_hbm, v_hbm, acc_ref, stat_ref, kbuf, vbuf, sems, *, share, scale
):
    j = pl.program_id(0)
    steps = pl.num_programs(0)
    pblk = kbuf.shape[1]
    width = kbuf.shape[3]
    kv_heads = width // HD

    block = kbuf.shape[2]

    @pl.when(j == 0)
    def _():
        vbuf[...] = jnp.zeros_like(vbuf)

    chunk = 8

    def used_chunks(group):
        return (len_ref[group] + block * chunk - 1) // (block * chunk)

    def fetch(group, slot):
        def one(c, carry):
            for i in range(chunk):
                b = c * chunk + i
                idx = table_ref[group * pblk + b]
                pltpu.make_async_copy(k_hbm.at[idx], kbuf.at[slot, b], sems.at[0, slot, c]).start()
                pltpu.make_async_copy(v_hbm.at[idx], vbuf.at[slot, b], sems.at[1, slot, c]).start()
            return carry

        lax.fori_loop(0, used_chunks(group), one, 0)

    @pl.when(j == 0)
    def _():
        fetch(0, 0)

    slot = j % 2

    @pl.when(j + 1 < steps)
    def _():
        fetch(j + 1, 1 - slot)

    def settle(c, carry):
        part = pl.ds(pl.multiple_of(c * chunk, chunk), chunk)
        pltpu.make_async_copy(
            k_hbm.at[pl.ds(0, chunk)], kbuf.at[slot, part], sems.at[0, slot, c]
        ).wait()
        pltpu.make_async_copy(
            v_hbm.at[pl.ds(0, chunk)], vbuf.at[slot, part], sems.at[1, slot, c]
        ).wait()
        return carry

    lax.fori_loop(0, used_chunks(j), settle, 0)
    keys = kbuf[slot].reshape(-1, width)
    values = vbuf[slot].reshape(-1, width)
    queries = q_ref[0]
    scores = (
        lax.dot_general(
            queries, keys, (((1,), (1,)), ((), ())), preferred_element_type=jnp.float32
        )
        * scale
    )
    valid = lax.broadcasted_iota(jnp.int32, scores.shape, 1) < len_ref[j]
    masked = jnp.where(valid, scores, masked_score)
    peak = jnp.max(masked, axis=1, keepdims=True)
    weights = jnp.where(valid, jnp.exp(masked - peak), 0.0)
    total = jnp.sum(weights, axis=1, keepdims=True)
    wide = jnp.dot(weights.astype(jnp.bfloat16), values, preferred_element_type=jnp.float32)
    rows = wide.shape[0]
    row_head = (lax.broadcasted_iota(jnp.int32, (rows, HD), 0) // share) % kv_heads
    acc = jnp.zeros((rows, HD), jnp.float32)
    for k in range(kv_heads):
        acc = jnp.where(row_head == k, wide[:, k * HD : (k + 1) * HD], acc)
    acc_ref[0] = acc
    lane = lax.broadcasted_iota(jnp.int32, (rows, HD), 1)
    stat_ref[0] = jnp.where(lane < HD // 2, peak, total)


def far_attention(table, lengths, queries, prefix_keys, prefix_values, share, scale):
    local_groups, pblk = table.shape
    assert pblk % 8 == 0
    _, rows, width = queries.shape
    block = prefix_keys.shape[1]
    tokens = pblk * block
    kernel = lambda *refs: far_kernel(*refs, share=share, scale=scale)
    grid_spec = pltpu.PrefetchScalarGridSpec(
        num_scalar_prefetch=2,
        grid=(local_groups,),
        in_specs=[
            pl.BlockSpec((1, rows, width), lambda j, *_: (j, 0, 0)),
            pl.BlockSpec(memory_space=pl.ANY),
            pl.BlockSpec(memory_space=pl.ANY),
        ],
        out_specs=[
            pl.BlockSpec((1, rows, HD), lambda j, *_: (j, 0, 0)),
            pl.BlockSpec((1, rows, HD), lambda j, *_: (j, 0, 0)),
        ],
        scratch_shapes=[
            pltpu.VMEM((2, pblk, block, width), prefix_keys.dtype),
            pltpu.VMEM((2, pblk, block, width), prefix_values.dtype),
            pltpu.SemaphoreType.DMA((2, 2, pblk // 8)),
        ],
    )
    cost = pl.CostEstimate(
        flops=4 * local_groups * rows * tokens * width,
        transcendentals=local_groups * rows * tokens,
        bytes_accessed=2 * local_groups * tokens * width * 2 + 3 * local_groups * rows * width * 2,
    )
    return pl.pallas_call(
        kernel,
        grid_spec=grid_spec,
        out_shape=[
            jax.ShapeDtypeStruct((local_groups, rows, HD), jnp.float32),
            jax.ShapeDtypeStruct((local_groups, rows, HD), jnp.float32),
        ],
        compiler_params=pltpu.CompilerParams(dimension_semantics=("arbitrary",)),
        cost_estimate=cost,
    )(table.reshape(-1), lengths, queries, prefix_keys, prefix_values)


def body(
    hidden,
    query_weight,
    out_weight,
    prefix_keys,
    prefix_values,
    block_table,
    prompt_len,
    prompt_group,
    suffix_keys,
    suffix_values,
    suffix_len,
):
    groups = lax.axis_size("group")
    local_groups = block_table.shape[0]
    first_group = lax.axis_index("group") * local_groups
    requests = hidden.shape[0]
    width = prefix_keys.shape[2]
    kv_heads = width // HD
    q_heads = query_weight.shape[1] // HD
    share = q_heads // kv_heads
    score_scale = 1.0 / math.sqrt(HD)

    projected = jnp.dot(hidden, query_weight, preferred_element_type=jnp.float32).reshape(
        requests, q_heads, HD
    )
    position = prompt_len[prompt_group] + suffix_len - 1
    rotated = rotate(projected, position).astype(jnp.bfloat16)

    slots = jnp.arange(groups * local_groups, dtype=jnp.int32)
    picks = (slots[:, None] == prompt_group[None, :]).astype(jnp.bfloat16)
    outgoing = jnp.dot(
        picks, rotated.reshape(requests, q_heads * HD), preferred_element_type=jnp.float32
    ).astype(jnp.bfloat16)
    arrived = lax.all_to_all(
        outgoing.reshape(groups, local_groups, q_heads * HD),
        "group",
        split_axis=0,
        concat_axis=0,
        tiled=True,
    )
    far_queries = jnp.transpose(
        arrived.reshape(groups, local_groups, kv_heads, share, HD), (1, 0, 2, 3, 4)
    )
    far_queries = spread_lanes(far_queries, kv_heads).reshape(
        local_groups, groups * q_heads, width
    )
    my_lengths = lax.dynamic_slice_in_dim(prompt_len, first_group, local_groups)
    held_acc, held_stat = far_attention(
        block_table, my_lengths, far_queries, prefix_keys, prefix_values, share, score_scale
    )
    held_acc = jnp.transpose(held_acc.reshape(local_groups, groups, q_heads, HD), (1, 0, 2, 3))
    held_peak = held_stat[:, :, 0]
    held_total = held_stat[:, :, HD // 2]
    stats = jnp.concatenate(
        [
            held_peak.reshape(local_groups, groups, q_heads),
            held_total.reshape(local_groups, groups, q_heads),
            jnp.zeros((local_groups, groups, HD - 2 * q_heads), jnp.float32),
        ],
        axis=-1,
    )
    stats = jnp.transpose(stats, (1, 0, 2))[:, :, None, :]
    packed = jnp.concatenate([held_acc, stats], axis=2)
    back = lax.all_to_all(packed, "group", split_axis=0, concat_axis=0, tiled=True)
    holder = prompt_group // local_groups
    slot_index = prompt_group % local_groups
    mine = back[holder, slot_index]
    far_acc = mine[:, :q_heads, :]
    far_peak = mine[:, q_heads, :q_heads]
    far_total = mine[:, q_heads, q_heads : 2 * q_heads]

    near_queries = spread_lanes(rotated.reshape(requests, kv_heads, share, HD), kv_heads)
    own_count = suffix_keys.shape[1]
    near_valid = jnp.arange(own_count, dtype=jnp.int32)[None, None, :] < suffix_len[:, None, None]
    near_scores = (
        jnp.einsum("rqc,rtc->rqt", near_queries, suffix_keys, preferred_element_type=jnp.float32)
        * score_scale
    )
    near_peak, near_total, near_weights = softmax_parts(near_scores, near_valid)
    near_wide = jnp.einsum(
        "rqt,rtc->rqc", near_weights, suffix_values, preferred_element_type=jnp.float32
    )
    near_acc = pick_lanes(near_wide, kv_heads).reshape(requests, q_heads, HD)
    attn = combine(far_peak, far_total, far_acc, near_peak, near_total, near_acc)
    attn = attn.reshape(requests, q_heads * HD).astype(jnp.bfloat16)
    parts = lax.axis_size("tensor")
    partial_out = lax.optimization_barrier(
        jnp.dot(attn, out_weight, preferred_element_type=jnp.float32)
    )
    pieces = lax.all_to_all(
        jnp.transpose(partial_out.reshape(requests, parts, -1), (1, 0, 2)),
        "tensor",
        split_axis=0,
        concat_axis=0,
        tiled=True,
    )
    return jnp.sum(pieces, axis=0).astype(jnp.bfloat16)


def solution(mesh):
    in_specs = (
        P("group", None),
        P(None, "tensor"),
        P("tensor", None),
        P("group", None, "tensor"),
        P("group", None, "tensor"),
        P("group", None),
        P(),
        P("group"),
        P("group", None, "tensor"),
        P("group", None, "tensor"),
        P("group"),
    )
    out_specs = P("group", "tensor")
    return jax.shard_map(body, mesh=mesh, in_specs=in_specs, out_specs=out_specs, check_vma=False)
```

```python
import math

import jax
import jax.numpy as jnp
from jax import lax
from jax.experimental import pallas as pl
from jax.experimental.pallas import tpu as pltpu
from jax.sharding import PartitionSpec as P

HD = 128


rope_base = 10000.0
masked_score = -1e30


def rotate(projected, position):
    half = projected.shape[-1] // 2
    freqs = rope_base ** (-(2.0 * jnp.arange(half, dtype=jnp.float32)) / projected.shape[-1])
    angles = position.astype(jnp.float32)[:, None, None] * freqs
    cosine = jnp.cos(angles)
    sine = jnp.sin(angles)
    former = projected[..., :half]
    latter = projected[..., half:]
    return jnp.concatenate(
        [former * cosine - latter * sine, latter * cosine + former * sine], axis=-1
    )


def softmax_parts(scores, valid_mask):
    masked = jnp.where(valid_mask, scores, masked_score)
    maximum = jnp.max(masked, axis=-1)
    weights = jnp.where(valid_mask, jnp.exp(masked - maximum[..., None]), 0.0)
    return (maximum, jnp.sum(weights, axis=-1), weights.astype(jnp.bfloat16))


def combine(far_peak, far_total, far_acc, near_peak, near_total, near_acc):
    highest = jnp.maximum(far_peak, near_peak)
    far_factor = jnp.exp(far_peak - highest)
    near_factor = jnp.exp(near_peak - highest)
    numer = far_acc * far_factor[..., None] + near_acc * near_factor[..., None]
    denom = far_total * far_factor + near_total * near_factor
    return numer / denom[..., None]


def spread_lanes(queries, kv_heads):
    lead = queries.shape[:-3]
    share = queries.shape[-2]
    eye = (jnp.arange(kv_heads)[:, None] == jnp.arange(kv_heads)[None, :]).astype(queries.dtype)
    eye = eye.reshape((1,) * len(lead) + (kv_heads, 1, kv_heads, 1))
    wide = queries[..., None, :] * eye
    return wide.reshape(lead + (kv_heads * share, kv_heads * HD))


def pick_lanes(wide, kv_heads):
    lead = wide.shape[:-2]
    share = wide.shape[-2] // kv_heads
    w = wide.reshape(lead + (kv_heads, share, kv_heads, HD))
    return jnp.stack([w[..., k, :, k, :] for k in range(kv_heads)], axis=-3)


def far_kernel(
    table_ref, len_ref, q_ref, k_hbm, v_hbm, acc_ref, stat_ref, kbuf, vbuf, sems, *, share, scale
):
    j = pl.program_id(0)
    steps = pl.num_programs(0)
    pblk = kbuf.shape[1]
    width = kbuf.shape[3]
    kv_heads = width // HD

    block = kbuf.shape[2]

    @pl.when(j == 0)
    def _():
        vbuf[...] = jnp.zeros_like(vbuf)

    chunk = 8

    def used_chunks(group):
        return (len_ref[group] + block * chunk - 1) // (block * chunk)

    def fetch(group, slot):
        def one(c, carry):
            for i in range(chunk):
                b = c * chunk + i
                idx = table_ref[group * pblk + b]
                pltpu.make_async_copy(k_hbm.at[idx], kbuf.at[slot, b], sems.at[0, slot, c]).start()
                pltpu.make_async_copy(v_hbm.at[idx], vbuf.at[slot, b], sems.at[1, slot, c]).start()
            return carry

        lax.fori_loop(0, used_chunks(group), one, 0)

    @pl.when(j == 0)
    def _():
        fetch(0, 0)

    slot = j % 2

    @pl.when(j + 1 < steps)
    def _():
        fetch(j + 1, 1 - slot)

    def settle(c, carry):
        part = pl.ds(pl.multiple_of(c * chunk, chunk), chunk)
        pltpu.make_async_copy(
            k_hbm.at[pl.ds(0, chunk)], kbuf.at[slot, part], sems.at[0, slot, c]
        ).wait()
        pltpu.make_async_copy(
            v_hbm.at[pl.ds(0, chunk)], vbuf.at[slot, part], sems.at[1, slot, c]
        ).wait()
        return carry

    lax.fori_loop(0, used_chunks(j), settle, 0)
    keys = kbuf[slot].reshape(-1, width)
    values = vbuf[slot].reshape(-1, width)
    queries = q_ref[0]
    scores = (
        lax.dot_general(
            queries, keys, (((1,), (1,)), ((), ())), preferred_element_type=jnp.float32
        )
        * scale
    )
    valid = lax.broadcasted_iota(jnp.int32, scores.shape, 1) < len_ref[j]
    masked = jnp.where(valid, scores, masked_score)
    peak = jnp.max(masked, axis=1, keepdims=True)
    weights = jnp.where(valid, jnp.exp(masked - peak), 0.0)
    total = jnp.sum(weights, axis=1, keepdims=True)
    wide = jnp.dot(weights.astype(jnp.bfloat16), values, preferred_element_type=jnp.float32)
    rows = wide.shape[0]
    row_head = (lax.broadcasted_iota(jnp.int32, (rows, HD), 0) // share) % kv_heads
    acc = jnp.zeros((rows, HD), jnp.float32)
    for k in range(kv_heads):
        acc = jnp.where(row_head == k, wide[:, k * HD : (k + 1) * HD], acc)
    acc_ref[0] = acc
    lane = lax.broadcasted_iota(jnp.int32, (rows, HD), 1)
    stat_ref[0] = jnp.where(lane < HD // 2, peak, total)


def far_attention(table, lengths, queries, prefix_keys, prefix_values, share, scale):
    local_groups, pblk = table.shape
    assert pblk % 8 == 0
    _, rows, width = queries.shape
    block = prefix_keys.shape[1]
    tokens = pblk * block
    kernel = lambda *refs: far_kernel(*refs, share=share, scale=scale)
    grid_spec = pltpu.PrefetchScalarGridSpec(
        num_scalar_prefetch=2,
        grid=(local_groups,),
        in_specs=[
            pl.BlockSpec((1, rows, width), lambda j, *_: (j, 0, 0)),
            pl.BlockSpec(memory_space=pl.ANY),
            pl.BlockSpec(memory_space=pl.ANY),
        ],
        out_specs=[
            pl.BlockSpec((1, rows, HD), lambda j, *_: (j, 0, 0)),
            pl.BlockSpec((1, rows, HD), lambda j, *_: (j, 0, 0)),
        ],
        scratch_shapes=[
            pltpu.VMEM((2, pblk, block, width), prefix_keys.dtype),
            pltpu.VMEM((2, pblk, block, width), prefix_values.dtype),
            pltpu.SemaphoreType.DMA((2, 2, pblk // 8)),
        ],
    )
    cost = pl.CostEstimate(
        flops=4 * local_groups * rows * tokens * width,
        transcendentals=local_groups * rows * tokens,
        bytes_accessed=2 * local_groups * tokens * width * 2 + 3 * local_groups * rows * width * 2,
    )
    return pl.pallas_call(
        kernel,
        grid_spec=grid_spec,
        out_shape=[
            jax.ShapeDtypeStruct((local_groups, rows, HD), jnp.float32),
            jax.ShapeDtypeStruct((local_groups, rows, HD), jnp.float32),
        ],
        compiler_params=pltpu.CompilerParams(dimension_semantics=("arbitrary",)),
        cost_estimate=cost,
    )(table.reshape(-1), lengths, queries, prefix_keys, prefix_values)


def body(
    hidden,
    query_weight,
    out_weight,
    prefix_keys,
    prefix_values,
    block_table,
    prompt_len,
    prompt_group,
    suffix_keys,
    suffix_values,
    suffix_len,
):
    groups = lax.axis_size("group")
    local_groups = block_table.shape[0]
    first_group = lax.axis_index("group") * local_groups
    requests = hidden.shape[0]
    width = prefix_keys.shape[2]
    kv_heads = width // HD
    q_heads = query_weight.shape[1] // HD
    share = q_heads // kv_heads
    score_scale = 1.0 / math.sqrt(HD)

    projected = jnp.dot(hidden, query_weight, preferred_element_type=jnp.float32).reshape(
        requests, q_heads, HD
    )
    position = prompt_len[prompt_group] + suffix_len - 1
    rotated = rotate(projected, position).astype(jnp.bfloat16)

    slots = jnp.arange(groups * local_groups, dtype=jnp.int32)
    picks = (slots[:, None] == prompt_group[None, :]).astype(jnp.bfloat16)
    outgoing = jnp.dot(
        picks, rotated.reshape(requests, q_heads * HD), preferred_element_type=jnp.float32
    ).astype(jnp.bfloat16)
    arrived = lax.all_to_all(
        outgoing.reshape(groups, local_groups, q_heads * HD),
        "group",
        split_axis=0,
        concat_axis=0,
        tiled=True,
    )
    far_queries = jnp.transpose(
        arrived.reshape(groups, local_groups, kv_heads, share, HD), (1, 0, 2, 3, 4)
    )
    far_queries = spread_lanes(far_queries, kv_heads).reshape(
        local_groups, groups * q_heads, width
    )
    my_lengths = lax.dynamic_slice_in_dim(prompt_len, first_group, local_groups)
    held_acc, held_stat = far_attention(
        block_table, my_lengths, far_queries, prefix_keys, prefix_values, share, score_scale
    )
    held_acc = jnp.transpose(held_acc.reshape(local_groups, groups, q_heads, HD), (1, 0, 2, 3))
    held_peak = held_stat[:, :, 0]
    held_total = held_stat[:, :, HD // 2]
    stats = jnp.concatenate(
        [
            held_peak.reshape(local_groups, groups, q_heads),
            held_total.reshape(local_groups, groups, q_heads),
            jnp.zeros((local_groups, groups, HD - 2 * q_heads), jnp.float32),
        ],
        axis=-1,
    )
    stats = jnp.transpose(stats, (1, 0, 2))[:, :, None, :]
    packed = jnp.concatenate([held_acc, stats], axis=2)
    back = lax.all_to_all(packed, "group", split_axis=0, concat_axis=0, tiled=True)
    holder = prompt_group // local_groups
    slot_index = prompt_group % local_groups
    mine = back[holder, slot_index]
    far_acc = mine[:, :q_heads, :]
    far_peak = mine[:, q_heads, :q_heads]
    far_total = mine[:, q_heads, q_heads : 2 * q_heads]

    near_queries = spread_lanes(rotated.reshape(requests, kv_heads, share, HD), kv_heads)
    own_count = suffix_keys.shape[1]
    near_valid = jnp.arange(own_count, dtype=jnp.int32)[None, None, :] < suffix_len[:, None, None]
    near_scores = (
        jnp.einsum("rqc,rtc->rqt", near_queries, suffix_keys, preferred_element_type=jnp.float32)
        * score_scale
    )
    near_peak, near_total, near_weights = softmax_parts(near_scores, near_valid)
    near_wide = jnp.einsum(
        "rqt,rtc->rqc", near_weights, suffix_values, preferred_element_type=jnp.float32
    )
    near_acc = pick_lanes(near_wide, kv_heads).reshape(requests, q_heads, HD)
    attn = combine(far_peak, far_total, far_acc, near_peak, near_total, near_acc)
    attn = attn.reshape(requests, q_heads * HD).astype(jnp.bfloat16)
    parts = lax.axis_size("tensor")
    partial_out = lax.optimization_barrier(
        jnp.dot(attn, out_weight, preferred_element_type=jnp.float32)
    )
    blocks = partial_out.reshape(requests, parts, -1)
    me = lax.axis_index("tensor")

    def block(c):
        return lax.dynamic_index_in_dim(blocks, jnp.clip(c, 0, parts - 1), axis=1, keepdims=False)

    rightward = [(i, i + 1) for i in range(parts - 1)]
    leftward = [(i + 1, i) for i in range(parts - 1)]
    from_left = jnp.zeros_like(block(me))
    from_right = jnp.zeros_like(block(me))
    for step in range(1, parts):
        send_right = block(me + parts - step) + from_left
        send_left = block(me - parts + step) + from_right
        from_left = lax.ppermute(send_right, "tensor", rightward)
        from_right = lax.ppermute(send_left, "tensor", leftward)
    return (block(me) + from_left + from_right).astype(jnp.bfloat16)


def solution(mesh):
    in_specs = (
        P("group", None),
        P(None, "tensor"),
        P("tensor", None),
        P("group", None, "tensor"),
        P("group", None, "tensor"),
        P("group", None),
        P(),
        P("group"),
        P("group", None, "tensor"),
        P("group", None, "tensor"),
        P("group"),
    )
    out_specs = P("group", "tensor")
    return jax.shard_map(body, mesh=mesh, in_specs=in_specs, out_specs=out_specs, check_vma=False)
```

```python
import math

import jax
import jax.numpy as jnp
from jax import lax
from jax.experimental import pallas as pl
from jax.experimental.pallas import tpu as pltpu
from jax.sharding import PartitionSpec as P

HD = 128


rope_base = 10000.0
masked_score = -1e30


def rotate(projected, position):
    half = projected.shape[-1] // 2
    freqs = rope_base ** (-(2.0 * jnp.arange(half, dtype=jnp.float32)) / projected.shape[-1])
    angles = position.astype(jnp.float32)[:, None, None] * freqs
    cosine = jnp.cos(angles)
    sine = jnp.sin(angles)
    former = projected[..., :half]
    latter = projected[..., half:]
    return jnp.concatenate(
        [former * cosine - latter * sine, latter * cosine + former * sine], axis=-1
    )


def softmax_parts(scores, valid_mask):
    masked = jnp.where(valid_mask, scores, masked_score)
    maximum = jnp.max(masked, axis=-1)
    weights = jnp.where(valid_mask, jnp.exp(masked - maximum[..., None]), 0.0)
    return (maximum, jnp.sum(weights, axis=-1), weights.astype(jnp.bfloat16))


def combine(far_peak, far_total, far_acc, near_peak, near_total, near_acc):
    highest = jnp.maximum(far_peak, near_peak)
    far_factor = jnp.exp(far_peak - highest)
    near_factor = jnp.exp(near_peak - highest)
    numer = far_acc * far_factor[..., None] + near_acc * near_factor[..., None]
    denom = far_total * far_factor + near_total * near_factor
    return numer / denom[..., None]


def spread_lanes(queries, kv_heads):
    lead = queries.shape[:-3]
    share = queries.shape[-2]
    eye = (jnp.arange(kv_heads)[:, None] == jnp.arange(kv_heads)[None, :]).astype(queries.dtype)
    eye = eye.reshape((1,) * len(lead) + (kv_heads, 1, kv_heads, 1))
    wide = queries[..., None, :] * eye
    return wide.reshape(lead + (kv_heads * share, kv_heads * HD))


def pick_lanes(wide, kv_heads):
    lead = wide.shape[:-2]
    share = wide.shape[-2] // kv_heads
    w = wide.reshape(lead + (kv_heads, share, kv_heads, HD))
    return jnp.stack([w[..., k, :, k, :] for k in range(kv_heads)], axis=-3)


def far_kernel(
    table_ref, len_ref, q_ref, k_hbm, v_hbm, acc_ref, stat_ref, kbuf, vbuf, sems, *, share, scale
):
    j = pl.program_id(0)
    steps = pl.num_programs(0)
    pblk = kbuf.shape[1]
    width = kbuf.shape[3]
    kv_heads = width // HD

    block = kbuf.shape[2]

    @pl.when(j == 0)
    def _():
        vbuf[...] = jnp.zeros_like(vbuf)

    chunk = 8

    def used_chunks(group):
        return (len_ref[group] + block * chunk - 1) // (block * chunk)

    def fetch(group, slot):
        def one(c, carry):
            for i in range(chunk):
                b = c * chunk + i
                idx = table_ref[group * pblk + b]
                pltpu.make_async_copy(k_hbm.at[idx], kbuf.at[slot, b], sems.at[0, slot, c]).start()
                pltpu.make_async_copy(v_hbm.at[idx], vbuf.at[slot, b], sems.at[1, slot, c]).start()
            return carry

        lax.fori_loop(0, used_chunks(group), one, 0)

    @pl.when(j == 0)
    def _():
        fetch(0, 0)

    slot = j % 2

    @pl.when(j + 1 < steps)
    def _():
        fetch(j + 1, 1 - slot)

    def settle(c, carry):
        part = pl.ds(pl.multiple_of(c * chunk, chunk), chunk)
        pltpu.make_async_copy(
            k_hbm.at[pl.ds(0, chunk)], kbuf.at[slot, part], sems.at[0, slot, c]
        ).wait()
        pltpu.make_async_copy(
            v_hbm.at[pl.ds(0, chunk)], vbuf.at[slot, part], sems.at[1, slot, c]
        ).wait()
        return carry

    lax.fori_loop(0, used_chunks(j), settle, 0)
    keys = kbuf[slot].reshape(-1, width)
    values = vbuf[slot].reshape(-1, width)
    queries = q_ref[0]
    scores = (
        lax.dot_general(
            queries, keys, (((1,), (1,)), ((), ())), preferred_element_type=jnp.float32
        )
        * scale
    )
    valid = lax.broadcasted_iota(jnp.int32, scores.shape, 1) < len_ref[j]
    masked = jnp.where(valid, scores, masked_score)
    peak = jnp.max(masked, axis=1, keepdims=True)
    weights = jnp.where(valid, jnp.exp(masked - peak), 0.0)
    total = jnp.sum(weights, axis=1, keepdims=True)
    wide = jnp.dot(weights.astype(jnp.bfloat16), values, preferred_element_type=jnp.float32)
    rows = wide.shape[0]
    row_head = (lax.broadcasted_iota(jnp.int32, (rows, HD), 0) // share) % kv_heads
    acc = jnp.zeros((rows, HD), jnp.float32)
    for k in range(kv_heads):
        acc = jnp.where(row_head == k, wide[:, k * HD : (k + 1) * HD], acc)
    acc_ref[0] = acc
    lane = lax.broadcasted_iota(jnp.int32, (rows, HD), 1)
    stat_ref[0] = jnp.where(lane < HD // 2, peak, total)


def far_attention(table, lengths, queries, prefix_keys, prefix_values, share, scale):
    local_groups, pblk = table.shape
    assert pblk % 8 == 0
    _, rows, width = queries.shape
    block = prefix_keys.shape[1]
    tokens = pblk * block
    kernel = lambda *refs: far_kernel(*refs, share=share, scale=scale)
    grid_spec = pltpu.PrefetchScalarGridSpec(
        num_scalar_prefetch=2,
        grid=(local_groups,),
        in_specs=[
            pl.BlockSpec((1, rows, width), lambda j, *_: (j, 0, 0)),
            pl.BlockSpec(memory_space=pl.ANY),
            pl.BlockSpec(memory_space=pl.ANY),
        ],
        out_specs=[
            pl.BlockSpec((1, rows, HD), lambda j, *_: (j, 0, 0)),
            pl.BlockSpec((1, rows, HD), lambda j, *_: (j, 0, 0)),
        ],
        scratch_shapes=[
            pltpu.VMEM((2, pblk, block, width), prefix_keys.dtype),
            pltpu.VMEM((2, pblk, block, width), prefix_values.dtype),
            pltpu.SemaphoreType.DMA((2, 2, pblk // 8)),
        ],
    )
    cost = pl.CostEstimate(
        flops=4 * local_groups * rows * tokens * width,
        transcendentals=local_groups * rows * tokens,
        bytes_accessed=2 * local_groups * tokens * width * 2 + 3 * local_groups * rows * width * 2,
    )
    return pl.pallas_call(
        kernel,
        grid_spec=grid_spec,
        out_shape=[
            jax.ShapeDtypeStruct((local_groups, rows, HD), jnp.float32),
            jax.ShapeDtypeStruct((local_groups, rows, HD), jnp.float32),
        ],
        compiler_params=pltpu.CompilerParams(dimension_semantics=("arbitrary",)),
        cost_estimate=cost,
    )(table.reshape(-1), lengths, queries, prefix_keys, prefix_values)


def body(
    hidden,
    query_weight,
    out_weight,
    prefix_keys,
    prefix_values,
    block_table,
    prompt_len,
    prompt_group,
    suffix_keys,
    suffix_values,
    suffix_len,
):
    groups = lax.axis_size("group")
    local_groups = block_table.shape[0]
    first_group = lax.axis_index("group") * local_groups
    requests = hidden.shape[0]
    width = prefix_keys.shape[2]
    kv_heads = width // HD
    q_heads = query_weight.shape[1] // HD
    share = q_heads // kv_heads
    score_scale = 1.0 / math.sqrt(HD)

    projected = jnp.dot(hidden, query_weight, preferred_element_type=jnp.float32).reshape(
        requests, q_heads, HD
    )
    everyone = jnp.arange(prompt_len.shape[0], dtype=jnp.int32)
    own_prompt = jnp.sum(
        jnp.where(prompt_group[:, None] == everyone[None, :], prompt_len[None, :], 0), axis=1
    )
    position = own_prompt + suffix_len - 1
    rotated = rotate(projected, position).astype(jnp.bfloat16)

    slots = jnp.arange(groups * local_groups, dtype=jnp.int32)
    picks = (slots[:, None] == prompt_group[None, :]).astype(jnp.bfloat16)
    outgoing = jnp.dot(
        picks, rotated.reshape(requests, q_heads * HD), preferred_element_type=jnp.float32
    ).astype(jnp.bfloat16)
    arrived = lax.all_to_all(
        outgoing.reshape(groups, local_groups, q_heads * HD),
        "group",
        split_axis=0,
        concat_axis=0,
        tiled=True,
    )
    far_queries = jnp.transpose(
        arrived.reshape(groups, local_groups, kv_heads, share, HD), (1, 0, 2, 3, 4)
    )
    far_queries = spread_lanes(far_queries, kv_heads).reshape(
        local_groups, groups * q_heads, width
    )
    my_lengths = lax.dynamic_slice_in_dim(prompt_len, first_group, local_groups)
    held_acc, held_stat = far_attention(
        block_table, my_lengths, far_queries, prefix_keys, prefix_values, share, score_scale
    )
    held_acc = jnp.transpose(held_acc.reshape(local_groups, groups, q_heads, HD), (1, 0, 2, 3))
    held_peak = held_stat[:, :, 0]
    held_total = held_stat[:, :, HD // 2]
    stats = jnp.concatenate(
        [
            held_peak.reshape(local_groups, groups, q_heads),
            held_total.reshape(local_groups, groups, q_heads),
            jnp.zeros((local_groups, groups, HD - 2 * q_heads), jnp.float32),
        ],
        axis=-1,
    )
    stats = jnp.transpose(stats, (1, 0, 2))[:, :, None, :]
    packed = jnp.concatenate([held_acc, stats], axis=2)
    back = lax.all_to_all(packed, "group", split_axis=0, concat_axis=0, tiled=True)
    returned = jnp.dot(
        picks.T.astype(jnp.float32),
        back.reshape(groups * local_groups, -1),
        precision=lax.Precision.HIGHEST,
        preferred_element_type=jnp.float32,
    )
    mine = returned.reshape(requests, q_heads + 1, HD)
    far_acc = mine[:, :q_heads, :]
    far_peak = mine[:, q_heads, :q_heads]
    far_total = mine[:, q_heads, q_heads : 2 * q_heads]

    near_queries = spread_lanes(rotated.reshape(requests, kv_heads, share, HD), kv_heads)
    own_count = suffix_keys.shape[1]
    near_valid = jnp.arange(own_count, dtype=jnp.int32)[None, None, :] < suffix_len[:, None, None]
    near_scores = (
        jnp.einsum("rqc,rtc->rqt", near_queries, suffix_keys, preferred_element_type=jnp.float32)
        * score_scale
    )
    near_peak, near_total, near_weights = softmax_parts(near_scores, near_valid)
    near_wide = jnp.einsum(
        "rqt,rtc->rqc", near_weights, suffix_values, preferred_element_type=jnp.float32
    )
    near_acc = pick_lanes(near_wide, kv_heads).reshape(requests, q_heads, HD)
    attn = combine(far_peak, far_total, far_acc, near_peak, near_total, near_acc)
    attn = attn.reshape(requests, q_heads * HD).astype(jnp.bfloat16)
    parts = lax.axis_size("tensor")
    partial_out = lax.optimization_barrier(
        jnp.dot(attn, out_weight, preferred_element_type=jnp.float32)
    )
    pieces = lax.all_to_all(
        jnp.transpose(partial_out.reshape(requests, parts, -1), (1, 0, 2)),
        "tensor",
        split_axis=0,
        concat_axis=0,
        tiled=True,
    )
    return jnp.sum(pieces, axis=0).astype(jnp.bfloat16)


def solution(mesh):
    in_specs = (
        P("group", None),
        P(None, "tensor"),
        P("tensor", None),
        P("group", None, "tensor"),
        P("group", None, "tensor"),
        P("group", None),
        P(),
        P("group"),
        P("group", None, "tensor"),
        P("group", None, "tensor"),
        P("group"),
    )
    out_specs = P("group", "tensor")
    return jax.shard_map(body, mesh=mesh, in_specs=in_specs, out_specs=out_specs, check_vma=False)
```

```python
import math

import jax
import jax.numpy as jnp
from jax import lax
from jax.experimental import pallas as pl
from jax.experimental.pallas import tpu as pltpu
from jax.sharding import PartitionSpec as P

HD = 128


rope_base = 10000.0
masked_score = -1e30


def rotate(projected, position):
    half = projected.shape[-1] // 2
    freqs = rope_base ** (-(2.0 * jnp.arange(half, dtype=jnp.float32)) / projected.shape[-1])
    angles = position.astype(jnp.float32)[:, None, None] * freqs
    cosine = jnp.cos(angles)
    sine = jnp.sin(angles)
    former = projected[..., :half]
    latter = projected[..., half:]
    return jnp.concatenate(
        [former * cosine - latter * sine, latter * cosine + former * sine], axis=-1
    )


def softmax_parts(scores, valid_mask):
    masked = jnp.where(valid_mask, scores, masked_score)
    maximum = jnp.max(masked, axis=-1)
    weights = jnp.where(valid_mask, jnp.exp(masked - maximum[..., None]), 0.0)
    return (maximum, jnp.sum(weights, axis=-1), weights.astype(jnp.bfloat16))


def combine(far_peak, far_total, far_acc, near_peak, near_total, near_acc):
    highest = jnp.maximum(far_peak, near_peak)
    far_factor = jnp.exp(far_peak - highest)
    near_factor = jnp.exp(near_peak - highest)
    numer = far_acc * far_factor[..., None] + near_acc * near_factor[..., None]
    denom = far_total * far_factor + near_total * near_factor
    return numer / denom[..., None]


def spread_lanes(queries, kv_heads):
    lead = queries.shape[:-3]
    share = queries.shape[-2]
    eye = (jnp.arange(kv_heads)[:, None] == jnp.arange(kv_heads)[None, :]).astype(queries.dtype)
    eye = eye.reshape((1,) * len(lead) + (kv_heads, 1, kv_heads, 1))
    wide = queries[..., None, :] * eye
    return wide.reshape(lead + (kv_heads * share, kv_heads * HD))


def pick_lanes(wide, kv_heads):
    lead = wide.shape[:-2]
    share = wide.shape[-2] // kv_heads
    w = wide.reshape(lead + (kv_heads, share, kv_heads, HD))
    return jnp.stack([w[..., k, :, k, :] for k in range(kv_heads)], axis=-3)


def far_kernel(
    table_ref, len_ref, q_ref, k_hbm, v_hbm, acc_ref, stat_ref, kbuf, vbuf, sems, *, share, scale
):
    j = pl.program_id(0)
    steps = pl.num_programs(0)
    pblk = kbuf.shape[1]
    width = kbuf.shape[3]
    kv_heads = width // HD

    block = kbuf.shape[2]

    @pl.when(j == 0)
    def _():
        vbuf[...] = jnp.zeros_like(vbuf)

    chunk = 8

    def used_chunks(group):
        return (len_ref[group] + block * chunk - 1) // (block * chunk)

    def fetch(group, slot):
        def one(c, carry):
            for i in range(chunk):
                b = c * chunk + i
                idx = table_ref[group * pblk + b]
                pltpu.make_async_copy(k_hbm.at[idx], kbuf.at[slot, b], sems.at[0, slot, c]).start()
                pltpu.make_async_copy(v_hbm.at[idx], vbuf.at[slot, b], sems.at[1, slot, c]).start()
            return carry

        lax.fori_loop(0, used_chunks(group), one, 0)

    @pl.when(j == 0)
    def _():
        fetch(0, 0)

    slot = j % 2

    @pl.when(j + 1 < steps)
    def _():
        fetch(j + 1, 1 - slot)

    def settle(c, carry):
        part = pl.ds(pl.multiple_of(c * chunk, chunk), chunk)
        pltpu.make_async_copy(
            k_hbm.at[pl.ds(0, chunk)], kbuf.at[slot, part], sems.at[0, slot, c]
        ).wait()
        pltpu.make_async_copy(
            v_hbm.at[pl.ds(0, chunk)], vbuf.at[slot, part], sems.at[1, slot, c]
        ).wait()
        return carry

    lax.fori_loop(0, used_chunks(j), settle, 0)
    keys = kbuf[slot].reshape(-1, width)
    values = vbuf[slot].reshape(-1, width)
    queries = q_ref[0]
    scores = (
        lax.dot_general(
            queries, keys, (((1,), (1,)), ((), ())), preferred_element_type=jnp.float32
        )
        * scale
    )
    valid = lax.broadcasted_iota(jnp.int32, scores.shape, 1) < len_ref[j]
    masked = jnp.where(valid, scores, masked_score)
    peak = jnp.max(masked, axis=1, keepdims=True)
    weights = jnp.where(valid, jnp.exp(masked - peak), 0.0)
    total = jnp.sum(weights, axis=1, keepdims=True)
    wide = jnp.dot(weights.astype(jnp.bfloat16), values, preferred_element_type=jnp.float32)
    rows = wide.shape[0]
    row_head = (lax.broadcasted_iota(jnp.int32, (rows, HD), 0) // share) % kv_heads
    acc = jnp.zeros((rows, HD), jnp.float32)
    for k in range(kv_heads):
        acc = jnp.where(row_head == k, wide[:, k * HD : (k + 1) * HD], acc)
    acc_ref[0] = acc
    lane = lax.broadcasted_iota(jnp.int32, (rows, HD), 1)
    stat_ref[0] = jnp.where(lane < HD // 2, peak, total)


def far_attention(table, lengths, queries, prefix_keys, prefix_values, share, scale):
    local_groups, pblk = table.shape
    assert pblk % 8 == 0
    _, rows, width = queries.shape
    block = prefix_keys.shape[1]
    tokens = pblk * block
    kernel = lambda *refs: far_kernel(*refs, share=share, scale=scale)
    grid_spec = pltpu.PrefetchScalarGridSpec(
        num_scalar_prefetch=2,
        grid=(local_groups,),
        in_specs=[
            pl.BlockSpec((1, rows, width), lambda j, *_: (j, 0, 0)),
            pl.BlockSpec(memory_space=pl.ANY),
            pl.BlockSpec(memory_space=pl.ANY),
        ],
        out_specs=[
            pl.BlockSpec((1, rows, HD), lambda j, *_: (j, 0, 0)),
            pl.BlockSpec((1, rows, HD), lambda j, *_: (j, 0, 0)),
        ],
        scratch_shapes=[
            pltpu.VMEM((2, pblk, block, width), prefix_keys.dtype),
            pltpu.VMEM((2, pblk, block, width), prefix_values.dtype),
            pltpu.SemaphoreType.DMA((2, 2, pblk // 8)),
        ],
    )
    cost = pl.CostEstimate(
        flops=4 * local_groups * rows * tokens * width,
        transcendentals=local_groups * rows * tokens,
        bytes_accessed=2 * local_groups * tokens * width * 2 + 3 * local_groups * rows * width * 2,
    )
    return pl.pallas_call(
        kernel,
        grid_spec=grid_spec,
        out_shape=[
            jax.ShapeDtypeStruct((local_groups, rows, HD), jnp.float32),
            jax.ShapeDtypeStruct((local_groups, rows, HD), jnp.float32),
        ],
        compiler_params=pltpu.CompilerParams(dimension_semantics=("arbitrary",)),
        cost_estimate=cost,
    )(table.reshape(-1), lengths, queries, prefix_keys, prefix_values)


def body(
    hidden,
    query_weight,
    out_weight,
    prefix_keys,
    prefix_values,
    block_table,
    prompt_len,
    prompt_group,
    suffix_keys,
    suffix_values,
    suffix_len,
):
    groups = lax.axis_size("group")
    local_groups = block_table.shape[0]
    first_group = lax.axis_index("group") * local_groups
    requests = hidden.shape[0]
    width = prefix_keys.shape[2]
    kv_heads = width // HD
    q_heads = query_weight.shape[1] // HD
    share = q_heads // kv_heads
    score_scale = 1.0 / math.sqrt(HD)

    projected = jnp.dot(hidden, query_weight, preferred_element_type=jnp.float32).reshape(
        requests, q_heads, HD
    )
    everyone = jnp.arange(prompt_len.shape[0], dtype=jnp.int32)
    own_prompt = jnp.sum(
        jnp.where(prompt_group[:, None] == everyone[None, :], prompt_len[None, :], 0), axis=1
    )
    position = own_prompt + suffix_len - 1
    rotated = rotate(projected, position).astype(jnp.bfloat16)

    slots = jnp.arange(groups * local_groups, dtype=jnp.int32)
    picks = (slots[:, None] == prompt_group[None, :]).astype(jnp.bfloat16)
    outgoing = jnp.dot(
        picks, rotated.reshape(requests, q_heads * HD), preferred_element_type=jnp.float32
    ).astype(jnp.bfloat16)
    arrived = lax.all_to_all(
        outgoing.reshape(groups, local_groups, q_heads * HD),
        "group",
        split_axis=0,
        concat_axis=0,
        tiled=True,
    )
    far_queries = jnp.transpose(
        arrived.reshape(groups, local_groups, kv_heads, share, HD), (1, 0, 2, 3, 4)
    )
    far_queries = spread_lanes(far_queries, kv_heads).reshape(
        local_groups, groups * q_heads, width
    )
    my_lengths = lax.dynamic_slice_in_dim(prompt_len, first_group, local_groups)
    held_acc, held_stat = far_attention(
        block_table, my_lengths, far_queries, prefix_keys, prefix_values, share, score_scale
    )
    held_acc = jnp.transpose(held_acc.reshape(local_groups, groups, q_heads, HD), (1, 0, 2, 3))
    held_peak = held_stat[:, :, 0]
    held_total = held_stat[:, :, HD // 2]
    stats = jnp.concatenate(
        [
            held_peak.reshape(local_groups, groups, q_heads),
            held_total.reshape(local_groups, groups, q_heads),
            jnp.zeros((local_groups, groups, HD - 2 * q_heads), jnp.float32),
        ],
        axis=-1,
    )
    stats = jnp.transpose(stats, (1, 0, 2))[:, :, None, :]
    packed = jnp.concatenate([held_acc, stats], axis=2)

    near_queries = spread_lanes(rotated.reshape(requests, kv_heads, share, HD), kv_heads)
    own_count = suffix_keys.shape[1]
    near_valid = jnp.arange(own_count, dtype=jnp.int32)[None, None, :] < suffix_len[:, None, None]
    near_scores = (
        jnp.einsum("rqc,rtc->rqt", near_queries, suffix_keys, preferred_element_type=jnp.float32)
        * score_scale
    )
    near_peak, near_total, near_weights = softmax_parts(near_scores, near_valid)
    packed, near_weights = lax.optimization_barrier((packed, near_weights))
    back = lax.all_to_all(packed, "group", split_axis=0, concat_axis=0, tiled=True)
    returned = jnp.dot(
        picks.T.astype(jnp.float32),
        back.reshape(groups * local_groups, -1),
        precision=lax.Precision.HIGHEST,
        preferred_element_type=jnp.float32,
    )
    mine = returned.reshape(requests, q_heads + 1, HD)
    far_acc = mine[:, :q_heads, :]
    far_peak = mine[:, q_heads, :q_heads]
    far_total = mine[:, q_heads, q_heads : 2 * q_heads]
    near_wide = jnp.einsum(
        "rqt,rtc->rqc", near_weights, suffix_values, preferred_element_type=jnp.float32
    )
    near_acc = pick_lanes(near_wide, kv_heads).reshape(requests, q_heads, HD)
    attn = combine(far_peak, far_total, far_acc, near_peak, near_total, near_acc)
    attn = attn.reshape(requests, q_heads * HD).astype(jnp.bfloat16)
    parts = lax.axis_size("tensor")
    partial_out = lax.optimization_barrier(
        jnp.dot(attn, out_weight, preferred_element_type=jnp.float32)
    )
    pieces = lax.all_to_all(
        jnp.transpose(partial_out.reshape(requests, parts, -1), (1, 0, 2)),
        "tensor",
        split_axis=0,
        concat_axis=0,
        tiled=True,
    )
    return jnp.sum(pieces, axis=0).astype(jnp.bfloat16)


def solution(mesh):
    in_specs = (
        P("group", None),
        P(None, "tensor"),
        P("tensor", None),
        P("group", None, "tensor"),
        P("group", None, "tensor"),
        P("group", None),
        P(),
        P("group"),
        P("group", None, "tensor"),
        P("group", None, "tensor"),
        P("group"),
    )
    out_specs = P("group", "tensor")
    return jax.shard_map(body, mesh=mesh, in_specs=in_specs, out_specs=out_specs, check_vma=False)
```

```python
import math

import jax
import jax.numpy as jnp
from jax import lax
from jax.experimental import pallas as pl
from jax.experimental.pallas import tpu as pltpu
from jax.sharding import PartitionSpec as P

HD = 128


rope_base = 10000.0
masked_score = -1e30


def rotate(projected, position):
    half = projected.shape[-1] // 2
    freqs = rope_base ** (-(2.0 * jnp.arange(half, dtype=jnp.float32)) / projected.shape[-1])
    angles = position.astype(jnp.float32)[:, None, None] * freqs
    cosine = jnp.cos(angles)
    sine = jnp.sin(angles)
    former = projected[..., :half]
    latter = projected[..., half:]
    return jnp.concatenate(
        [former * cosine - latter * sine, latter * cosine + former * sine], axis=-1
    )


def softmax_parts(scores, valid_mask):
    masked = jnp.where(valid_mask, scores, masked_score)
    maximum = jnp.max(masked, axis=-1)
    weights = jnp.where(valid_mask, jnp.exp(masked - maximum[..., None]), 0.0)
    return (maximum, jnp.sum(weights, axis=-1), weights.astype(jnp.bfloat16))


def combine(far_peak, far_total, far_acc, near_peak, near_total, near_acc):
    highest = jnp.maximum(far_peak, near_peak)
    far_factor = jnp.exp(far_peak - highest)
    near_factor = jnp.exp(near_peak - highest)
    numer = far_acc * far_factor[..., None] + near_acc * near_factor[..., None]
    denom = far_total * far_factor + near_total * near_factor
    return numer / denom[..., None]


def spread_lanes(queries, kv_heads):
    lead = queries.shape[:-3]
    share = queries.shape[-2]
    eye = (jnp.arange(kv_heads)[:, None] == jnp.arange(kv_heads)[None, :]).astype(queries.dtype)
    eye = eye.reshape((1,) * len(lead) + (kv_heads, 1, kv_heads, 1))
    wide = queries[..., None, :] * eye
    return wide.reshape(lead + (kv_heads * share, kv_heads * HD))


def pick_lanes(wide, kv_heads):
    lead = wide.shape[:-2]
    share = wide.shape[-2] // kv_heads
    w = wide.reshape(lead + (kv_heads, share, kv_heads, HD))
    return jnp.stack([w[..., k, :, k, :] for k in range(kv_heads)], axis=-3)


def far_kernel(
    table_ref, len_ref, q_ref, k_hbm, v_hbm, out_ref, kbuf, vbuf, sems, *, share, scale
):
    j = pl.program_id(0)
    steps = pl.num_programs(0)
    pblk = kbuf.shape[1]
    width = kbuf.shape[3]
    kv_heads = width // HD

    block = kbuf.shape[2]

    @pl.when(j == 0)
    def _():
        vbuf[...] = jnp.zeros_like(vbuf)

    chunk = 8

    def used_chunks(group):
        return (len_ref[group] + block * chunk - 1) // (block * chunk)

    def fetch(group, slot):
        def one(c, carry):
            for i in range(chunk):
                b = c * chunk + i
                idx = table_ref[group * pblk + b]
                pltpu.make_async_copy(k_hbm.at[idx], kbuf.at[slot, b], sems.at[0, slot, c]).start()
                pltpu.make_async_copy(v_hbm.at[idx], vbuf.at[slot, b], sems.at[1, slot, c]).start()
            return carry

        lax.fori_loop(0, used_chunks(group), one, 0)

    @pl.when(j == 0)
    def _():
        fetch(0, 0)

    slot = j % 2

    @pl.when(j + 1 < steps)
    def _():
        fetch(j + 1, 1 - slot)

    def settle(c, carry):
        part = pl.ds(pl.multiple_of(c * chunk, chunk), chunk)
        pltpu.make_async_copy(
            k_hbm.at[pl.ds(0, chunk)], kbuf.at[slot, part], sems.at[0, slot, c]
        ).wait()
        pltpu.make_async_copy(
            v_hbm.at[pl.ds(0, chunk)], vbuf.at[slot, part], sems.at[1, slot, c]
        ).wait()
        return carry

    lax.fori_loop(0, used_chunks(j), settle, 0)
    keys = kbuf[slot].reshape(-1, width)
    values = vbuf[slot].reshape(-1, width)
    queries = q_ref[0]
    scores = (
        lax.dot_general(
            queries, keys, (((1,), (1,)), ((), ())), preferred_element_type=jnp.float32
        )
        * scale
    )
    valid = lax.broadcasted_iota(jnp.int32, scores.shape, 1) < len_ref[j]
    masked = jnp.where(valid, scores, masked_score)
    peak = jnp.max(masked, axis=1, keepdims=True)
    weights = jnp.where(valid, jnp.exp(masked - peak), 0.0)
    total = jnp.sum(weights, axis=1, keepdims=True)
    wide = jnp.dot(weights.astype(jnp.bfloat16), values, preferred_element_type=jnp.float32)
    rows = wide.shape[0]
    row_head = (lax.broadcasted_iota(jnp.int32, (rows, HD), 0) // share) % kv_heads
    acc = jnp.zeros((rows, HD), jnp.float32)
    for k in range(kv_heads):
        acc = jnp.where(row_head == k, wide[:, k * HD : (k + 1) * HD], acc)
    sources = out_ref.shape[0]
    q_heads = out_ref.shape[1] - 1
    out_ref[:, :q_heads, pl.ds(j, 1), :] = acc.reshape(sources, q_heads, 1, HD)
    lane = lax.broadcasted_iota(jnp.int32, (sources, q_heads, HD), 2)
    head = lax.broadcasted_iota(jnp.int32, (sources, q_heads, HD), 1)
    peak3 = jnp.broadcast_to(peak, (rows, HD)).reshape(sources, q_heads, HD)
    total3 = jnp.broadcast_to(total, (rows, HD)).reshape(sources, q_heads, HD)
    stat = jnp.where(lane == head, peak3, 0.0) + jnp.where(lane == head + q_heads, total3, 0.0)
    out_ref[:, q_heads:, pl.ds(j, 1), :] = jnp.sum(stat, axis=1).reshape(sources, 1, 1, HD)


def far_attention(table, lengths, queries, prefix_keys, prefix_values, share, scale, sources):
    local_groups, pblk = table.shape
    assert pblk % 8 == 0
    _, rows, width = queries.shape
    q_heads = rows // sources
    assert 2 * q_heads <= HD
    block = prefix_keys.shape[1]
    tokens = pblk * block
    kernel = lambda *refs: far_kernel(*refs, share=share, scale=scale)
    grid_spec = pltpu.PrefetchScalarGridSpec(
        num_scalar_prefetch=2,
        grid=(local_groups,),
        in_specs=[
            pl.BlockSpec((1, rows, width), lambda j, *_: (j, 0, 0)),
            pl.BlockSpec(memory_space=pl.ANY),
            pl.BlockSpec(memory_space=pl.ANY),
        ],
        out_specs=pl.BlockSpec(
            (sources, q_heads + 1, local_groups, HD), lambda j, *_: (0, 0, 0, 0)
        ),
        scratch_shapes=[
            pltpu.VMEM((2, pblk, block, width), prefix_keys.dtype),
            pltpu.VMEM((2, pblk, block, width), prefix_values.dtype),
            pltpu.SemaphoreType.DMA((2, 2, pblk // 8)),
        ],
    )
    cost = pl.CostEstimate(
        flops=4 * local_groups * rows * tokens * width,
        transcendentals=local_groups * rows * tokens,
        bytes_accessed=2 * local_groups * tokens * width * 2 + 3 * local_groups * rows * width * 2,
    )
    return pl.pallas_call(
        kernel,
        grid_spec=grid_spec,
        out_shape=jax.ShapeDtypeStruct((sources, q_heads + 1, local_groups, HD), jnp.float32),
        compiler_params=pltpu.CompilerParams(dimension_semantics=("arbitrary",)),
        cost_estimate=cost,
    )(table.reshape(-1), lengths, queries, prefix_keys, prefix_values)


def body(
    hidden,
    query_weight,
    out_weight,
    prefix_keys,
    prefix_values,
    block_table,
    prompt_len,
    prompt_group,
    suffix_keys,
    suffix_values,
    suffix_len,
):
    groups = lax.axis_size("group")
    local_groups = block_table.shape[0]
    first_group = lax.axis_index("group") * local_groups
    requests = hidden.shape[0]
    width = prefix_keys.shape[2]
    kv_heads = width // HD
    q_heads = query_weight.shape[1] // HD
    share = q_heads // kv_heads
    score_scale = 1.0 / math.sqrt(HD)

    projected = jnp.dot(hidden, query_weight, preferred_element_type=jnp.float32).reshape(
        requests, q_heads, HD
    )
    everyone = jnp.arange(prompt_len.shape[0], dtype=jnp.int32)
    own_prompt = jnp.sum(
        jnp.where(prompt_group[:, None] == everyone[None, :], prompt_len[None, :], 0), axis=1
    )
    position = own_prompt + suffix_len - 1
    rotated = rotate(projected, position).astype(jnp.bfloat16)

    slots = jnp.arange(groups * local_groups, dtype=jnp.int32)
    picks = (slots[:, None] == prompt_group[None, :]).astype(jnp.bfloat16)
    outgoing = jnp.dot(
        picks, rotated.reshape(requests, q_heads * HD), preferred_element_type=jnp.float32
    ).astype(jnp.bfloat16)
    arrived = lax.all_to_all(
        outgoing.reshape(groups, local_groups, q_heads * HD),
        "group",
        split_axis=0,
        concat_axis=0,
        tiled=True,
    )
    far_queries = jnp.transpose(
        arrived.reshape(groups, local_groups, kv_heads, share, HD), (1, 0, 2, 3, 4)
    )
    far_queries = spread_lanes(far_queries, kv_heads).reshape(
        local_groups, groups * q_heads, width
    )
    my_lengths = lax.dynamic_slice_in_dim(prompt_len, first_group, local_groups)
    packed = far_attention(
        block_table, my_lengths, far_queries, prefix_keys, prefix_values, share, score_scale,
        groups,
    )
    packed = jnp.transpose(packed, (0, 2, 1, 3))

    near_queries = spread_lanes(rotated.reshape(requests, kv_heads, share, HD), kv_heads)
    own_count = suffix_keys.shape[1]
    near_valid = jnp.arange(own_count, dtype=jnp.int32)[None, None, :] < suffix_len[:, None, None]
    near_scores = (
        jnp.einsum("rqc,rtc->rqt", near_queries, suffix_keys, preferred_element_type=jnp.float32)
        * score_scale
    )
    near_peak, near_total, near_weights = softmax_parts(near_scores, near_valid)
    packed, near_weights = lax.optimization_barrier((packed, near_weights))
    back = lax.all_to_all(packed, "group", split_axis=0, concat_axis=0, tiled=True)
    returned = jnp.dot(
        picks.T.astype(jnp.float32),
        back.reshape(groups * local_groups, -1),
        precision=lax.Precision.HIGHEST,
        preferred_element_type=jnp.float32,
    )
    mine = returned.reshape(requests, q_heads + 1, HD)
    far_acc = mine[:, :q_heads, :]
    far_peak = mine[:, q_heads, :q_heads]
    far_total = mine[:, q_heads, q_heads : 2 * q_heads]
    near_wide = jnp.einsum(
        "rqt,rtc->rqc", near_weights, suffix_values, preferred_element_type=jnp.float32
    )
    near_acc = pick_lanes(near_wide, kv_heads).reshape(requests, q_heads, HD)
    attn = combine(far_peak, far_total, far_acc, near_peak, near_total, near_acc)
    attn = attn.reshape(requests, q_heads * HD).astype(jnp.bfloat16)
    parts = lax.axis_size("tensor")
    partial_out = lax.optimization_barrier(
        jnp.dot(attn, out_weight, preferred_element_type=jnp.float32)
    )
    pieces = lax.all_to_all(
        jnp.transpose(partial_out.reshape(requests, parts, -1), (1, 0, 2)),
        "tensor",
        split_axis=0,
        concat_axis=0,
        tiled=True,
    )
    return jnp.sum(pieces, axis=0).astype(jnp.bfloat16)


def solution(mesh):
    in_specs = (
        P("group", None),
        P(None, "tensor"),
        P("tensor", None),
        P("group", None, "tensor"),
        P("group", None, "tensor"),
        P("group", None),
        P(),
        P("group"),
        P("group", None, "tensor"),
        P("group", None, "tensor"),
        P("group"),
    )
    out_specs = P("group", "tensor")
    return jax.shard_map(body, mesh=mesh, in_specs=in_specs, out_specs=out_specs, check_vma=False)
```

```python
import math

import jax
import jax.numpy as jnp
from jax import lax
from jax.experimental import pallas as pl
from jax.experimental.pallas import tpu as pltpu
from jax.sharding import PartitionSpec as P

HD = 128


rope_base = 10000.0
masked_score = -1e30


def rotate(projected, position):
    half = projected.shape[-1] // 2
    freqs = rope_base ** (-(2.0 * jnp.arange(half, dtype=jnp.float32)) / projected.shape[-1])
    angles = position.astype(jnp.float32)[:, None, None] * freqs
    cosine = jnp.cos(angles)
    sine = jnp.sin(angles)
    former = projected[..., :half]
    latter = projected[..., half:]
    return jnp.concatenate(
        [former * cosine - latter * sine, latter * cosine + former * sine], axis=-1
    )


def softmax_parts(scores, valid_mask):
    masked = jnp.where(valid_mask, scores, masked_score)
    maximum = jnp.max(masked, axis=-1)
    weights = jnp.where(valid_mask, jnp.exp(masked - maximum[..., None]), 0.0)
    return (maximum, jnp.sum(weights, axis=-1), weights.astype(jnp.bfloat16))


def combine(far_peak, far_total, far_acc, near_peak, near_total, near_acc):
    highest = jnp.maximum(far_peak, near_peak)
    far_factor = jnp.exp(far_peak - highest)
    near_factor = jnp.exp(near_peak - highest)
    numer = far_acc * far_factor[..., None] + near_acc * near_factor[..., None]
    denom = far_total * far_factor + near_total * near_factor
    return numer / denom[..., None]


def spread_lanes(queries, kv_heads):
    lead = queries.shape[:-3]
    share = queries.shape[-2]
    eye = (jnp.arange(kv_heads)[:, None] == jnp.arange(kv_heads)[None, :]).astype(queries.dtype)
    eye = eye.reshape((1,) * len(lead) + (kv_heads, 1, kv_heads, 1))
    wide = queries[..., None, :] * eye
    return wide.reshape(lead + (kv_heads * share, kv_heads * HD))


def pick_lanes(wide, kv_heads):
    lead = wide.shape[:-2]
    share = wide.shape[-2] // kv_heads
    w = wide.reshape(lead + (kv_heads, share, kv_heads, HD))
    return jnp.stack([w[..., k, :, k, :] for k in range(kv_heads)], axis=-3)


def far_kernel(
    table_ref, len_ref, q_ref, k_hbm, v_hbm, out_ref, kbuf, vbuf, sems, *, share, scale
):
    j = pl.program_id(0)
    steps = pl.num_programs(0)
    pblk = kbuf.shape[1]
    width = kbuf.shape[3]
    kv_heads = width // HD

    block = kbuf.shape[2]

    @pl.when(j == 0)
    def _():
        vbuf[...] = jnp.zeros_like(vbuf)

    chunk = 8

    def used_chunks(group):
        return (len_ref[group] + block * chunk - 1) // (block * chunk)

    def fetch(group, slot):
        def one(c, carry):
            for i in range(chunk):
                b = c * chunk + i
                idx = table_ref[group * pblk + b]
                pltpu.make_async_copy(k_hbm.at[idx], kbuf.at[slot, b], sems.at[0, slot, c]).start()
                pltpu.make_async_copy(v_hbm.at[idx], vbuf.at[slot, b], sems.at[1, slot, c]).start()
            return carry

        lax.fori_loop(0, used_chunks(group), one, 0)

    @pl.when(j == 0)
    def _():
        fetch(0, 0)

    slot = j % 2

    @pl.when(j + 1 < steps)
    def _():
        fetch(j + 1, 1 - slot)

    def settle(c, carry):
        part = pl.ds(pl.multiple_of(c * chunk, chunk), chunk)
        pltpu.make_async_copy(
            k_hbm.at[pl.ds(0, chunk)], kbuf.at[slot, part], sems.at[0, slot, c]
        ).wait()
        pltpu.make_async_copy(
            v_hbm.at[pl.ds(0, chunk)], vbuf.at[slot, part], sems.at[1, slot, c]
        ).wait()
        return carry

    lax.fori_loop(0, used_chunks(j), settle, 0)
    keys = kbuf[slot].reshape(-1, width)
    values = vbuf[slot].reshape(-1, width)
    queries = q_ref[0]
    scores = (
        lax.dot_general(
            keys, queries, (((1,), (1,)), ((), ())), preferred_element_type=jnp.float32
        )
        * scale
    )
    valid = lax.broadcasted_iota(jnp.int32, scores.shape, 0) < len_ref[j]
    masked = jnp.where(valid, scores, masked_score)
    peak_row = jnp.max(masked, axis=0, keepdims=True)
    weights = jnp.where(valid, jnp.exp(masked - peak_row), 0.0)
    total_row = jnp.sum(weights, axis=0, keepdims=True)
    wide = lax.dot_general(
        weights.astype(jnp.bfloat16), values, (((0,), (0,)), ((), ())),
        preferred_element_type=jnp.float32,
    )
    count = scores.shape[1]
    eye = (
        lax.broadcasted_iota(jnp.int32, (count, count), 0)
        == lax.broadcasted_iota(jnp.int32, (count, count), 1)
    )
    peak = jnp.sum(jnp.where(eye, peak_row, 0.0), axis=1, keepdims=True)
    total = jnp.sum(jnp.where(eye, total_row, 0.0), axis=1, keepdims=True)
    rows = wide.shape[0]
    row_head = (lax.broadcasted_iota(jnp.int32, (rows, HD), 0) // share) % kv_heads
    acc = jnp.zeros((rows, HD), jnp.float32)
    for k in range(kv_heads):
        acc = jnp.where(row_head == k, wide[:, k * HD : (k + 1) * HD], acc)
    sources = out_ref.shape[0]
    q_heads = out_ref.shape[1] - 1
    out_ref[:, :q_heads, pl.ds(j, 1), :] = acc.reshape(sources, q_heads, 1, HD)
    lane = lax.broadcasted_iota(jnp.int32, (sources, q_heads, HD), 2)
    head = lax.broadcasted_iota(jnp.int32, (sources, q_heads, HD), 1)
    peak3 = jnp.broadcast_to(peak, (rows, HD)).reshape(sources, q_heads, HD)
    total3 = jnp.broadcast_to(total, (rows, HD)).reshape(sources, q_heads, HD)
    stat = jnp.where(lane == head, peak3, 0.0) + jnp.where(lane == head + q_heads, total3, 0.0)
    out_ref[:, q_heads:, pl.ds(j, 1), :] = jnp.sum(stat, axis=1).reshape(sources, 1, 1, HD)


def far_attention(table, lengths, queries, prefix_keys, prefix_values, share, scale, sources):
    local_groups, pblk = table.shape
    assert pblk % 8 == 0
    _, rows, width = queries.shape
    q_heads = rows // sources
    assert 2 * q_heads <= HD
    block = prefix_keys.shape[1]
    tokens = pblk * block
    kernel = lambda *refs: far_kernel(*refs, share=share, scale=scale)
    grid_spec = pltpu.PrefetchScalarGridSpec(
        num_scalar_prefetch=2,
        grid=(local_groups,),
        in_specs=[
            pl.BlockSpec((1, rows, width), lambda j, *_: (j, 0, 0)),
            pl.BlockSpec(memory_space=pl.ANY),
            pl.BlockSpec(memory_space=pl.ANY),
        ],
        out_specs=pl.BlockSpec(
            (sources, q_heads + 1, local_groups, HD), lambda j, *_: (0, 0, 0, 0)
        ),
        scratch_shapes=[
            pltpu.VMEM((2, pblk, block, width), prefix_keys.dtype),
            pltpu.VMEM((2, pblk, block, width), prefix_values.dtype),
            pltpu.SemaphoreType.DMA((2, 2, pblk // 8)),
        ],
    )
    cost = pl.CostEstimate(
        flops=4 * local_groups * rows * tokens * width,
        transcendentals=local_groups * rows * tokens,
        bytes_accessed=2 * local_groups * tokens * width * 2 + 3 * local_groups * rows * width * 2,
    )
    return pl.pallas_call(
        kernel,
        grid_spec=grid_spec,
        out_shape=jax.ShapeDtypeStruct((sources, q_heads + 1, local_groups, HD), jnp.float32),
        compiler_params=pltpu.CompilerParams(dimension_semantics=("arbitrary",)),
        cost_estimate=cost,
    )(table.reshape(-1), lengths, queries, prefix_keys, prefix_values)


def body(
    hidden,
    query_weight,
    out_weight,
    prefix_keys,
    prefix_values,
    block_table,
    prompt_len,
    prompt_group,
    suffix_keys,
    suffix_values,
    suffix_len,
):
    groups = lax.axis_size("group")
    local_groups = block_table.shape[0]
    first_group = lax.axis_index("group") * local_groups
    requests = hidden.shape[0]
    width = prefix_keys.shape[2]
    kv_heads = width // HD
    q_heads = query_weight.shape[1] // HD
    share = q_heads // kv_heads
    score_scale = 1.0 / math.sqrt(HD)

    projected = jnp.dot(hidden, query_weight, preferred_element_type=jnp.float32).reshape(
        requests, q_heads, HD
    )
    everyone = jnp.arange(prompt_len.shape[0], dtype=jnp.int32)
    own_prompt = jnp.sum(
        jnp.where(prompt_group[:, None] == everyone[None, :], prompt_len[None, :], 0), axis=1
    )
    position = own_prompt + suffix_len - 1
    rotated = rotate(projected, position).astype(jnp.bfloat16)

    slots = jnp.arange(groups * local_groups, dtype=jnp.int32)
    picks = (slots[:, None] == prompt_group[None, :]).astype(jnp.bfloat16)
    outgoing = jnp.dot(
        picks, rotated.reshape(requests, q_heads * HD), preferred_element_type=jnp.float32
    ).astype(jnp.bfloat16)
    arrived = lax.all_to_all(
        outgoing.reshape(groups, local_groups, q_heads * HD),
        "group",
        split_axis=0,
        concat_axis=0,
        tiled=True,
    )
    far_queries = jnp.transpose(
        arrived.reshape(groups, local_groups, kv_heads, share, HD), (1, 0, 2, 3, 4)
    )
    far_queries = spread_lanes(far_queries, kv_heads).reshape(
        local_groups, groups * q_heads, width
    )
    my_lengths = lax.dynamic_slice_in_dim(prompt_len, first_group, local_groups)
    packed = far_attention(
        block_table, my_lengths, far_queries, prefix_keys, prefix_values, share, score_scale,
        groups,
    )
    packed = jnp.transpose(packed, (0, 2, 1, 3))

    near_queries = spread_lanes(rotated.reshape(requests, kv_heads, share, HD), kv_heads)
    own_count = suffix_keys.shape[1]
    near_valid = jnp.arange(own_count, dtype=jnp.int32)[None, None, :] < suffix_len[:, None, None]
    near_scores = (
        jnp.einsum("rqc,rtc->rqt", near_queries, suffix_keys, preferred_element_type=jnp.float32)
        * score_scale
    )
    near_peak, near_total, near_weights = softmax_parts(near_scores, near_valid)
    packed, near_weights = lax.optimization_barrier((packed, near_weights))
    back = lax.all_to_all(packed, "group", split_axis=0, concat_axis=0, tiled=True)
    returned = jnp.dot(
        picks.T.astype(jnp.float32),
        back.reshape(groups * local_groups, -1),
        precision=lax.Precision.HIGHEST,
        preferred_element_type=jnp.float32,
    )
    mine = returned.reshape(requests, q_heads + 1, HD)
    far_acc = mine[:, :q_heads, :]
    far_peak = mine[:, q_heads, :q_heads]
    far_total = mine[:, q_heads, q_heads : 2 * q_heads]
    near_wide = jnp.einsum(
        "rqt,rtc->rqc", near_weights, suffix_values, preferred_element_type=jnp.float32
    )
    near_acc = pick_lanes(near_wide, kv_heads).reshape(requests, q_heads, HD)
    attn = combine(far_peak, far_total, far_acc, near_peak, near_total, near_acc)
    attn = attn.reshape(requests, q_heads * HD).astype(jnp.bfloat16)
    parts = lax.axis_size("tensor")
    partial_out = lax.optimization_barrier(
        jnp.dot(attn, out_weight, preferred_element_type=jnp.float32)
    )
    pieces = lax.all_to_all(
        jnp.transpose(partial_out.reshape(requests, parts, -1), (1, 0, 2)),
        "tensor",
        split_axis=0,
        concat_axis=0,
        tiled=True,
    )
    return jnp.sum(pieces, axis=0).astype(jnp.bfloat16)


def solution(mesh):
    in_specs = (
        P("group", None),
        P(None, "tensor"),
        P("tensor", None),
        P("group", None, "tensor"),
        P("group", None, "tensor"),
        P("group", None),
        P(),
        P("group"),
        P("group", None, "tensor"),
        P("group", None, "tensor"),
        P("group"),
    )
    out_specs = P("group", "tensor")
    return jax.shard_map(body, mesh=mesh, in_specs=in_specs, out_specs=out_specs, check_vma=False)
```

```python
import math

import jax
import jax.numpy as jnp
from jax import lax
from jax.experimental import pallas as pl
from jax.experimental.pallas import tpu as pltpu
from jax.sharding import PartitionSpec as P

HD = 128


rope_base = 10000.0
masked_score = -1e30


def rotate(projected, position):
    half = projected.shape[-1] // 2
    freqs = rope_base ** (-(2.0 * jnp.arange(half, dtype=jnp.float32)) / projected.shape[-1])
    angles = position.astype(jnp.float32)[:, None, None] * freqs
    cosine = jnp.cos(angles)
    sine = jnp.sin(angles)
    former = projected[..., :half]
    latter = projected[..., half:]
    return jnp.concatenate(
        [former * cosine - latter * sine, latter * cosine + former * sine], axis=-1
    )


def softmax_parts(scores, valid_mask):
    masked = jnp.where(valid_mask, scores, masked_score)
    maximum = jnp.max(masked, axis=-1)
    weights = jnp.where(valid_mask, jnp.exp(masked - maximum[..., None]), 0.0)
    return (maximum, jnp.sum(weights, axis=-1), weights.astype(jnp.bfloat16))


def combine(far_peak, far_total, far_acc, near_peak, near_total, near_acc):
    highest = jnp.maximum(far_peak, near_peak)
    far_factor = jnp.exp(far_peak - highest)
    near_factor = jnp.exp(near_peak - highest)
    numer = far_acc * far_factor[..., None] + near_acc * near_factor[..., None]
    denom = far_total * far_factor + near_total * near_factor
    return numer / denom[..., None]


def spread_lanes(queries, kv_heads):
    lead = queries.shape[:-3]
    share = queries.shape[-2]
    eye = (jnp.arange(kv_heads)[:, None] == jnp.arange(kv_heads)[None, :]).astype(queries.dtype)
    eye = eye.reshape((1,) * len(lead) + (kv_heads, 1, kv_heads, 1))
    wide = queries[..., None, :] * eye
    return wide.reshape(lead + (kv_heads * share, kv_heads * HD))


def pick_lanes(wide, kv_heads):
    lead = wide.shape[:-2]
    share = wide.shape[-2] // kv_heads
    w = wide.reshape(lead + (kv_heads, share, kv_heads, HD))
    return jnp.stack([w[..., k, :, k, :] for k in range(kv_heads)], axis=-3)


def far_kernel(
    table_ref, len_ref, q_ref, k_hbm, v_hbm, out_ref, kbuf, vbuf, sems, *, share, scale
):
    steps = q_ref.shape[0]
    pblk = kbuf.shape[1]
    block = kbuf.shape[2]
    width = kbuf.shape[3]
    kv_heads = width // HD
    chunk = 8
    sources = out_ref.shape[0]
    q_heads = out_ref.shape[1] - 1

    vbuf[...] = jnp.zeros_like(vbuf)

    def used_chunks(group):
        return (len_ref[group] + block * chunk - 1) // (block * chunk)

    def fetch(group, slot):
        def one(c, carry):
            for i in range(chunk):
                b = c * chunk + i
                idx = table_ref[group * pblk + b]
                pltpu.make_async_copy(k_hbm.at[idx], kbuf.at[slot, b], sems.at[0, slot, c]).start()
                pltpu.make_async_copy(v_hbm.at[idx], vbuf.at[slot, b], sems.at[1, slot, c]).start()
            return carry

        lax.fori_loop(0, used_chunks(group), one, 0)

    fetch(0, 0)

    def group_step(j, carry):
        slot = j % 2

        @pl.when(j + 1 < steps)
        def _():
            fetch(j + 1, 1 - slot)

        def settle(c, carry):
            part = pl.ds(pl.multiple_of(c * chunk, chunk), chunk)
            pltpu.make_async_copy(
                k_hbm.at[pl.ds(0, chunk)], kbuf.at[slot, part], sems.at[0, slot, c]
            ).wait()
            pltpu.make_async_copy(
                v_hbm.at[pl.ds(0, chunk)], vbuf.at[slot, part], sems.at[1, slot, c]
            ).wait()
            return carry

        lax.fori_loop(0, used_chunks(j), settle, 0)
        keys = kbuf[slot].reshape(-1, width)
        values = vbuf[slot].reshape(-1, width)
        queries = q_ref[j]
        scores = (
            lax.dot_general(
                queries, keys, (((1,), (1,)), ((), ())), preferred_element_type=jnp.float32
            )
            * scale
        )
        valid = lax.broadcasted_iota(jnp.int32, scores.shape, 1) < len_ref[j]
        masked = jnp.where(valid, scores, masked_score)
        peak = jnp.max(masked, axis=1, keepdims=True)
        weights = jnp.where(valid, jnp.exp(masked - peak), 0.0)
        total = jnp.sum(weights, axis=1, keepdims=True)
        wide = jnp.dot(weights.astype(jnp.bfloat16), values, preferred_element_type=jnp.float32)
        rows = wide.shape[0]
        row_head = (lax.broadcasted_iota(jnp.int32, (rows, HD), 0) // share) % kv_heads
        acc = jnp.zeros((rows, HD), jnp.float32)
        for k in range(kv_heads):
            acc = jnp.where(row_head == k, wide[:, k * HD : (k + 1) * HD], acc)
        out_ref[:, :q_heads, pl.ds(j, 1), :] = acc.reshape(sources, q_heads, 1, HD)
        lane = lax.broadcasted_iota(jnp.int32, (sources, q_heads, HD), 2)
        head = lax.broadcasted_iota(jnp.int32, (sources, q_heads, HD), 1)
        peak3 = jnp.broadcast_to(peak, (rows, HD)).reshape(sources, q_heads, HD)
        total3 = jnp.broadcast_to(total, (rows, HD)).reshape(sources, q_heads, HD)
        stat = jnp.where(lane == head, peak3, 0.0) + jnp.where(lane == head + q_heads, total3, 0.0)
        out_ref[:, q_heads:, pl.ds(j, 1), :] = jnp.sum(stat, axis=1).reshape(sources, 1, 1, HD)
        return carry

    lax.fori_loop(0, steps, group_step, 0)


def far_attention(table, lengths, queries, prefix_keys, prefix_values, share, scale, sources):
    local_groups, pblk = table.shape
    assert pblk % 8 == 0
    _, rows, width = queries.shape
    q_heads = rows // sources
    assert 2 * q_heads <= HD
    block = prefix_keys.shape[1]
    tokens = pblk * block
    kernel = lambda *refs: far_kernel(*refs, share=share, scale=scale)
    grid_spec = pltpu.PrefetchScalarGridSpec(
        num_scalar_prefetch=2,
        grid=(1,),
        in_specs=[
            pl.BlockSpec((local_groups, rows, width), lambda j, *_: (0, 0, 0)),
            pl.BlockSpec(memory_space=pl.ANY),
            pl.BlockSpec(memory_space=pl.ANY),
        ],
        out_specs=pl.BlockSpec(
            (sources, q_heads + 1, local_groups, HD), lambda j, *_: (0, 0, 0, 0)
        ),
        scratch_shapes=[
            pltpu.VMEM((2, pblk, block, width), prefix_keys.dtype),
            pltpu.VMEM((2, pblk, block, width), prefix_values.dtype),
            pltpu.SemaphoreType.DMA((2, 2, pblk // 8)),
        ],
    )
    cost = pl.CostEstimate(
        flops=4 * local_groups * rows * tokens * width,
        transcendentals=local_groups * rows * tokens,
        bytes_accessed=2 * local_groups * tokens * width * 2 + 3 * local_groups * rows * width * 2,
    )
    return pl.pallas_call(
        kernel,
        grid_spec=grid_spec,
        out_shape=jax.ShapeDtypeStruct((sources, q_heads + 1, local_groups, HD), jnp.float32),
        compiler_params=pltpu.CompilerParams(dimension_semantics=("arbitrary",)),
        cost_estimate=cost,
    )(table.reshape(-1), lengths, queries, prefix_keys, prefix_values)


def body(
    hidden,
    query_weight,
    out_weight,
    prefix_keys,
    prefix_values,
    block_table,
    prompt_len,
    prompt_group,
    suffix_keys,
    suffix_values,
    suffix_len,
):
    groups = lax.axis_size("group")
    local_groups = block_table.shape[0]
    first_group = lax.axis_index("group") * local_groups
    requests = hidden.shape[0]
    width = prefix_keys.shape[2]
    kv_heads = width // HD
    q_heads = query_weight.shape[1] // HD
    share = q_heads // kv_heads
    score_scale = 1.0 / math.sqrt(HD)

    projected = jnp.dot(hidden, query_weight, preferred_element_type=jnp.float32).reshape(
        requests, q_heads, HD
    )
    everyone = jnp.arange(prompt_len.shape[0], dtype=jnp.int32)
    own_prompt = jnp.sum(
        jnp.where(prompt_group[:, None] == everyone[None, :], prompt_len[None, :], 0), axis=1
    )
    position = own_prompt + suffix_len - 1
    rotated = rotate(projected, position).astype(jnp.bfloat16)

    slots = jnp.arange(groups * local_groups, dtype=jnp.int32)
    picks = (slots[:, None] == prompt_group[None, :]).astype(jnp.bfloat16)
    outgoing = jnp.dot(
        picks, rotated.reshape(requests, q_heads * HD), preferred_element_type=jnp.float32
    ).astype(jnp.bfloat16)
    arrived = lax.all_to_all(
        outgoing.reshape(groups, local_groups, q_heads * HD),
        "group",
        split_axis=0,
        concat_axis=0,
        tiled=True,
    )
    far_queries = jnp.transpose(
        arrived.reshape(groups, local_groups, kv_heads, share, HD), (1, 0, 2, 3, 4)
    )
    far_queries = spread_lanes(far_queries, kv_heads).reshape(
        local_groups, groups * q_heads, width
    )
    my_lengths = lax.dynamic_slice_in_dim(prompt_len, first_group, local_groups)
    packed = far_attention(
        block_table, my_lengths, far_queries, prefix_keys, prefix_values, share, score_scale,
        groups,
    )
    packed = jnp.transpose(packed, (0, 2, 1, 3))

    near_queries = spread_lanes(rotated.reshape(requests, kv_heads, share, HD), kv_heads)
    own_count = suffix_keys.shape[1]
    near_valid = jnp.arange(own_count, dtype=jnp.int32)[None, None, :] < suffix_len[:, None, None]
    near_scores = (
        jnp.einsum("rqc,rtc->rqt", near_queries, suffix_keys, preferred_element_type=jnp.float32)
        * score_scale
    )
    near_peak, near_total, near_weights = softmax_parts(near_scores, near_valid)
    packed, near_weights = lax.optimization_barrier((packed, near_weights))
    back = lax.all_to_all(packed, "group", split_axis=0, concat_axis=0, tiled=True)
    returned = jnp.dot(
        picks.T.astype(jnp.float32),
        back.reshape(groups * local_groups, -1),
        precision=lax.Precision.HIGHEST,
        preferred_element_type=jnp.float32,
    )
    mine = returned.reshape(requests, q_heads + 1, HD)
    far_acc = mine[:, :q_heads, :]
    far_peak = mine[:, q_heads, :q_heads]
    far_total = mine[:, q_heads, q_heads : 2 * q_heads]
    near_wide = jnp.einsum(
        "rqt,rtc->rqc", near_weights, suffix_values, preferred_element_type=jnp.float32
    )
    near_acc = pick_lanes(near_wide, kv_heads).reshape(requests, q_heads, HD)
    attn = combine(far_peak, far_total, far_acc, near_peak, near_total, near_acc)
    attn = attn.reshape(requests, q_heads * HD).astype(jnp.bfloat16)
    parts = lax.axis_size("tensor")
    partial_out = lax.optimization_barrier(
        jnp.dot(attn, out_weight, preferred_element_type=jnp.float32)
    )
    pieces = lax.all_to_all(
        jnp.transpose(partial_out.reshape(requests, parts, -1), (1, 0, 2)),
        "tensor",
        split_axis=0,
        concat_axis=0,
        tiled=True,
    )
    return jnp.sum(pieces, axis=0).astype(jnp.bfloat16)


def solution(mesh):
    in_specs = (
        P("group", None),
        P(None, "tensor"),
        P("tensor", None),
        P("group", None, "tensor"),
        P("group", None, "tensor"),
        P("group", None),
        P(),
        P("group"),
        P("group", None, "tensor"),
        P("group", None, "tensor"),
        P("group"),
    )
    out_specs = P("group", "tensor")
    return jax.shard_map(body, mesh=mesh, in_specs=in_specs, out_specs=out_specs, check_vma=False)
```

```python
import math

import jax
import jax.numpy as jnp
from jax import lax
from jax.experimental import pallas as pl
from jax.experimental.pallas import tpu as pltpu
from jax.sharding import PartitionSpec as P

HD = 128


rope_base = 10000.0
masked_score = -1e30


def rotate(projected, position):
    half = projected.shape[-1] // 2
    freqs = rope_base ** (-(2.0 * jnp.arange(half, dtype=jnp.float32)) / projected.shape[-1])
    angles = position.astype(jnp.float32)[:, None, None] * freqs
    cosine = jnp.cos(angles)
    sine = jnp.sin(angles)
    former = projected[..., :half]
    latter = projected[..., half:]
    return jnp.concatenate(
        [former * cosine - latter * sine, latter * cosine + former * sine], axis=-1
    )


def softmax_parts(scores, valid_mask):
    masked = jnp.where(valid_mask, scores, masked_score)
    maximum = jnp.max(masked, axis=-1)
    weights = jnp.where(valid_mask, jnp.exp(masked - maximum[..., None]), 0.0)
    return (maximum, jnp.sum(weights, axis=-1), weights.astype(jnp.bfloat16))


def combine(far_peak, far_total, far_acc, near_peak, near_total, near_acc):
    highest = jnp.maximum(far_peak, near_peak)
    far_factor = jnp.exp(far_peak - highest)
    near_factor = jnp.exp(near_peak - highest)
    numer = far_acc * far_factor[..., None] + near_acc * near_factor[..., None]
    denom = far_total * far_factor + near_total * near_factor
    return numer / denom[..., None]


def spread_lanes(queries, kv_heads):
    lead = queries.shape[:-3]
    share = queries.shape[-2]
    eye = (jnp.arange(kv_heads)[:, None] == jnp.arange(kv_heads)[None, :]).astype(queries.dtype)
    eye = eye.reshape((1,) * len(lead) + (kv_heads, 1, kv_heads, 1))
    wide = queries[..., None, :] * eye
    return wide.reshape(lead + (kv_heads * share, kv_heads * HD))


def pick_lanes(wide, kv_heads):
    lead = wide.shape[:-2]
    share = wide.shape[-2] // kv_heads
    w = wide.reshape(lead + (kv_heads, share, kv_heads, HD))
    return jnp.stack([w[..., k, :, k, :] for k in range(kv_heads)], axis=-3)


def far_kernel(
    table_ref, len_ref, q_ref, k_hbm, v_hbm, out_ref, kbuf, vbuf, sems, *, share, scale
):
    steps = q_ref.shape[0]
    pblk = kbuf.shape[1]
    block = kbuf.shape[2]
    width = kbuf.shape[3]
    kv_heads = width // HD
    chunk = 8
    sources = out_ref.shape[0]
    q_heads = out_ref.shape[1] - 1

    vbuf[...] = jnp.zeros_like(vbuf)

    def used_chunks(group):
        return (len_ref[group] + block * chunk - 1) // (block * chunk)

    def fetch(group, slot):
        def one(c, carry):
            for i in range(chunk):
                b = c * chunk + i
                idx = table_ref[group * pblk + b]
                pltpu.make_async_copy(k_hbm.at[idx], kbuf.at[slot, b], sems.at[0, slot, c]).start()
                pltpu.make_async_copy(v_hbm.at[idx], vbuf.at[slot, b], sems.at[1, slot, c]).start()
            return carry

        lax.fori_loop(0, used_chunks(group), one, 0)

    fetch(0, 0)

    def group_step(j, carry):
        slot = j % 2

        @pl.when(j + 1 < steps)
        def _():
            fetch(j + 1, 1 - slot)

        def settle(c, carry):
            part = pl.ds(pl.multiple_of(c * chunk, chunk), chunk)
            pltpu.make_async_copy(
                k_hbm.at[pl.ds(0, chunk)], kbuf.at[slot, part], sems.at[0, slot, c]
            ).wait()
            pltpu.make_async_copy(
                v_hbm.at[pl.ds(0, chunk)], vbuf.at[slot, part], sems.at[1, slot, c]
            ).wait()
            return carry

        lax.fori_loop(0, used_chunks(j), settle, 0)
        keys = kbuf[slot].reshape(-1, width)
        values = vbuf[slot].reshape(-1, width)
        compact = q_ref[j]
        rows = compact.shape[0]
        row_head = (lax.broadcasted_iota(jnp.int32, (rows, HD), 0) // share) % kv_heads
        queries = jnp.concatenate(
            [jnp.where(row_head == k, compact, jnp.zeros_like(compact)) for k in range(kv_heads)],
            axis=1,
        )
        scores = (
            lax.dot_general(
                queries, keys, (((1,), (1,)), ((), ())), preferred_element_type=jnp.float32
            )
            * scale
        )
        valid = lax.broadcasted_iota(jnp.int32, scores.shape, 1) < len_ref[j]
        masked = jnp.where(valid, scores, masked_score)
        peak = jnp.max(masked, axis=1, keepdims=True)
        weights = jnp.where(valid, jnp.exp(masked - peak), 0.0)
        total = jnp.sum(weights, axis=1, keepdims=True)
        wide = jnp.dot(weights.astype(jnp.bfloat16), values, preferred_element_type=jnp.float32)
        acc = jnp.zeros((rows, HD), jnp.float32)
        for k in range(kv_heads):
            acc = jnp.where(row_head == k, wide[:, k * HD : (k + 1) * HD], acc)
        out_ref[:, :q_heads, pl.ds(j, 1), :] = acc.reshape(sources, q_heads, 1, HD)
        lane = lax.broadcasted_iota(jnp.int32, (sources, q_heads, HD), 2)
        head = lax.broadcasted_iota(jnp.int32, (sources, q_heads, HD), 1)
        peak3 = jnp.broadcast_to(peak, (rows, HD)).reshape(sources, q_heads, HD)
        total3 = jnp.broadcast_to(total, (rows, HD)).reshape(sources, q_heads, HD)
        stat = jnp.where(lane == head, peak3, 0.0) + jnp.where(lane == head + q_heads, total3, 0.0)
        out_ref[:, q_heads:, pl.ds(j, 1), :] = jnp.sum(stat, axis=1).reshape(sources, 1, 1, HD)
        return carry

    lax.fori_loop(0, steps, group_step, 0)


def far_attention(table, lengths, queries, prefix_keys, prefix_values, share, scale, sources):
    local_groups, pblk = table.shape
    assert pblk % 8 == 0
    _, rows, _ = queries.shape
    width = prefix_keys.shape[2]
    q_heads = rows // sources
    assert 2 * q_heads <= HD
    block = prefix_keys.shape[1]
    tokens = pblk * block
    kernel = lambda *refs: far_kernel(*refs, share=share, scale=scale)
    grid_spec = pltpu.PrefetchScalarGridSpec(
        num_scalar_prefetch=2,
        grid=(1,),
        in_specs=[
            pl.BlockSpec((local_groups, rows, HD), lambda j, *_: (0, 0, 0)),
            pl.BlockSpec(memory_space=pl.ANY),
            pl.BlockSpec(memory_space=pl.ANY),
        ],
        out_specs=pl.BlockSpec(
            (sources, q_heads + 1, local_groups, HD), lambda j, *_: (0, 0, 0, 0)
        ),
        scratch_shapes=[
            pltpu.VMEM((2, pblk, block, width), prefix_keys.dtype),
            pltpu.VMEM((2, pblk, block, width), prefix_values.dtype),
            pltpu.SemaphoreType.DMA((2, 2, pblk // 8)),
        ],
    )
    cost = pl.CostEstimate(
        flops=4 * local_groups * rows * tokens * width,
        transcendentals=local_groups * rows * tokens,
        bytes_accessed=2 * local_groups * tokens * width * 2 + 3 * local_groups * rows * width * 2,
    )
    return pl.pallas_call(
        kernel,
        grid_spec=grid_spec,
        out_shape=jax.ShapeDtypeStruct((sources, q_heads + 1, local_groups, HD), jnp.float32),
        compiler_params=pltpu.CompilerParams(dimension_semantics=("arbitrary",)),
        cost_estimate=cost,
    )(table.reshape(-1), lengths, queries, prefix_keys, prefix_values)


def body(
    hidden,
    query_weight,
    out_weight,
    prefix_keys,
    prefix_values,
    block_table,
    prompt_len,
    prompt_group,
    suffix_keys,
    suffix_values,
    suffix_len,
):
    groups = lax.axis_size("group")
    local_groups = block_table.shape[0]
    first_group = lax.axis_index("group") * local_groups
    requests = hidden.shape[0]
    width = prefix_keys.shape[2]
    kv_heads = width // HD
    q_heads = query_weight.shape[1] // HD
    share = q_heads // kv_heads
    score_scale = 1.0 / math.sqrt(HD)

    projected = jnp.dot(hidden, query_weight, preferred_element_type=jnp.float32).reshape(
        requests, q_heads, HD
    )
    everyone = jnp.arange(prompt_len.shape[0], dtype=jnp.int32)
    own_prompt = jnp.sum(
        jnp.where(prompt_group[:, None] == everyone[None, :], prompt_len[None, :], 0), axis=1
    )
    position = own_prompt + suffix_len - 1
    rotated = rotate(projected, position).astype(jnp.bfloat16)

    slots = jnp.arange(groups * local_groups, dtype=jnp.int32)
    picks = (slots[:, None] == prompt_group[None, :]).astype(jnp.bfloat16)
    outgoing = jnp.dot(
        picks, rotated.reshape(requests, q_heads * HD), preferred_element_type=jnp.float32
    ).astype(jnp.bfloat16)
    arrived = lax.all_to_all(
        outgoing.reshape(groups, local_groups, q_heads * HD),
        "group",
        split_axis=0,
        concat_axis=0,
        tiled=True,
    )
    far_queries = jnp.transpose(
        arrived.reshape(groups, local_groups, kv_heads, share, HD), (1, 0, 2, 3, 4)
    )
    far_queries = far_queries.reshape(local_groups, groups * q_heads, HD)
    my_lengths = lax.dynamic_slice_in_dim(prompt_len, first_group, local_groups)
    packed = far_attention(
        block_table, my_lengths, far_queries, prefix_keys, prefix_values, share, score_scale,
        groups,
    )
    packed = jnp.transpose(packed, (0, 2, 1, 3))

    near_queries = spread_lanes(rotated.reshape(requests, kv_heads, share, HD), kv_heads)
    own_count = suffix_keys.shape[1]
    near_valid = jnp.arange(own_count, dtype=jnp.int32)[None, None, :] < suffix_len[:, None, None]
    near_scores = (
        jnp.einsum("rqc,rtc->rqt", near_queries, suffix_keys, preferred_element_type=jnp.float32)
        * score_scale
    )
    near_peak, near_total, near_weights = softmax_parts(near_scores, near_valid)
    packed, near_weights = lax.optimization_barrier((packed, near_weights))
    back = lax.all_to_all(packed, "group", split_axis=0, concat_axis=0, tiled=True)
    returned = jnp.dot(
        picks.T.astype(jnp.float32),
        back.reshape(groups * local_groups, -1),
        precision=lax.Precision.HIGHEST,
        preferred_element_type=jnp.float32,
    )
    mine = returned.reshape(requests, q_heads + 1, HD)
    far_acc = mine[:, :q_heads, :]
    far_peak = mine[:, q_heads, :q_heads]
    far_total = mine[:, q_heads, q_heads : 2 * q_heads]
    near_wide = jnp.einsum(
        "rqt,rtc->rqc", near_weights, suffix_values, preferred_element_type=jnp.float32
    )
    near_acc = pick_lanes(near_wide, kv_heads).reshape(requests, q_heads, HD)
    attn = combine(far_peak, far_total, far_acc, near_peak, near_total, near_acc)
    attn = attn.reshape(requests, q_heads * HD).astype(jnp.bfloat16)
    parts = lax.axis_size("tensor")
    partial_out = lax.optimization_barrier(
        jnp.dot(attn, out_weight, preferred_element_type=jnp.float32)
    )
    pieces = lax.all_to_all(
        jnp.transpose(partial_out.reshape(requests, parts, -1), (1, 0, 2)),
        "tensor",
        split_axis=0,
        concat_axis=0,
        tiled=True,
    )
    return jnp.sum(pieces, axis=0).astype(jnp.bfloat16)


def solution(mesh):
    in_specs = (
        P("group", None),
        P(None, "tensor"),
        P("tensor", None),
        P("group", None, "tensor"),
        P("group", None, "tensor"),
        P("group", None),
        P(),
        P("group"),
        P("group", None, "tensor"),
        P("group", None, "tensor"),
        P("group"),
    )
    out_specs = P("group", "tensor")
    return jax.shard_map(body, mesh=mesh, in_specs=in_specs, out_specs=out_specs, check_vma=False)
```

```python
import math

import jax
import jax.numpy as jnp
from jax import lax
from jax.experimental import pallas as pl
from jax.experimental.pallas import tpu as pltpu
from jax.sharding import PartitionSpec as P

HD = 128


rope_base = 10000.0
masked_score = -1e30


def rotate(projected, position):
    half = projected.shape[-1] // 2
    freqs = rope_base ** (-(2.0 * jnp.arange(half, dtype=jnp.float32)) / projected.shape[-1])
    angles = position.astype(jnp.float32)[:, None, None] * freqs
    cosine = jnp.cos(angles)
    sine = jnp.sin(angles)
    former = projected[..., :half]
    latter = projected[..., half:]
    return jnp.concatenate(
        [former * cosine - latter * sine, latter * cosine + former * sine], axis=-1
    )


def softmax_parts(scores, valid_mask):
    masked = jnp.where(valid_mask, scores, masked_score)
    maximum = jnp.max(masked, axis=-1)
    weights = jnp.where(valid_mask, jnp.exp(masked - maximum[..., None]), 0.0)
    return (maximum, jnp.sum(weights, axis=-1), weights.astype(jnp.bfloat16))


def combine(far_peak, far_total, far_acc, near_peak, near_total, near_acc):
    highest = jnp.maximum(far_peak, near_peak)
    far_factor = jnp.exp(far_peak - highest)
    near_factor = jnp.exp(near_peak - highest)
    numer = far_acc * far_factor[..., None] + near_acc * near_factor[..., None]
    denom = far_total * far_factor + near_total * near_factor
    return numer / denom[..., None]


def spread_lanes(queries, kv_heads):
    lead = queries.shape[:-3]
    share = queries.shape[-2]
    eye = (jnp.arange(kv_heads)[:, None] == jnp.arange(kv_heads)[None, :]).astype(queries.dtype)
    eye = eye.reshape((1,) * len(lead) + (kv_heads, 1, kv_heads, 1))
    wide = queries[..., None, :] * eye
    return wide.reshape(lead + (kv_heads * share, kv_heads * HD))


def pick_lanes(wide, kv_heads):
    lead = wide.shape[:-2]
    share = wide.shape[-2] // kv_heads
    w = wide.reshape(lead + (kv_heads, share, kv_heads, HD))
    return jnp.stack([w[..., k, :, k, :] for k in range(kv_heads)], axis=-3)


def far_kernel(
    table_ref, len_ref, q_ref, k_hbm, v_hbm, out_ref, kbuf, vbuf, sems, *, share, scale
):
    steps = q_ref.shape[0]
    pblk = kbuf.shape[1]
    block = kbuf.shape[2]
    width = kbuf.shape[3]
    kv_heads = width // HD
    chunk = 8
    sources = out_ref.shape[0]
    q_heads = out_ref.shape[1] - 1

    vbuf[...] = jnp.zeros_like(vbuf)

    def used_chunks(group):
        return (len_ref[group] + block * chunk - 1) // (block * chunk)

    def fetch(group, slot):
        def one(c, carry):
            for i in range(chunk):
                b = c * chunk + i
                idx = table_ref[group * pblk + b]
                pltpu.make_async_copy(k_hbm.at[idx], kbuf.at[slot, b], sems.at[0, slot, c]).start()
                pltpu.make_async_copy(v_hbm.at[idx], vbuf.at[slot, b], sems.at[1, slot, c]).start()
            return carry

        lax.fori_loop(0, used_chunks(group), one, 0)

    fetch(0, 0)

    def group_step(j, carry):
        slot = j % 2

        @pl.when(j + 1 < steps)
        def _():
            fetch(j + 1, 1 - slot)

        def settle(c, carry):
            part = pl.ds(pl.multiple_of(c * chunk, chunk), chunk)
            pltpu.make_async_copy(
                k_hbm.at[pl.ds(0, chunk)], kbuf.at[slot, part], sems.at[0, slot, c]
            ).wait()
            pltpu.make_async_copy(
                v_hbm.at[pl.ds(0, chunk)], vbuf.at[slot, part], sems.at[1, slot, c]
            ).wait()
            return carry

        lax.fori_loop(0, used_chunks(j), settle, 0)
        keys = kbuf[slot].reshape(-1, width)
        values = vbuf[slot].reshape(-1, width)
        arrived = q_ref[j].astype(jnp.float32)
        compact = jnp.concatenate(
            [arrived[:, h * HD : (h + 1) * HD] for h in range(q_heads)], axis=0
        )
        rows = compact.shape[0]
        row_head = (lax.broadcasted_iota(jnp.int32, (rows, HD), 0) // (sources * share)) % kv_heads
        queries = jnp.concatenate(
            [jnp.where(row_head == k, compact, 0.0) for k in range(kv_heads)], axis=1
        ).astype(jnp.bfloat16)
        scores = (
            lax.dot_general(
                queries, keys, (((1,), (1,)), ((), ())), preferred_element_type=jnp.float32
            )
            * scale
        )
        valid = lax.broadcasted_iota(jnp.int32, scores.shape, 1) < len_ref[j]
        masked = jnp.where(valid, scores, masked_score)
        peak = jnp.max(masked, axis=1, keepdims=True)
        weights = jnp.where(valid, jnp.exp(masked - peak), 0.0)
        total = jnp.sum(weights, axis=1, keepdims=True)
        wide = jnp.dot(weights.astype(jnp.bfloat16), values, preferred_element_type=jnp.float32)
        acc = jnp.zeros((rows, HD), jnp.float32)
        for k in range(kv_heads):
            acc = jnp.where(row_head == k, wide[:, k * HD : (k + 1) * HD], acc)
        for h in range(q_heads):
            out_ref[:, h : h + 1, pl.ds(j, 1), :] = acc[h * sources : (h + 1) * sources].reshape(
                sources, 1, 1, HD
            )
        lane = lax.broadcasted_iota(jnp.int32, (q_heads, sources, HD), 2)
        head = lax.broadcasted_iota(jnp.int32, (q_heads, sources, HD), 0)
        peak3 = jnp.broadcast_to(peak, (rows, HD)).reshape(q_heads, sources, HD)
        total3 = jnp.broadcast_to(total, (rows, HD)).reshape(q_heads, sources, HD)
        stat = jnp.where(lane == head, peak3, 0.0) + jnp.where(lane == head + q_heads, total3, 0.0)
        out_ref[:, q_heads:, pl.ds(j, 1), :] = jnp.sum(stat, axis=0).reshape(sources, 1, 1, HD)
        return carry

    lax.fori_loop(0, steps, group_step, 0)


def far_attention(table, lengths, queries, prefix_keys, prefix_values, share, scale, sources):
    local_groups, pblk = table.shape
    assert pblk % 8 == 0
    _, _, wide_q = queries.shape
    q_heads = wide_q // HD
    rows = sources * q_heads
    width = prefix_keys.shape[2]
    assert 2 * q_heads <= HD
    block = prefix_keys.shape[1]
    tokens = pblk * block
    kernel = lambda *refs: far_kernel(*refs, share=share, scale=scale)
    grid_spec = pltpu.PrefetchScalarGridSpec(
        num_scalar_prefetch=2,
        grid=(1,),
        in_specs=[
            pl.BlockSpec((local_groups, sources, wide_q), lambda j, *_: (0, 0, 0)),
            pl.BlockSpec(memory_space=pl.ANY),
            pl.BlockSpec(memory_space=pl.ANY),
        ],
        out_specs=pl.BlockSpec(
            (sources, q_heads + 1, local_groups, HD), lambda j, *_: (0, 0, 0, 0)
        ),
        scratch_shapes=[
            pltpu.VMEM((2, pblk, block, width), prefix_keys.dtype),
            pltpu.VMEM((2, pblk, block, width), prefix_values.dtype),
            pltpu.SemaphoreType.DMA((2, 2, pblk // 8)),
        ],
    )
    cost = pl.CostEstimate(
        flops=4 * local_groups * rows * tokens * width,
        transcendentals=local_groups * rows * tokens,
        bytes_accessed=2 * local_groups * tokens * width * 2 + 3 * local_groups * rows * width * 2,
    )
    return pl.pallas_call(
        kernel,
        grid_spec=grid_spec,
        out_shape=jax.ShapeDtypeStruct((sources, q_heads + 1, local_groups, HD), jnp.float32),
        compiler_params=pltpu.CompilerParams(dimension_semantics=("arbitrary",)),
        cost_estimate=cost,
    )(table.reshape(-1), lengths, queries, prefix_keys, prefix_values)


def body(
    hidden,
    query_weight,
    out_weight,
    prefix_keys,
    prefix_values,
    block_table,
    prompt_len,
    prompt_group,
    suffix_keys,
    suffix_values,
    suffix_len,
):
    groups = lax.axis_size("group")
    local_groups = block_table.shape[0]
    first_group = lax.axis_index("group") * local_groups
    requests = hidden.shape[0]
    width = prefix_keys.shape[2]
    kv_heads = width // HD
    q_heads = query_weight.shape[1] // HD
    share = q_heads // kv_heads
    score_scale = 1.0 / math.sqrt(HD)

    projected = jnp.dot(hidden, query_weight, preferred_element_type=jnp.float32).reshape(
        requests, q_heads, HD
    )
    everyone = jnp.arange(prompt_len.shape[0], dtype=jnp.int32)
    own_prompt = jnp.sum(
        jnp.where(prompt_group[:, None] == everyone[None, :], prompt_len[None, :], 0), axis=1
    )
    position = own_prompt + suffix_len - 1
    rotated = rotate(projected, position).astype(jnp.bfloat16)

    slots = jnp.arange(groups * local_groups, dtype=jnp.int32)
    picks = (slots[:, None] == prompt_group[None, :]).astype(jnp.bfloat16)
    outgoing = jnp.dot(
        picks, rotated.reshape(requests, q_heads * HD), preferred_element_type=jnp.float32
    ).astype(jnp.bfloat16)
    arrived = lax.all_to_all(
        outgoing.reshape(groups, local_groups, 1, q_heads * HD),
        "group",
        split_axis=0,
        concat_axis=2,
        tiled=True,
    )
    far_queries = arrived.reshape(local_groups, groups, q_heads * HD)
    my_lengths = lax.dynamic_slice_in_dim(prompt_len, first_group, local_groups)
    packed = far_attention(
        block_table, my_lengths, far_queries, prefix_keys, prefix_values, share, score_scale,
        groups,
    )
    packed = jnp.transpose(packed, (0, 2, 1, 3))

    near_queries = spread_lanes(rotated.reshape(requests, kv_heads, share, HD), kv_heads)
    own_count = suffix_keys.shape[1]
    near_valid = jnp.arange(own_count, dtype=jnp.int32)[None, None, :] < suffix_len[:, None, None]
    near_scores = (
        jnp.einsum("rqc,rtc->rqt", near_queries, suffix_keys, preferred_element_type=jnp.float32)
        * score_scale
    )
    near_peak, near_total, near_weights = softmax_parts(near_scores, near_valid)
    packed, near_weights = lax.optimization_barrier((packed, near_weights))
    back = lax.all_to_all(packed, "group", split_axis=0, concat_axis=0, tiled=True)
    returned = jnp.dot(
        picks.T.astype(jnp.float32),
        back.reshape(groups * local_groups, -1),
        precision=lax.Precision.HIGHEST,
        preferred_element_type=jnp.float32,
    )
    mine = returned.reshape(requests, q_heads + 1, HD)
    far_acc = mine[:, :q_heads, :]
    far_peak = mine[:, q_heads, :q_heads]
    far_total = mine[:, q_heads, q_heads : 2 * q_heads]
    near_wide = jnp.einsum(
        "rqt,rtc->rqc", near_weights, suffix_values, preferred_element_type=jnp.float32
    )
    near_acc = pick_lanes(near_wide, kv_heads).reshape(requests, q_heads, HD)
    attn = combine(far_peak, far_total, far_acc, near_peak, near_total, near_acc)
    attn = attn.reshape(requests, q_heads * HD).astype(jnp.bfloat16)
    parts = lax.axis_size("tensor")
    partial_out = lax.optimization_barrier(
        jnp.dot(attn, out_weight, preferred_element_type=jnp.float32)
    )
    pieces = lax.all_to_all(
        jnp.transpose(partial_out.reshape(requests, parts, -1), (1, 0, 2)),
        "tensor",
        split_axis=0,
        concat_axis=0,
        tiled=True,
    )
    return jnp.sum(pieces, axis=0).astype(jnp.bfloat16)


def solution(mesh):
    in_specs = (
        P("group", None),
        P(None, "tensor"),
        P("tensor", None),
        P("group", None, "tensor"),
        P("group", None, "tensor"),
        P("group", None),
        P(),
        P("group"),
        P("group", None, "tensor"),
        P("group", None, "tensor"),
        P("group"),
    )
    out_specs = P("group", "tensor")
    return jax.shard_map(body, mesh=mesh, in_specs=in_specs, out_specs=out_specs, check_vma=False)
```

```python
import math

import jax
import jax.numpy as jnp
from jax import lax
from jax.experimental import pallas as pl
from jax.experimental.pallas import tpu as pltpu
from jax.sharding import PartitionSpec as P

HD = 128


rope_base = 10000.0
masked_score = -1e30


def rotate(projected, position):
    half = projected.shape[-1] // 2
    freqs = rope_base ** (-(2.0 * jnp.arange(half, dtype=jnp.float32)) / projected.shape[-1])
    angles = position.astype(jnp.float32)[:, None, None] * freqs
    cosine = jnp.cos(angles)
    sine = jnp.sin(angles)
    former = projected[..., :half]
    latter = projected[..., half:]
    return jnp.concatenate(
        [former * cosine - latter * sine, latter * cosine + former * sine], axis=-1
    )


def softmax_parts(scores, valid_mask):
    masked = jnp.where(valid_mask, scores, masked_score)
    maximum = jnp.max(masked, axis=-1)
    weights = jnp.where(valid_mask, jnp.exp(masked - maximum[..., None]), 0.0)
    return (maximum, jnp.sum(weights, axis=-1), weights.astype(jnp.bfloat16))


def combine(far_peak, far_total, far_acc, near_peak, near_total, near_acc):
    highest = jnp.maximum(far_peak, near_peak)
    far_factor = jnp.exp(far_peak - highest)
    near_factor = jnp.exp(near_peak - highest)
    numer = far_acc * far_factor[..., None] + near_acc * near_factor[..., None]
    denom = far_total * far_factor + near_total * near_factor
    return numer / denom[..., None]


def spread_lanes(queries, kv_heads):
    lead = queries.shape[:-3]
    share = queries.shape[-2]
    eye = (jnp.arange(kv_heads)[:, None] == jnp.arange(kv_heads)[None, :]).astype(queries.dtype)
    eye = eye.reshape((1,) * len(lead) + (kv_heads, 1, kv_heads, 1))
    wide = queries[..., None, :] * eye
    return wide.reshape(lead + (kv_heads * share, kv_heads * HD))


def pick_lanes(wide, kv_heads):
    lead = wide.shape[:-2]
    share = wide.shape[-2] // kv_heads
    w = wide.reshape(lead + (kv_heads, share, kv_heads, HD))
    return jnp.stack([w[..., k, :, k, :] for k in range(kv_heads)], axis=-3)


def far_kernel(
    table_ref, len_ref, q_ref, k_hbm, v_hbm, out_ref, kbuf, vbuf, sems, *, share, scale
):
    steps = q_ref.shape[0]
    pblk = kbuf.shape[1]
    block = kbuf.shape[2]
    width = kbuf.shape[3]
    kv_heads = width // HD
    chunk = 8
    sources = out_ref.shape[0]
    q_heads = out_ref.shape[1] - 1

    vbuf[...] = jnp.zeros_like(vbuf)

    def used_chunks(group):
        return (len_ref[group] + block * chunk - 1) // (block * chunk)

    def fetch(group, slot):
        def one(c, carry):
            for i in range(chunk):
                b = c * chunk + i
                idx = table_ref[group * pblk + b]
                pltpu.make_async_copy(k_hbm.at[idx], kbuf.at[slot, b], sems.at[0, slot, c]).start()
                pltpu.make_async_copy(v_hbm.at[idx], vbuf.at[slot, b], sems.at[1, slot, c]).start()
            return carry

        lax.fori_loop(0, used_chunks(group), one, 0)

    fetch(0, 0)

    def group_step(j, carry):
        slot = j % 2

        @pl.when(j + 1 < steps)
        def _():
            fetch(j + 1, 1 - slot)

        def settle(c, carry):
            part = pl.ds(pl.multiple_of(c * chunk, chunk), chunk)
            pltpu.make_async_copy(
                k_hbm.at[pl.ds(0, chunk)], kbuf.at[slot, part], sems.at[0, slot, c]
            ).wait()
            pltpu.make_async_copy(
                v_hbm.at[pl.ds(0, chunk)], vbuf.at[slot, part], sems.at[1, slot, c]
            ).wait()
            return carry

        lax.fori_loop(0, used_chunks(j), settle, 0)
        keys = kbuf[slot].reshape(-1, width)
        values = vbuf[slot].reshape(-1, width)
        arrived = q_ref[j].astype(jnp.float32)
        compact = jnp.concatenate(
            [arrived[:, h * HD : (h + 1) * HD] for h in range(q_heads)], axis=0
        )
        rows = compact.shape[0]
        row_head = (lax.broadcasted_iota(jnp.int32, (rows, HD), 0) // (sources * share)) % kv_heads
        queries = jnp.concatenate(
            [jnp.where(row_head == k, compact, 0.0) for k in range(kv_heads)], axis=1
        ).astype(jnp.bfloat16)
        scores = (
            lax.dot_general(
                queries, keys, (((1,), (1,)), ((), ())), preferred_element_type=jnp.float32
            )
            * scale
        )
        valid = lax.broadcasted_iota(jnp.int32, scores.shape, 1) < len_ref[j]
        masked = jnp.where(valid, scores, masked_score)
        peak = jnp.max(masked, axis=1, keepdims=True)
        weights = jnp.where(valid, jnp.exp(masked - peak), 0.0)
        total = jnp.sum(weights, axis=1, keepdims=True)
        wide = jnp.dot(weights.astype(jnp.bfloat16), values, preferred_element_type=jnp.float32)
        acc = jnp.zeros((rows, HD), jnp.float32)
        for k in range(kv_heads):
            acc = jnp.where(row_head == k, wide[:, k * HD : (k + 1) * HD], acc)
        for h in range(q_heads):
            out_ref[:, h : h + 1, pl.ds(j, 1), :] = acc[h * sources : (h + 1) * sources].reshape(
                sources, 1, 1, HD
            )
        lane = lax.broadcasted_iota(jnp.int32, (q_heads, sources, HD), 2)
        head = lax.broadcasted_iota(jnp.int32, (q_heads, sources, HD), 0)
        peak3 = jnp.broadcast_to(peak, (rows, HD)).reshape(q_heads, sources, HD)
        total3 = jnp.broadcast_to(total, (rows, HD)).reshape(q_heads, sources, HD)
        stat = jnp.where(lane == head, peak3, 0.0) + jnp.where(lane == head + q_heads, total3, 0.0)
        out_ref[:, q_heads:, pl.ds(j, 1), :] = jnp.sum(stat, axis=0).reshape(sources, 1, 1, HD)
        return carry

    lax.fori_loop(0, steps, group_step, 0)


def far_attention(table, lengths, queries, prefix_keys, prefix_values, share, scale, sources):
    local_groups, pblk = table.shape
    assert pblk % 8 == 0
    _, _, wide_q = queries.shape
    q_heads = wide_q // HD
    rows = sources * q_heads
    width = prefix_keys.shape[2]
    assert 2 * q_heads <= HD
    block = prefix_keys.shape[1]
    tokens = pblk * block
    kernel = lambda *refs: far_kernel(*refs, share=share, scale=scale)
    grid_spec = pltpu.PrefetchScalarGridSpec(
        num_scalar_prefetch=2,
        grid=(1,),
        in_specs=[
            pl.BlockSpec((local_groups, sources, wide_q), lambda j, *_: (0, 0, 0)),
            pl.BlockSpec(memory_space=pl.ANY),
            pl.BlockSpec(memory_space=pl.ANY),
        ],
        out_specs=pl.BlockSpec(
            (sources, q_heads + 1, local_groups, HD), lambda j, *_: (0, 0, 0, 0)
        ),
        scratch_shapes=[
            pltpu.VMEM((2, pblk, block, width), prefix_keys.dtype),
            pltpu.VMEM((2, pblk, block, width), prefix_values.dtype),
            pltpu.SemaphoreType.DMA((2, 2, pblk // 8)),
        ],
    )
    cost = pl.CostEstimate(
        flops=4 * local_groups * rows * tokens * width,
        transcendentals=local_groups * rows * tokens,
        bytes_accessed=2 * local_groups * tokens * width * 2 + 3 * local_groups * rows * width * 2,
    )
    return pl.pallas_call(
        kernel,
        grid_spec=grid_spec,
        out_shape=jax.ShapeDtypeStruct((sources, q_heads + 1, local_groups, HD), jnp.float32),
        compiler_params=pltpu.CompilerParams(dimension_semantics=("arbitrary",)),
        cost_estimate=cost,
    )(table.reshape(-1), lengths, queries, prefix_keys, prefix_values)


def body(
    hidden,
    query_weight,
    out_weight,
    prefix_keys,
    prefix_values,
    block_table,
    prompt_len,
    prompt_group,
    suffix_keys,
    suffix_values,
    suffix_len,
):
    groups = lax.axis_size("group")
    local_groups = block_table.shape[0]
    first_group = lax.axis_index("group") * local_groups
    requests = hidden.shape[0]
    width = prefix_keys.shape[2]
    kv_heads = width // HD
    q_heads = query_weight.shape[1] // HD
    share = q_heads // kv_heads
    score_scale = 1.0 / math.sqrt(HD)

    projected = jnp.dot(hidden, query_weight, preferred_element_type=jnp.float32).reshape(
        requests, q_heads, HD
    )
    everyone = jnp.arange(prompt_len.shape[0], dtype=jnp.int32)
    own_prompt = jnp.sum(
        jnp.where(prompt_group[:, None] == everyone[None, :], prompt_len[None, :], 0), axis=1
    )
    position = own_prompt + suffix_len - 1
    rotated = rotate(projected, position).astype(jnp.bfloat16)

    slots = jnp.arange(groups * local_groups, dtype=jnp.int32)
    picks = (slots[:, None] == prompt_group[None, :]).astype(jnp.bfloat16)
    outgoing = jnp.einsum(
        "glr,rf->glf",
        picks.reshape(groups, local_groups, requests),
        rotated.reshape(requests, q_heads * HD),
        preferred_element_type=jnp.float32,
    ).astype(jnp.bfloat16)
    arrived = lax.all_to_all(
        outgoing.reshape(groups, local_groups, 1, q_heads * HD),
        "group",
        split_axis=0,
        concat_axis=2,
        tiled=True,
    )
    far_queries = arrived.reshape(local_groups, groups, q_heads * HD)
    my_lengths = lax.dynamic_slice_in_dim(prompt_len, first_group, local_groups)
    packed = far_attention(
        block_table, my_lengths, far_queries, prefix_keys, prefix_values, share, score_scale,
        groups,
    )
    packed = jnp.transpose(packed, (0, 2, 1, 3))

    near_queries = spread_lanes(rotated.reshape(requests, kv_heads, share, HD), kv_heads)
    own_count = suffix_keys.shape[1]
    near_valid = jnp.arange(own_count, dtype=jnp.int32)[None, None, :] < suffix_len[:, None, None]
    near_scores = (
        jnp.einsum("rqc,rtc->rqt", near_queries, suffix_keys, preferred_element_type=jnp.float32)
        * score_scale
    )
    near_peak, near_total, near_weights = softmax_parts(near_scores, near_valid)
    packed, near_weights = lax.optimization_barrier((packed, near_weights))
    back = lax.all_to_all(packed, "group", split_axis=0, concat_axis=0, tiled=True)
    returned = jnp.dot(
        picks.T.astype(jnp.float32),
        back.reshape(groups * local_groups, -1),
        precision=lax.Precision.HIGHEST,
        preferred_element_type=jnp.float32,
    )
    mine = returned.reshape(requests, q_heads + 1, HD)
    far_acc = mine[:, :q_heads, :]
    far_peak = mine[:, q_heads, :q_heads]
    far_total = mine[:, q_heads, q_heads : 2 * q_heads]
    near_wide = jnp.einsum(
        "rqt,rtc->rqc", near_weights, suffix_values, preferred_element_type=jnp.float32
    )
    near_acc = pick_lanes(near_wide, kv_heads).reshape(requests, q_heads, HD)
    attn = combine(far_peak, far_total, far_acc, near_peak, near_total, near_acc)
    attn = attn.reshape(requests, q_heads * HD).astype(jnp.bfloat16)
    parts = lax.axis_size("tensor")
    partial_out = lax.optimization_barrier(
        jnp.dot(attn, out_weight, preferred_element_type=jnp.float32)
    )
    pieces = lax.all_to_all(
        jnp.transpose(partial_out.reshape(requests, parts, -1), (1, 0, 2)),
        "tensor",
        split_axis=0,
        concat_axis=0,
        tiled=True,
    )
    return jnp.sum(pieces, axis=0).astype(jnp.bfloat16)


def solution(mesh):
    in_specs = (
        P("group", None),
        P(None, "tensor"),
        P("tensor", None),
        P("group", None, "tensor"),
        P("group", None, "tensor"),
        P("group", None),
        P(),
        P("group"),
        P("group", None, "tensor"),
        P("group", None, "tensor"),
        P("group"),
    )
    out_specs = P("group", "tensor")
    return jax.shard_map(body, mesh=mesh, in_specs=in_specs, out_specs=out_specs, check_vma=False)
```
